32 devices in a mesh: tm: 4 (over x, core), tile: 8 (over z, y).
Axes of the slice: x: 2, y: 2, z: 4, core: 2. Of those that a mesh axis runs over, the one named last changes fastest.
Arguments:
- latent_tokens: bfloat16 [24576, 16], P(('tm', 'tile')), may hold values from -6 to 6
- entry_kernel: bfloat16 [3, 3, 3, 16, 384], replicated, may hold values from -0.3125 to 0.3125
- entry_bias: float32 [384], replicated, may hold values from -3 to 3
- gain_one: float32 [384], replicated, may hold values from 0.5 to 2
- first_kernel: bfloat16 [3, 3, 3, 384, 384], replicated, may hold values from -0.0625 to 0.0625
- first_bias: float32 [384], replicated, may hold values from -3 to 3
- gain_two: float32 [384], replicated, may hold values from 0.5 to 2
- second_kernel: bfloat16 [3, 3, 3, 384, 384], replicated, may hold values from -0.0625 to 0.0625
- second_bias: float32 [384], replicated, may hold values from -3 to 3
Outputs:
- decoded: bfloat16 [8, 96, 32, 384], P('tm', None, 'tile')
The draws below stay inside these ranges and needn't reach their ends.
All inputs are finite; a program needn't handle non-finite values.
Results may differ from the reference program's by a relative error of at most 0.0065.
Values may be sent and summed in bfloat16 or wider, within the bound.
No kernel may reach another device: no remote copies, remote signals or barrier semaphores. Data moves between devices by JAX's collectives and lax.ppermute only.
A program may use at most 64 MiB of HBM per device.

```python
import math
import jax
import jax.numpy as jnp
from jax import lax

C = 384
LAT = 16
H = 96
W = 32
FRAMES = 8
TOKENS = 24576


def block_levels(stream_key, extent, shards, least, high):
    def one(axis_at, shards_of):
        steps = jax.random.uniform(jax.random.fold_in(jax.random.fold_in(stream_key, 6), axis_at), (shards_of,), jnp.float32, least / len(shards), high / len(shards))
        return jnp.repeat(jnp.exp(steps), extent[axis_at] // shards_of).reshape((-1,) + (1,) * (len(extent) - axis_at - 1))

    loudness = one(*shards[0])
    for cut in shards[1:]:
        loudness = loudness * one(*cut)
    return loudness


def gaussian(rng, dims, deviation, limit, split=(), kind=jnp.bfloat16):
    array = jax.random.normal(rng, dims, jnp.float32) * deviation
    if len(split) > 0:
        array = block_levels(rng, dims, split, -0.22, 0.18) * array
    return jnp.clip(array, min=-limit, max=limit).astype(kind)


def setup_inputs(seed: int = 0) -> dict:
    seeds = jax.random.split(jax.random.key(seed), 10)
    return {
        "latent_tokens": gaussian(seeds[0], (TOKENS, LAT), 1.0, 6.0, ((0, 32),)),
        "entry_kernel": gaussian(seeds[1], (3, 3, 3, LAT, C), (27 * LAT) ** -0.5, 0.3125),
        "entry_bias": gaussian(seeds[2], (C,), 0.5, 3.0, (), jnp.float32),
        "gain_one": jnp.clip(jnp.exp(jax.random.uniform(seeds[3], (C,), jnp.float32, math.log(0.5), math.log(2.0))), 0.5, 2.0),
        "first_kernel": gaussian(seeds[4], (3, 3, 3, C, C), (27 * C) ** -0.5, 0.0625),
        "first_bias": gaussian(seeds[5], (C,), 0.5, 3.0, (), jnp.float32),
        "gain_two": jnp.clip(jnp.exp(jax.random.uniform(seeds[6], (C,), jnp.float32, math.log(0.5), math.log(2.0))), 0.5, 2.0),
        "second_kernel": gaussian(seeds[7], (3, 3, 3, C, C), (27 * C) ** -0.5, 0.0625),
        "second_bias": gaussian(seeds[8], (C,), 0.5, 3.0, (), jnp.float32),
    }


def causal_conv(field_in, kernel, offset):
    padded = jnp.pad(field_in, ((2, 0), (0, 0), (1, 1), (0, 0)))
    result = lax.conv_general_dilated(padded[None], kernel.astype(jnp.float32), (1, 1, 1), ((0, 0), (1, 1), (0, 0)), dimension_numbers=('NDHWC', 'DHWIO', 'NDHWC'), precision=lax.Precision.HIGHEST)
    return result[0] + offset

def norm_silu(values, gain_vec):
    scaled = values.astype(jnp.float32)
    scaled = scaled * lax.rsqrt(lax.optimization_barrier(jnp.mean(scaled * scaled, axis=-1, keepdims=True)) + 1e-06) * gain_vec
    return jax.nn.silu(scaled).astype(jnp.bfloat16)

def reference(latent_tokens, entry_kernel, entry_bias, gain_one, first_kernel, first_bias, gain_two, second_kernel, second_bias):
    latent = latent_tokens.reshape(FRAMES, H, W, LAT).astype(jnp.float32)
    entry = causal_conv(latent, entry_kernel, entry_bias).astype(jnp.bfloat16)
    first_act = norm_silu(entry, gain_one)
    middle = causal_conv(first_act.astype(jnp.float32), first_kernel, first_bias).astype(jnp.bfloat16)
    second_act = norm_silu(middle, gain_two)
    branch = causal_conv(second_act.astype(jnp.float32), second_kernel, second_bias)
    return (entry.astype(jnp.float32) + branch).astype(jnp.bfloat16)
```

```python
import functools

import jax
import jax.numpy as jnp
from jax import lax
from jax.experimental import pallas as pl
from jax.experimental.pallas import tpu as pltpu
from jax.sharding import PartitionSpec as P

LAT = 16
FR_DEV = 2
H = 96
W_DEV = 4


def shift_from(value, axis, steps):
    count = lax.axis_size(axis)
    pairs = [(i, i + steps) for i in range(max(0, -steps), min(count, count - steps))]
    return lax.ppermute(value, axis, pairs)


def _norm_silu(v, gain):
    scaled = v * lax.rsqrt(jnp.mean(v * v, axis=-1, keepdims=True) + 1e-06) * gain
    return scaled / (1.0 + jnp.exp(-scaled))


def _conv_kernel(mode, x_ref, w_ref, b_ref, e_ref, o_ref, acc_ref):
    d = pl.program_id(0)
    t_out, w_out, rows, co = o_ref.shape
    m = t_out * w_out * rows
    part = None
    for dt in range(3):
        for dj in range(3):
            lhs = x_ref[0, dt : dt + t_out, dj : dj + w_out].reshape(m, x_ref.shape[-1])
            p = jnp.dot(lhs, w_ref[dt, 0, dj], preferred_element_type=jnp.float32)
            part = p if part is None else part + p

    @pl.when(d == 0)
    def _():
        acc_ref[...] = part

    @pl.when(d > 0)
    def _():
        acc_ref[...] += part

    @pl.when(d == 2)
    def _():
        total = acc_ref[...] + b_ref[...]
        if mode == "act":
            mid = total.astype(jnp.bfloat16).astype(jnp.float32)
            res = _norm_silu(mid, e_ref[...])
        else:
            res = e_ref[...].reshape(m, co).astype(jnp.float32) + total
        o_ref[...] = res.astype(o_ref.dtype).reshape(o_ref.shape)


def conv_pallas(mode, shifted, kernel, bias, extra):
    _, tp, wp, rows, c = shifted.shape
    co = kernel.shape[-1]
    t_out, w_out = tp - 2, wp - 2
    out_shape = (t_out, w_out, rows, co)
    if mode == "act":
        e_spec = pl.BlockSpec((1, co), lambda d: (0, 0))
    else:
        e_spec = pl.BlockSpec(out_shape, lambda d: (0, 0, 0, 0))
    flops = 2 * t_out * w_out * rows * 27 * c * co
    return pl.pallas_call(
        functools.partial(_conv_kernel, mode),
        grid=(3,),
        in_specs=[
            pl.BlockSpec((1, tp, wp, rows, c), lambda d: (d, 0, 0, 0, 0)),
            pl.BlockSpec((3, 1, 3, c, co), lambda d: (0, d, 0, 0, 0)),
            pl.BlockSpec((1, co), lambda d: (0, 0)),
            e_spec,
        ],
        out_specs=pl.BlockSpec(out_shape, lambda d: (0, 0, 0, 0)),
        out_shape=jax.ShapeDtypeStruct(out_shape, jnp.bfloat16),
        scratch_shapes=[pltpu.VMEM((t_out * w_out * rows, co), jnp.float32)],
        compiler_params=pltpu.CompilerParams(
            dimension_semantics=("arbitrary",), vmem_limit_bytes=48 * 1024 * 1024
        ),
        cost_estimate=pl.CostEstimate(
            flops=flops,
            transcendentals=0,
            bytes_accessed=shifted.size * 2 + kernel.size * 2 + t_out * w_out * rows * co * 4,
        ),
    )(shifted, kernel, bias.reshape(1, co), extra)


def row_shifts(values):
    padded = jnp.pad(values, ((0, 0), (0, 0), (1, 1), (0, 0)))
    return jnp.stack([padded[:, :, di : di + H] for di in range(3)], axis=0)


def body(
    latent_tokens,
    entry_kernel,
    entry_bias,
    gain_one,
    first_kernel,
    first_bias,
    gain_two,
    second_kernel,
    second_bias,
):
    tiles = lax.axis_size("tile")
    total_cols = W_DEV * tiles
    s = lax.axis_index("tm")
    k = lax.axis_index("tile")
    c = entry_kernel.shape[-1]

    section = lax.all_gather(latent_tokens, "tile", axis=0, tiled=True)
    section = section.reshape(FR_DEV, H, total_cols, LAT)
    section = jnp.pad(section, ((0, 0), (1, 1), (2, 2), (0, 0)))
    slab = lax.dynamic_slice_in_dim(section, k * W_DEV, W_DEV + 4, axis=2)
    back1 = shift_from(slab, "tm", 1)
    back2 = shift_from(slab, "tm", 2)
    lat = jnp.concatenate([back2, back1, slab], axis=0)
    lat = jnp.transpose(lat, (0, 2, 1, 3))

    t_ext, w_ext = FR_DEV + 2, W_DEV + 2
    cols = []
    for dt in range(3):
        for di in range(3):
            for dj in range(3):
                cols.append(lat[dt : dt + t_ext, dj : dj + w_ext, di : di + H, :])
    patches = jnp.concatenate(cols, axis=-1)
    entry_ext = (
        jnp.dot(
            patches.reshape(-1, 27 * LAT),
            entry_kernel.reshape(27 * LAT, c),
            preferred_element_type=jnp.float32,
        )
        + entry_bias
    ).astype(jnp.bfloat16)
    entry_ext = entry_ext.reshape(t_ext, w_ext, H, c)
    entry_own = entry_ext[2:, 1 : 1 + W_DEV]

    frame_ok = (s * FR_DEV - 2 + jnp.arange(t_ext)) >= 0
    col_id = k * W_DEV - 1 + jnp.arange(w_ext)
    col_ok = (col_id >= 0) & (col_id < total_cols)
    ok = frame_ok[:, None, None, None] & col_ok[None, :, None, None]
    first_act = jnp.where(ok, _norm_silu(entry_ext.astype(jnp.float32), gain_one), 0.0)
    first_act = first_act.astype(jnp.bfloat16)

    second_act = conv_pallas(
        "act", row_shifts(first_act), first_kernel, first_bias, gain_two.reshape(1, c)
    )

    left = shift_from(second_act[:, W_DEV - 1 :], "tile", 1)
    right = shift_from(second_act[:, :1], "tile", -1)
    colext = jnp.concatenate([left, second_act, right], axis=1)
    prev = shift_from(colext, "tm", 1)
    ext2 = jnp.concatenate([prev, colext], axis=0)

    decoded = conv_pallas("res", row_shifts(ext2), second_kernel, second_bias, entry_own)
    return jnp.transpose(decoded, (0, 2, 1, 3))


def solution(mesh):
    in_specs = (P(("tm", "tile"), None), P(), P(), P(), P(), P(), P(), P(), P())
    out_specs = P("tm", None, "tile", None)
    return jax.shard_map(body, mesh=mesh, in_specs=in_specs, out_specs=out_specs, check_vma=False)
```

```python
import functools

import jax
import jax.numpy as jnp
from jax import lax
from jax.experimental import pallas as pl
from jax.experimental.pallas import tpu as pltpu
from jax.sharding import PartitionSpec as P

LAT = 16
FR_DEV = 2
H = 96
W_DEV = 4


def shift_from(value, axis, steps):
    count = lax.axis_size(axis)
    pairs = [(i, i + steps) for i in range(max(0, -steps), min(count, count - steps))]
    return lax.ppermute(value, axis, pairs)


def _norm_silu(v, gain):
    scaled = v * lax.rsqrt(jnp.mean(v * v, axis=-1, keepdims=True) + 1e-06) * gain
    return scaled / (1.0 + jnp.exp(-scaled))


def _conv_kernel(mode, x_ref, w_ref, b_ref, e_ref, o_ref, acc_ref):
    d = pl.program_id(0)
    t_out, w_out, rows, co = o_ref.shape
    m = t_out * w_out * rows
    part = None
    for dt in range(3):
        for dj in range(3):
            lhs = x_ref[0, dt : dt + t_out, dj : dj + w_out].reshape(m, x_ref.shape[-1])
            p = jnp.dot(lhs, w_ref[dt, 0, dj], preferred_element_type=jnp.float32)
            part = p if part is None else part + p

    @pl.when(d == 0)
    def _():
        acc_ref[...] = part

    @pl.when(d > 0)
    def _():
        acc_ref[...] += part

    @pl.when(d == 2)
    def _():
        total = acc_ref[...] + b_ref[...]
        if mode == "act":
            mid = total.astype(jnp.bfloat16).astype(jnp.float32)
            res = _norm_silu(mid, e_ref[...])
        else:
            res = e_ref[...].reshape(m, co).astype(jnp.float32) + total
        o_ref[...] = res.astype(o_ref.dtype).reshape(o_ref.shape)


def conv_pallas(mode, shifted, kernel, bias, extra):
    _, tp, wp, rows, c = shifted.shape
    co = kernel.shape[-1]
    t_out, w_out = tp - 2, wp - 2
    out_shape = (t_out, w_out, rows, co)
    if mode == "act":
        e_spec = pl.BlockSpec((1, co), lambda d: (0, 0))
    else:
        e_spec = pl.BlockSpec(out_shape, lambda d: (0, 0, 0, 0))
    flops = 2 * t_out * w_out * rows * 27 * c * co
    return pl.pallas_call(
        functools.partial(_conv_kernel, mode),
        grid=(3,),
        in_specs=[
            pl.BlockSpec((1, tp, wp, rows, c), lambda d: (d, 0, 0, 0, 0)),
            pl.BlockSpec((3, 1, 3, c, co), lambda d: (0, d, 0, 0, 0)),
            pl.BlockSpec((1, co), lambda d: (0, 0)),
            e_spec,
        ],
        out_specs=pl.BlockSpec(out_shape, lambda d: (0, 0, 0, 0)),
        out_shape=jax.ShapeDtypeStruct(out_shape, jnp.bfloat16),
        scratch_shapes=[pltpu.VMEM((t_out * w_out * rows, co), jnp.float32)],
        compiler_params=pltpu.CompilerParams(
            dimension_semantics=("arbitrary",), vmem_limit_bytes=48 * 1024 * 1024
        ),
        cost_estimate=pl.CostEstimate(
            flops=flops,
            transcendentals=0,
            bytes_accessed=shifted.size * 2 + kernel.size * 2 + t_out * w_out * rows * co * 4,
        ),
    )(shifted, kernel, bias.reshape(1, co), extra)


def row_shifts(values):
    padded = jnp.pad(values, ((0, 0), (0, 0), (1, 1), (0, 0)))
    return jnp.stack([padded[:, :, di : di + H] for di in range(3)], axis=0)


def shift2(value, ds, dk):
    n_tm, n_tile = lax.axis_size("tm"), lax.axis_size("tile")
    pairs = []
    for s in range(n_tm):
        for k in range(n_tile):
            if 0 <= s + ds < n_tm and 0 <= k + dk < n_tile:
                pairs.append((s * n_tile + k, (s + ds) * n_tile + k + dk))
    return lax.ppermute(value, ("tm", "tile"), pairs)


def shift2_ring(value_for, ds, dk):
    n_tm, n_tile = lax.axis_size("tm"), lax.axis_size("tile")
    k = lax.axis_index("tile")
    value = value_for((k + dk) % n_tile)
    pairs = []
    for s in range(n_tm - ds):
        for kk in range(n_tile):
            pairs.append((s * n_tile + kk, (s + ds) * n_tile + (kk + dk) % n_tile))
    return lax.ppermute(value, ("tm", "tile"), pairs)


def gather_latent(latent_tokens, total_cols):
    n_tile = lax.axis_size("tile")
    k = lax.axis_index("tile")
    rows_per = FR_DEV * H // n_tile
    strip = latent_tokens.reshape(rows_per, total_cols, LAT)
    strip = jnp.pad(strip, ((0, 0), (2, 2), (0, 0)))

    def cols_for(target):
        return lax.dynamic_slice_in_dim(strip, target * W_DEV, W_DEV + 4, axis=1)

    sections = []
    for ds in (2, 1, 0):
        rel = []
        for dk in range(n_tile):
            if ds == 0 and dk == 0:
                rel.append(cols_for(k))
            else:
                rel.append(shift2_ring(cols_for, ds, dk))
        rev = jnp.stack([rel[(-m) % n_tile] for m in range(n_tile)], axis=0)
        sections.append(jnp.roll(rev, k, axis=0))
    pieces = jnp.concatenate(sections, axis=0)
    return pieces.reshape(3 * FR_DEV, H, W_DEV + 4, LAT)


def body(
    latent_tokens,
    entry_kernel,
    entry_bias,
    gain_one,
    first_kernel,
    first_bias,
    gain_two,
    second_kernel,
    second_bias,
):
    tiles = lax.axis_size("tile")
    total_cols = W_DEV * tiles
    s = lax.axis_index("tm")
    k = lax.axis_index("tile")
    c = entry_kernel.shape[-1]
    t_ext, w_ext = FR_DEV + 2, W_DEV + 2

    lat = gather_latent(latent_tokens, total_cols)
    lat = jnp.pad(lat, ((0, 0), (1, 1), (0, 0), (0, 0)))
    lat = lat.reshape(3 * FR_DEV, H + 2, (W_DEV + 4) * LAT)

    patches = jnp.concatenate(
        [lat[dt : dt + t_ext, di : di + H] for dt in range(3) for di in range(3)], axis=-1
    )
    band = jnp.stack(
        [
            jnp.pad(entry_kernel, ((0, 0), (0, 0), (j, w_ext - 1 - j), (0, 0), (0, 0)))
            for j in range(w_ext)
        ],
        axis=-2,
    )
    entry_ext = jnp.dot(
        patches.reshape(t_ext * H, -1),
        band.reshape(9 * (W_DEV + 4) * LAT, w_ext * c),
        preferred_element_type=jnp.float32,
    ).reshape(t_ext, H, w_ext, c) + entry_bias
    entry_ext = jnp.transpose(entry_ext.astype(jnp.bfloat16), (0, 2, 1, 3))
    entry_own = entry_ext[2:, 1 : 1 + W_DEV]

    frame_ok = (s * FR_DEV - 2 + jnp.arange(t_ext)) >= 0
    col_id = k * W_DEV - 1 + jnp.arange(w_ext)
    col_ok = (col_id >= 0) & (col_id < total_cols)
    ok = frame_ok[:, None, None, None] & col_ok[None, :, None, None]
    first_act = jnp.where(ok, _norm_silu(entry_ext.astype(jnp.float32), gain_one), 0.0)
    first_act = first_act.astype(jnp.bfloat16)

    second_act = conv_pallas(
        "act", row_shifts(first_act), first_kernel, first_bias, gain_two.reshape(1, c)
    )

    last, first = second_act[:, W_DEV - 1 :], second_act[:, :1]
    own_row = [shift2(last, 0, 1), second_act, shift2(first, 0, -1)]
    prev_row = [shift2(last, 1, 1), shift2(second_act, 1, 0), shift2(first, 1, -1)]
    ext2 = jnp.concatenate(
        [jnp.concatenate(prev_row, axis=1), jnp.concatenate(own_row, axis=1)], axis=0
    )

    decoded = conv_pallas("res", row_shifts(ext2), second_kernel, second_bias, entry_own)
    return jnp.transpose(decoded, (0, 2, 1, 3))


def solution(mesh):
    in_specs = (P(("tm", "tile"), None), P(), P(), P(), P(), P(), P(), P(), P())
    out_specs = P("tm", None, "tile", None)
    return jax.shard_map(body, mesh=mesh, in_specs=in_specs, out_specs=out_specs, check_vma=False)
```

```python
import functools

import jax
import jax.numpy as jnp
from jax import lax
from jax.experimental import pallas as pl
from jax.experimental.pallas import tpu as pltpu
from jax.sharding import PartitionSpec as P

LAT = 16
FR_DEV = 2
H = 96
W_DEV = 4


def shift_from(value, axis, steps):
    count = lax.axis_size(axis)
    pairs = [(i, i + steps) for i in range(max(0, -steps), min(count, count - steps))]
    return lax.ppermute(value, axis, pairs)


def _norm_silu(v, gain):
    scaled = v * lax.rsqrt(jnp.mean(v * v, axis=-1, keepdims=True) + 1e-06) * gain
    return scaled / (1.0 + jnp.exp(-scaled))


def _conv_kernel(mode, x_ref, w_ref, b_ref, e_ref, o_ref, acc_ref):
    d = pl.program_id(0)
    t_out, w_out, rows, co = o_ref.shape
    m = t_out * w_out * rows
    part = None
    for dt in range(3):
        for dj in range(3):
            lhs = x_ref[0, dt : dt + t_out, dj : dj + w_out].reshape(m, x_ref.shape[-1])
            p = jnp.dot(lhs, w_ref[dt, 0, dj], preferred_element_type=jnp.float32)
            part = p if part is None else part + p

    @pl.when(d == 0)
    def _():
        acc_ref[...] = part

    @pl.when(d > 0)
    def _():
        acc_ref[...] += part

    @pl.when(d == 2)
    def _():
        total = acc_ref[...] + b_ref[...]
        if mode == "act":
            mid = total.astype(jnp.bfloat16).astype(jnp.float32)
            res = _norm_silu(mid, e_ref[...])
        else:
            res = e_ref[...].reshape(m, co).astype(jnp.float32) + total
        o_ref[...] = res.astype(o_ref.dtype).reshape(o_ref.shape)


def conv_pallas(mode, shifted, kernel, bias, extra):
    _, tp, wp, rows, c = shifted.shape
    co = kernel.shape[-1]
    t_out, w_out = tp - 2, wp - 2
    out_shape = (t_out, w_out, rows, co)
    if mode == "act":
        e_spec = pl.BlockSpec((1, co), lambda d: (0, 0))
    else:
        e_spec = pl.BlockSpec(out_shape, lambda d: (0, 0, 0, 0))
    flops = 2 * t_out * w_out * rows * 27 * c * co
    return pl.pallas_call(
        functools.partial(_conv_kernel, mode),
        grid=(3,),
        in_specs=[
            pl.BlockSpec((1, tp, wp, rows, c), lambda d: (d, 0, 0, 0, 0)),
            pl.BlockSpec((3, 1, 3, c, co), lambda d: (0, d, 0, 0, 0)),
            pl.BlockSpec((1, co), lambda d: (0, 0)),
            e_spec,
        ],
        out_specs=pl.BlockSpec(out_shape, lambda d: (0, 0, 0, 0)),
        out_shape=jax.ShapeDtypeStruct(out_shape, jnp.bfloat16),
        scratch_shapes=[pltpu.VMEM((t_out * w_out * rows, co), jnp.float32)],
        compiler_params=pltpu.CompilerParams(
            dimension_semantics=("arbitrary",), vmem_limit_bytes=48 * 1024 * 1024
        ),
        cost_estimate=pl.CostEstimate(
            flops=flops,
            transcendentals=0,
            bytes_accessed=shifted.size * 2 + kernel.size * 2 + t_out * w_out * rows * co * 4,
        ),
    )(shifted, kernel, bias.reshape(1, co), extra)


def row_shifts(values):
    padded = jnp.pad(values, ((0, 0), (0, 0), (1, 1), (0, 0)))
    return jnp.stack([padded[:, :, di : di + H] for di in range(3)], axis=0)


def shift2(value, ds, dk):
    n_tm, n_tile = lax.axis_size("tm"), lax.axis_size("tile")
    pairs = []
    for s in range(n_tm):
        for k in range(n_tile):
            if 0 <= s + ds < n_tm and 0 <= k + dk < n_tile:
                pairs.append((s * n_tile + k, (s + ds) * n_tile + k + dk))
    return lax.ppermute(value, ("tm", "tile"), pairs)


def gather_latent(latent_tokens, total_cols):
    n_tile = lax.axis_size("tile")
    rows_per = FR_DEV * H // n_tile
    strip = latent_tokens.reshape(rows_per, total_cols, LAT)
    strip = jnp.pad(strip, ((0, 0), (2, 2), (0, 0)))
    windows = jnp.stack(
        [strip[:, t * W_DEV : t * W_DEV + W_DEV + 4] for t in range(n_tile)], axis=0
    )
    section = lax.all_to_all(windows, "tile", 0, 0, tiled=True)
    section = section.reshape(FR_DEV, H, W_DEV + 4, LAT)
    back1 = shift_from(section, "tm", 1)
    back2 = shift_from(section, "tm", 2)
    return jnp.concatenate([back2, back1, section], axis=0)


def body(
    latent_tokens,
    entry_kernel,
    entry_bias,
    gain_one,
    first_kernel,
    first_bias,
    gain_two,
    second_kernel,
    second_bias,
):
    tiles = lax.axis_size("tile")
    total_cols = W_DEV * tiles
    s = lax.axis_index("tm")
    k = lax.axis_index("tile")
    c = entry_kernel.shape[-1]
    t_ext, w_ext = FR_DEV + 2, W_DEV + 2

    lat = gather_latent(latent_tokens, total_cols)
    lat = jnp.pad(lat, ((0, 0), (1, 1), (0, 0), (0, 0)))
    lat = lat.reshape(3 * FR_DEV, H + 2, (W_DEV + 4) * LAT)

    patches = jnp.concatenate(
        [lat[dt : dt + t_ext, di : di + H] for dt in range(3) for di in range(3)], axis=-1
    )
    band = jnp.concatenate(
        [
            jnp.pad(
                entry_kernel, ((0, 0), (0, 0), (j, w_ext - 1 - j), (0, 0), (0, 0))
            ).reshape(9 * (W_DEV + 4) * LAT, c)
            for j in range(w_ext)
        ],
        axis=-1,
    )
    entry_ext = jnp.dot(
        patches.reshape(t_ext * H, -1),
        band,
        preferred_element_type=jnp.float32,
    ).reshape(t_ext, H, w_ext, c) + entry_bias
    entry_ext = jnp.transpose(entry_ext.astype(jnp.bfloat16), (0, 2, 1, 3))
    entry_own = entry_ext[2:, 1 : 1 + W_DEV]

    frame_ok = (s * FR_DEV - 2 + jnp.arange(t_ext)) >= 0
    col_id = k * W_DEV - 1 + jnp.arange(w_ext)
    col_ok = (col_id >= 0) & (col_id < total_cols)
    ok = frame_ok[:, None, None, None] & col_ok[None, :, None, None]
    first_act = jnp.where(ok, _norm_silu(entry_ext.astype(jnp.float32), gain_one), 0.0)
    first_act = first_act.astype(jnp.bfloat16)

    second_act = conv_pallas(
        "act", row_shifts(first_act), first_kernel, first_bias, gain_two.reshape(1, c)
    )

    last, first = second_act[:, W_DEV - 1 :], second_act[:, :1]
    own_row = [shift2(last, 0, 1), second_act, shift2(first, 0, -1)]
    prev_row = [shift2(last, 1, 1), shift2(second_act, 1, 0), shift2(first, 1, -1)]
    ext2 = jnp.concatenate(
        [jnp.concatenate(prev_row, axis=1), jnp.concatenate(own_row, axis=1)], axis=0
    )

    decoded = conv_pallas("res", row_shifts(ext2), second_kernel, second_bias, entry_own)
    return jnp.transpose(decoded, (0, 2, 1, 3))


def solution(mesh):
    in_specs = (P(("tm", "tile"), None), P(), P(), P(), P(), P(), P(), P(), P())
    out_specs = P("tm", None, "tile", None)
    return jax.shard_map(body, mesh=mesh, in_specs=in_specs, out_specs=out_specs, check_vma=False)
```

```python
import functools

import jax
import jax.numpy as jnp
from jax import lax
from jax.experimental import pallas as pl
from jax.experimental.pallas import tpu as pltpu
from jax.sharding import PartitionSpec as P

LAT = 16
FR_DEV = 2
H = 96
W_DEV = 4


def shift_from(value, axis, steps):
    count = lax.axis_size(axis)
    pairs = [(i, i + steps) for i in range(max(0, -steps), min(count, count - steps))]
    return lax.ppermute(value, axis, pairs)


def _norm_silu(v, gain):
    scaled = v * lax.rsqrt(jnp.mean(v * v, axis=-1, keepdims=True) + 1e-06) * gain
    return scaled / (1.0 + jnp.exp(-scaled))


def _conv_kernel(mode, x_ref, w_ref, b_ref, e_ref, o_ref, acc_ref):
    d = pl.program_id(0)
    t_out, w_out, rows, co = o_ref.shape
    m = t_out * w_out * rows
    part = None
    for dt in range(3):
        for dj in range(3):
            lhs = x_ref[dt : dt + t_out, dj : dj + w_out].reshape(m, x_ref.shape[-1])
            p = jnp.dot(lhs, w_ref[dt, 0, dj], preferred_element_type=jnp.float32)
            part = p if part is None else part + p
    row = lax.broadcasted_iota(jnp.int32, (t_out * w_out, rows, co), 1).reshape(m, co)

    @pl.when(d == 0)
    def _():
        acc_ref[...] = jnp.where(row == 0, 0.0, pltpu.roll(part, 1, 0))

    @pl.when(d == 1)
    def _():
        acc_ref[...] += part

    @pl.when(d == 2)
    def _():
        below = jnp.where(row == rows - 1, 0.0, pltpu.roll(part, m - 1, 0))
        total = acc_ref[...] + below + b_ref[...]
        if mode == "act":
            mid = total.astype(jnp.bfloat16).astype(jnp.float32)
            res = _norm_silu(mid, e_ref[...])
        else:
            res = e_ref[...].reshape(m, co).astype(jnp.float32) + total
        o_ref[...] = res.astype(o_ref.dtype).reshape(o_ref.shape)


def conv_pallas(mode, field, kernel, bias, extra):
    tp, wp, rows, c = field.shape
    co = kernel.shape[-1]
    t_out, w_out = tp - 2, wp - 2
    out_shape = (t_out, w_out, rows, co)
    if mode == "act":
        e_spec = pl.BlockSpec((1, co), lambda d: (0, 0))
    else:
        e_spec = pl.BlockSpec(out_shape, lambda d: (0, 0, 0, 0))
    flops = 2 * t_out * w_out * rows * 27 * c * co
    return pl.pallas_call(
        functools.partial(_conv_kernel, mode),
        grid=(3,),
        in_specs=[
            pl.BlockSpec((tp, wp, rows, c), lambda d: (0, 0, 0, 0)),
            pl.BlockSpec((3, 1, 3, c, co), lambda d: (0, d, 0, 0, 0)),
            pl.BlockSpec((1, co), lambda d: (0, 0)),
            e_spec,
        ],
        out_specs=pl.BlockSpec(out_shape, lambda d: (0, 0, 0, 0)),
        out_shape=jax.ShapeDtypeStruct(out_shape, jnp.bfloat16),
        scratch_shapes=[pltpu.VMEM((t_out * w_out * rows, co), jnp.float32)],
        compiler_params=pltpu.CompilerParams(
            dimension_semantics=("arbitrary",), vmem_limit_bytes=48 * 1024 * 1024
        ),
        cost_estimate=pl.CostEstimate(
            flops=flops,
            transcendentals=0,
            bytes_accessed=field.size * 2 + kernel.size * 2 + t_out * w_out * rows * co * 4,
        ),
    )(field, kernel, bias.reshape(1, co), extra)


def _entry_kernel(lat_ref, k_ref, b_ref, g_ref, ok_ref, act_ref, own_ref, band_ref, patch_ref):
    t_ext, w_ext, rows, c = act_ref.shape
    lanes = lat_ref.shape[-1]
    lat_ch = k_ref.shape[1]
    band_ref[...] = jnp.zeros(band_ref.shape, band_ref.dtype)
    for dt in range(3):
        for di in range(3):
            p = dt * 3 + di
            for dj in range(3):
                for j in range(w_ext):
                    r0 = p * lanes + (j + dj) * lat_ch
                    band_ref[r0 : r0 + lat_ch, j * c : (j + 1) * c] = k_ref[p * 3 + dj]
            slab = lat_ref[dt : dt + t_ext, di : di + rows, :].reshape(t_ext * rows, lanes)
            patch_ref[:, p * lanes : (p + 1) * lanes] = slab.astype(patch_ref.dtype)
    for j in range(w_ext):
        e = jnp.dot(
            patch_ref[...], band_ref[:, j * c : (j + 1) * c], preferred_element_type=jnp.float32
        )
        e = (e + b_ref[...]).astype(jnp.bfloat16)
        if 1 <= j <= w_ext - 2:
            own_ref[:, j - 1] = e.reshape(t_ext, rows, c)[t_ext - FR_DEV :]
        fa = _norm_silu(e.astype(jnp.float32), g_ref[...]).reshape(t_ext, rows, c)
        for t in range(t_ext):
            act_ref[t, j] = (fa[t] * ok_ref[t * w_ext + j]).astype(act_ref.dtype)


def entry_pallas(lat, entry_kernel, entry_bias, gain_one, ok):
    t_ext, w_ext = FR_DEV + 2, W_DEV + 2
    lanes = lat.shape[-1]
    c = entry_kernel.shape[-1]
    kr = entry_kernel.reshape(27, LAT, c)
    vmem = pl.BlockSpec(memory_space=pltpu.VMEM)
    return pl.pallas_call(
        _entry_kernel,
        in_specs=[vmem, vmem, vmem, vmem, pl.BlockSpec(memory_space=pltpu.SMEM)],
        out_specs=(vmem, vmem),
        out_shape=(
            jax.ShapeDtypeStruct((t_ext, w_ext, H, c), jnp.bfloat16),
            jax.ShapeDtypeStruct((FR_DEV, W_DEV, H, c), jnp.bfloat16),
        ),
        scratch_shapes=[
            pltpu.VMEM((9 * lanes, w_ext * c), jnp.bfloat16),
            pltpu.VMEM((t_ext * H, 9 * lanes), jnp.bfloat16),
        ],
        compiler_params=pltpu.CompilerParams(vmem_limit_bytes=48 * 1024 * 1024),
        cost_estimate=pl.CostEstimate(
            flops=2 * t_ext * H * 9 * lanes * w_ext * c,
            transcendentals=t_ext * w_ext * H * c,
            bytes_accessed=lat.size * 4 + kr.size * 2 + (t_ext * w_ext + FR_DEV * W_DEV) * H * c * 2,
        ),
    )(lat, kr, entry_bias.reshape(1, c), gain_one.reshape(1, c), ok)


def shift2(value, ds, dk):
    n_tm, n_tile = lax.axis_size("tm"), lax.axis_size("tile")
    pairs = []
    for s in range(n_tm):
        for k in range(n_tile):
            if 0 <= s + ds < n_tm and 0 <= k + dk < n_tile:
                pairs.append((s * n_tile + k, (s + ds) * n_tile + k + dk))
    return lax.ppermute(value, ("tm", "tile"), pairs)


def gather_latent(latent_tokens, total_cols):
    n_tile = lax.axis_size("tile")
    rows_per = FR_DEV * H // n_tile
    strip = latent_tokens.reshape(rows_per, total_cols, LAT)
    strip = jnp.pad(strip, ((0, 0), (2, 2), (0, 0)))
    windows = jnp.stack(
        [strip[:, t * W_DEV : t * W_DEV + W_DEV + 4] for t in range(n_tile)], axis=0
    )
    section = lax.all_to_all(windows, "tile", 0, 0, tiled=True)
    section = section.reshape(FR_DEV, H, W_DEV + 4, LAT)
    back1 = shift_from(section, "tm", 1)
    back2 = shift_from(section, "tm", 2)
    return jnp.concatenate([back2, back1, section], axis=0)


def body(
    latent_tokens,
    entry_kernel,
    entry_bias,
    gain_one,
    first_kernel,
    first_bias,
    gain_two,
    second_kernel,
    second_bias,
):
    tiles = lax.axis_size("tile")
    total_cols = W_DEV * tiles
    s = lax.axis_index("tm")
    k = lax.axis_index("tile")
    c = entry_kernel.shape[-1]
    t_ext, w_ext = FR_DEV + 2, W_DEV + 2

    lat = gather_latent(latent_tokens, total_cols)
    lat = jnp.pad(lat, ((0, 0), (1, 1), (0, 0), (0, 0)))
    lat = lat.reshape(3 * FR_DEV, H + 2, (W_DEV + 4) * LAT).astype(jnp.float32)

    frame_ok = (s * FR_DEV - 2 + jnp.arange(t_ext)) >= 0
    col_id = k * W_DEV - 1 + jnp.arange(w_ext)
    col_ok = (col_id >= 0) & (col_id < total_cols)
    ok = (frame_ok[:, None] & col_ok[None, :]).astype(jnp.float32).reshape(-1)
    first_act, entry_own = entry_pallas(lat, entry_kernel, entry_bias, gain_one, ok)

    second_act = conv_pallas("act", first_act, first_kernel, first_bias, gain_two.reshape(1, c))

    last, first = second_act[:, W_DEV - 1 :], second_act[:, :1]
    own_row = [shift2(last, 0, 1), second_act, shift2(first, 0, -1)]
    prev_row = [shift2(last, 1, 1), shift2(second_act, 1, 0), shift2(first, 1, -1)]
    ext2 = jnp.concatenate(
        [jnp.concatenate(prev_row, axis=1), jnp.concatenate(own_row, axis=1)], axis=0
    )

    decoded = conv_pallas("res", ext2, second_kernel, second_bias, entry_own)
    return jnp.transpose(decoded, (0, 2, 1, 3))


def solution(mesh):
    in_specs = (P(("tm", "tile"), None), P(), P(), P(), P(), P(), P(), P(), P())
    out_specs = P("tm", None, "tile", None)
    return jax.shard_map(body, mesh=mesh, in_specs=in_specs, out_specs=out_specs, check_vma=False)
```

```python
import functools

import jax
import jax.numpy as jnp
from jax import lax
from jax.experimental import pallas as pl
from jax.experimental.pallas import tpu as pltpu
from jax.sharding import PartitionSpec as P

LAT = 16
FR_DEV = 2
H = 96
W_DEV = 4


def shift_from(value, axis, steps):
    count = lax.axis_size(axis)
    pairs = [(i, i + steps) for i in range(max(0, -steps), min(count, count - steps))]
    return lax.ppermute(value, axis, pairs)


def _norm_silu(v, gain):
    scaled = v * lax.rsqrt(jnp.mean(v * v, axis=-1, keepdims=True) + 1e-06) * gain
    return scaled / (1.0 + jnp.exp(-scaled))


def _conv_kernel(terms, mode, x_ref, w_ref, b_ref, e_ref, *rest):
    if mode == "res":
        p_ref, o_ref, acc_ref = rest
    else:
        o_ref, acc_ref = rest
    d = pl.program_id(0)
    t_out, w_out, rows, co = o_ref.shape
    fm = w_out * rows

    @pl.when(d == 0)
    def _():
        acc_ref[...] = jnp.zeros(acc_ref.shape, acc_ref.dtype)

    for o0, n, dt, i0 in terms:
        m = n * fm
        val = None
        for dj in range(3):
            lhs = x_ref[i0 : i0 + n, dj : dj + w_out].reshape(m, x_ref.shape[-1])
            p = jnp.dot(lhs, w_ref[dt, 0, dj], preferred_element_type=jnp.float32)
            val = p if val is None else val + p
        row = lax.broadcasted_iota(jnp.int32, (n * w_out, rows, co), 1).reshape(m, co)
        lo, hi = o0 * fm, o0 * fm + m

        @pl.when(d == 0)
        def _():
            acc_ref[lo:hi] += jnp.where(row == 0, 0.0, pltpu.roll(val, 1, 0))

        @pl.when(d == 1)
        def _():
            acc_ref[lo:hi] += val

        @pl.when(d == 2)
        def _():
            acc_ref[lo:hi] += jnp.where(row == rows - 1, 0.0, pltpu.roll(val, m - 1, 0))

    @pl.when(d == 2)
    def _():
        total = acc_ref[...]
        if mode == "act":
            mid = (total + b_ref[...]).astype(jnp.bfloat16).astype(jnp.float32)
            res = _norm_silu(mid, e_ref[...])
        elif mode == "part":
            res = total
        else:
            branch = p_ref[...].reshape(total.shape) + total + b_ref[...]
            res = e_ref[...].reshape(total.shape).astype(jnp.float32) + branch
        o_ref[...] = res.astype(o_ref.dtype).reshape(o_ref.shape)


def conv_pallas(mode, terms, field, kernel, bias, extra, partial=None):
    _, wp, rows, c = field.shape
    co = kernel.shape[-1]
    t_out, w_out = FR_DEV, wp - 2
    out_shape = (t_out, w_out, rows, co)
    whole = pl.BlockSpec(out_shape, lambda d: (0, 0, 0, 0))
    e_spec = pl.BlockSpec((1, co), lambda d: (0, 0)) if mode == "act" else whole
    in_specs = [
        pl.BlockSpec(field.shape, lambda d: (0, 0, 0, 0)),
        pl.BlockSpec((3, 1, 3, c, co), lambda d: (0, d, 0, 0, 0)),
        pl.BlockSpec((1, co), lambda d: (0, 0)),
        e_spec,
    ]
    args = [field, kernel, bias.reshape(1, co), extra]
    if partial is not None:
        in_specs.append(whole)
        args.append(partial)
    out_dtype = jnp.float32 if mode == "part" else jnp.bfloat16
    flops = 2 * sum(n for _, n, _, _ in terms) * w_out * rows * 9 * c * co
    return pl.pallas_call(
        functools.partial(_conv_kernel, tuple(terms), mode),
        grid=(3,),
        in_specs=in_specs,
        out_specs=whole,
        out_shape=jax.ShapeDtypeStruct(out_shape, out_dtype),
        scratch_shapes=[pltpu.VMEM((t_out * w_out * rows, co), jnp.float32)],
        compiler_params=pltpu.CompilerParams(
            dimension_semantics=("arbitrary",), vmem_limit_bytes=48 * 1024 * 1024
        ),
        cost_estimate=pl.CostEstimate(
            flops=flops,
            transcendentals=0,
            bytes_accessed=field.size * 2 + kernel.size * 2 + t_out * w_out * rows * co * 8,
        ),
    )(*args)


def _entry_kernel(lat_ref, k_ref, b_ref, g_ref, ok_ref, act_ref, own_ref, band_ref, patch_ref):
    t_ext, w_ext, rows, c = act_ref.shape
    lanes = lat_ref.shape[-1]
    lat_ch = k_ref.shape[1]
    band_ref[...] = jnp.zeros(band_ref.shape, band_ref.dtype)
    for dt in range(3):
        for di in range(3):
            p = dt * 3 + di
            for dj in range(3):
                for j in range(w_ext):
                    r0 = p * lanes + (j + dj) * lat_ch
                    band_ref[r0 : r0 + lat_ch, j * c : (j + 1) * c] = k_ref[p * 3 + dj]
            slab = lat_ref[dt : dt + t_ext, di : di + rows, :].reshape(t_ext * rows, lanes)
            patch_ref[:, p * lanes : (p + 1) * lanes] = slab.astype(patch_ref.dtype)
    for j in range(w_ext):
        e = jnp.dot(
            patch_ref[...], band_ref[:, j * c : (j + 1) * c], preferred_element_type=jnp.float32
        )
        e = (e + b_ref[...]).astype(jnp.bfloat16)
        if 1 <= j <= w_ext - 2:
            own_ref[:, j - 1] = e.reshape(t_ext, rows, c)[t_ext - FR_DEV :]
        fa = _norm_silu(e.astype(jnp.float32), g_ref[...]).reshape(t_ext, rows, c)
        for t in range(t_ext):
            act_ref[t, j] = (fa[t] * ok_ref[t * w_ext + j]).astype(act_ref.dtype)


def entry_pallas(lat, entry_kernel, entry_bias, gain_one, ok):
    t_ext, w_ext = FR_DEV + 2, W_DEV + 2
    lanes = lat.shape[-1]
    c = entry_kernel.shape[-1]
    kr = entry_kernel.reshape(27, LAT, c)
    vmem = pl.BlockSpec(memory_space=pltpu.VMEM)
    return pl.pallas_call(
        _entry_kernel,
        in_specs=[vmem, vmem, vmem, vmem, pl.BlockSpec(memory_space=pltpu.SMEM)],
        out_specs=(vmem, vmem),
        out_shape=(
            jax.ShapeDtypeStruct((t_ext, w_ext, H, c), jnp.bfloat16),
            jax.ShapeDtypeStruct((FR_DEV, W_DEV, H, c), jnp.bfloat16),
        ),
        scratch_shapes=[
            pltpu.VMEM((9 * lanes, w_ext * c), jnp.bfloat16),
            pltpu.VMEM((t_ext * H, 9 * lanes), jnp.bfloat16),
        ],
        compiler_params=pltpu.CompilerParams(vmem_limit_bytes=48 * 1024 * 1024),
        cost_estimate=pl.CostEstimate(
            flops=2 * t_ext * H * 9 * lanes * w_ext * c,
            transcendentals=t_ext * w_ext * H * c,
            bytes_accessed=lat.size * 4 + kr.size * 2 + (t_ext * w_ext + FR_DEV * W_DEV) * H * c * 2,
        ),
    )(lat, kr, entry_bias.reshape(1, c), gain_one.reshape(1, c), ok)


def shift2(value, ds, dk):
    n_tm, n_tile = lax.axis_size("tm"), lax.axis_size("tile")
    pairs = []
    for s in range(n_tm):
        for k in range(n_tile):
            if 0 <= s + ds < n_tm and 0 <= k + dk < n_tile:
                pairs.append((s * n_tile + k, (s + ds) * n_tile + k + dk))
    return lax.ppermute(value, ("tm", "tile"), pairs)


def gather_latent(latent_tokens, total_cols):
    n_tile = lax.axis_size("tile")
    rows_per = FR_DEV * H // n_tile
    strip = latent_tokens.reshape(rows_per, total_cols, LAT)
    strip = jnp.pad(strip, ((0, 0), (2, 2), (0, 0)))
    windows = jnp.stack(
        [strip[:, t * W_DEV : t * W_DEV + W_DEV + 4] for t in range(n_tile)], axis=0
    )
    section = lax.all_to_all(windows, "tile", 0, 0, tiled=True)
    section = section.reshape(FR_DEV, H, W_DEV + 4, LAT)
    back1 = shift_from(section, "tm", 1)
    back2 = shift_from(section, "tm", 2)
    return jnp.concatenate([back2, back1, section], axis=0)


def body(
    latent_tokens,
    entry_kernel,
    entry_bias,
    gain_one,
    first_kernel,
    first_bias,
    gain_two,
    second_kernel,
    second_bias,
):
    tiles = lax.axis_size("tile")
    total_cols = W_DEV * tiles
    s = lax.axis_index("tm")
    k = lax.axis_index("tile")
    c = entry_kernel.shape[-1]
    t_ext, w_ext = FR_DEV + 2, W_DEV + 2

    lat = gather_latent(latent_tokens, total_cols)
    lat = jnp.pad(lat, ((0, 0), (1, 1), (0, 0), (0, 0)))
    lat = lat.reshape(3 * FR_DEV, H + 2, (W_DEV + 4) * LAT).astype(jnp.float32)

    frame_ok = (s * FR_DEV - 2 + jnp.arange(t_ext)) >= 0
    col_id = k * W_DEV - 1 + jnp.arange(w_ext)
    col_ok = (col_id >= 0) & (col_id < total_cols)
    ok = (frame_ok[:, None] & col_ok[None, :]).astype(jnp.float32).reshape(-1)
    first_act, entry_own = entry_pallas(lat, entry_kernel, entry_bias, gain_one, ok)

    taps1 = [(0, FR_DEV, dt, dt) for dt in range(3)]
    second_act = conv_pallas("act", taps1, first_act, first_kernel, first_bias, gain_two.reshape(1, c))

    left = shift2(second_act[:, W_DEV - 1 :], 0, 1)
    right = shift2(second_act[:, :1], 0, -1)
    ext_own = jnp.concatenate([left, second_act, right], axis=1)
    prev = shift_from(ext_own, "tm", 1)
    local = [(0, FR_DEV, 2, 0), (1, FR_DEV - 1, 1, 0)]
    remote = [(0, FR_DEV, 0, 0), (0, 1, 1, FR_DEV - 1)]
    partial = conv_pallas("part", local, ext_own, second_kernel, second_bias, entry_own)
    decoded = conv_pallas(
        "res", remote, prev, second_kernel, second_bias, entry_own, partial=partial
    )
    return jnp.transpose(decoded, (0, 2, 1, 3))


def solution(mesh):
    in_specs = (P(("tm", "tile"), None), P(), P(), P(), P(), P(), P(), P(), P())
    out_specs = P("tm", None, "tile", None)
    return jax.shard_map(body, mesh=mesh, in_specs=in_specs, out_specs=out_specs, check_vma=False)
```

```python
import functools

import jax
import jax.numpy as jnp
from jax import lax
from jax.experimental import pallas as pl
from jax.experimental.pallas import tpu as pltpu
from jax.sharding import PartitionSpec as P

LAT = 16
FR_DEV = 2
H = 96
W_DEV = 4


def shift_from(value, axis, steps):
    count = lax.axis_size(axis)
    pairs = [(i, i + steps) for i in range(max(0, -steps), min(count, count - steps))]
    return lax.ppermute(value, axis, pairs)


def _norm_silu(v, gain):
    scaled = v * lax.rsqrt(jnp.mean(v * v, axis=-1, keepdims=True) + 1e-06) * gain
    return scaled / (1.0 + jnp.exp(-scaled))


def _conv_kernel(mode, x_ref, w_ref, b_ref, e_ref, o_ref, acc_ref):
    d = pl.program_id(0)
    t_out, w_out, rows, co = o_ref.shape
    m = t_out * w_out * rows
    part = None
    for dt in range(3):
        for dj in range(3):
            lhs = x_ref[dt : dt + t_out, dj : dj + w_out].reshape(m, x_ref.shape[-1])
            p = jnp.dot(lhs, w_ref[dt, 0, dj], preferred_element_type=jnp.float32)
            part = p if part is None else part + p
    row = lax.broadcasted_iota(jnp.int32, (t_out * w_out, rows, co), 1).reshape(m, co)

    @pl.when(d == 0)
    def _():
        acc_ref[...] = jnp.where(row == 0, 0.0, pltpu.roll(part, 1, 0))

    @pl.when(d == 1)
    def _():
        acc_ref[...] += part

    @pl.when(d == 2)
    def _():
        below = jnp.where(row == rows - 1, 0.0, pltpu.roll(part, m - 1, 0))
        total = acc_ref[...] + below + b_ref[...]
        if mode == "act":
            mid = total.astype(jnp.bfloat16).astype(jnp.float32)
            res = _norm_silu(mid, e_ref[...])
        else:
            res = e_ref[...].reshape(m, co).astype(jnp.float32) + total
        o_ref[...] = res.astype(o_ref.dtype).reshape(o_ref.shape)


def conv_pallas(mode, field, kernel, bias, extra):
    tp, wp, rows, c = field.shape
    co = kernel.shape[-1]
    t_out, w_out = tp - 2, wp - 2
    out_shape = (t_out, w_out, rows, co)
    if mode == "act":
        e_spec = pl.BlockSpec((1, co), lambda d: (0, 0))
    else:
        e_spec = pl.BlockSpec(out_shape, lambda d: (0, 0, 0, 0))
    flops = 2 * t_out * w_out * rows * 27 * c * co
    return pl.pallas_call(
        functools.partial(_conv_kernel, mode),
        grid=(3,),
        in_specs=[
            pl.BlockSpec((tp, wp, rows, c), lambda d: (0, 0, 0, 0)),
            pl.BlockSpec((3, 1, 3, c, co), lambda d: (0, d, 0, 0, 0)),
            pl.BlockSpec((1, co), lambda d: (0, 0)),
            e_spec,
        ],
        out_specs=pl.BlockSpec(out_shape, lambda d: (0, 0, 0, 0)),
        out_shape=jax.ShapeDtypeStruct(out_shape, jnp.bfloat16),
        scratch_shapes=[pltpu.VMEM((t_out * w_out * rows, co), jnp.float32)],
        compiler_params=pltpu.CompilerParams(
            dimension_semantics=("arbitrary",), vmem_limit_bytes=48 * 1024 * 1024
        ),
        cost_estimate=pl.CostEstimate(
            flops=flops,
            transcendentals=0,
            bytes_accessed=field.size * 2 + kernel.size * 2 + t_out * w_out * rows * co * 4,
        ),
    )(field, kernel, bias.reshape(1, co), extra)


def _entry_kernel(lat_ref, k_ref, b_ref, g_ref, ok_ref, act_ref, own_ref, band_ref, patch_ref):
    t_ext, w_ext, rows, c = act_ref.shape
    lanes = lat_ref.shape[-1]
    lat_ch = k_ref.shape[1]
    band_ref[...] = jnp.zeros(band_ref.shape, band_ref.dtype)
    for dt in range(3):
        for di in range(3):
            p = dt * 3 + di
            for dj in range(3):
                for j in range(w_ext):
                    r0 = p * lanes + (j + dj) * lat_ch
                    band_ref[r0 : r0 + lat_ch, j * c : (j + 1) * c] = k_ref[p * 3 + dj]
            slab = lat_ref[dt : dt + t_ext, di : di + rows, :].reshape(t_ext * rows, lanes)
            patch_ref[:, p * lanes : (p + 1) * lanes] = slab.astype(patch_ref.dtype)
    for j in range(w_ext):
        e = jnp.dot(
            patch_ref[...], band_ref[:, j * c : (j + 1) * c], preferred_element_type=jnp.float32
        )
        e = (e + b_ref[...]).astype(jnp.bfloat16)
        if 1 <= j <= w_ext - 2:
            own_ref[:, j - 1] = e.reshape(t_ext, rows, c)[t_ext - FR_DEV :]
        fa = _norm_silu(e.astype(jnp.float32), g_ref[...]).reshape(t_ext, rows, c)
        for t in range(t_ext):
            act_ref[t, j] = (fa[t] * ok_ref[t * w_ext + j]).astype(act_ref.dtype)


def entry_pallas(lat, entry_kernel, entry_bias, gain_one, ok):
    t_ext, w_ext = FR_DEV + 2, W_DEV + 2
    lanes = lat.shape[-1]
    c = entry_kernel.shape[-1]
    kr = entry_kernel.reshape(27, LAT, c)
    vmem = pl.BlockSpec(memory_space=pltpu.VMEM)
    return pl.pallas_call(
        _entry_kernel,
        in_specs=[vmem, vmem, vmem, vmem, pl.BlockSpec(memory_space=pltpu.SMEM)],
        out_specs=(vmem, vmem),
        out_shape=(
            jax.ShapeDtypeStruct((t_ext, w_ext, H, c), jnp.bfloat16),
            jax.ShapeDtypeStruct((FR_DEV, W_DEV, H, c), jnp.bfloat16),
        ),
        scratch_shapes=[
            pltpu.VMEM((9 * lanes, w_ext * c), jnp.bfloat16),
            pltpu.VMEM((t_ext * H, 9 * lanes), jnp.bfloat16),
        ],
        compiler_params=pltpu.CompilerParams(vmem_limit_bytes=48 * 1024 * 1024),
        cost_estimate=pl.CostEstimate(
            flops=2 * t_ext * H * 9 * lanes * w_ext * c,
            transcendentals=t_ext * w_ext * H * c,
            bytes_accessed=lat.size * 4 + kr.size * 2 + (t_ext * w_ext + FR_DEV * W_DEV) * H * c * 2,
        ),
    )(lat, kr, entry_bias.reshape(1, c), gain_one.reshape(1, c), ok)


def shift2(value, ds, dk):
    n_tm, n_tile = lax.axis_size("tm"), lax.axis_size("tile")
    pairs = []
    for s in range(n_tm):
        for k in range(n_tile):
            if 0 <= s + ds < n_tm and 0 <= k + dk < n_tile:
                pairs.append((s * n_tile + k, (s + ds) * n_tile + k + dk))
    return lax.ppermute(value, ("tm", "tile"), pairs)


def gather_latent(latent_tokens, total_cols):
    n_tile = lax.axis_size("tile")
    rows_per = FR_DEV * H // n_tile
    strip = latent_tokens.reshape(rows_per, total_cols, LAT)
    strip = jnp.pad(strip, ((0, 0), (2, 2), (0, 0)))
    windows = jnp.stack(
        [strip[:, t * W_DEV : t * W_DEV + W_DEV + 4] for t in range(n_tile)], axis=0
    )
    section = lax.all_to_all(windows, "tile", 0, 0, tiled=True)
    section = section.reshape(FR_DEV, H, W_DEV + 4, LAT)
    back1 = shift_from(section, "tm", 1)
    back2 = shift_from(section, "tm", 2)
    return jnp.concatenate([back2, back1, section], axis=0)


def body(
    latent_tokens,
    entry_kernel,
    entry_bias,
    gain_one,
    first_kernel,
    first_bias,
    gain_two,
    second_kernel,
    second_bias,
):
    tiles = lax.axis_size("tile")
    total_cols = W_DEV * tiles
    s = lax.axis_index("tm")
    k = lax.axis_index("tile")
    c = entry_kernel.shape[-1]
    t_ext, w_ext = FR_DEV + 2, W_DEV + 2

    lat = gather_latent(latent_tokens, total_cols)
    lat = jnp.pad(lat, ((0, 0), (1, 1), (0, 0), (0, 0)))
    lat = lat.reshape(3 * FR_DEV, H + 2, (W_DEV + 4) * LAT).astype(jnp.float32)

    frame_ok = (s * FR_DEV - 2 + jnp.arange(t_ext)) >= 0
    col_id = k * W_DEV - 1 + jnp.arange(w_ext)
    col_ok = (col_id >= 0) & (col_id < total_cols)
    ok = (frame_ok[:, None] & col_ok[None, :]).astype(jnp.float32).reshape(-1)
    first_act, entry_own = entry_pallas(lat, entry_kernel, entry_bias, gain_one, ok)

    second_act = conv_pallas("act", first_act, first_kernel, first_bias, gain_two.reshape(1, c))

    left = shift2(second_act[:, W_DEV - 1 :], 0, 1)
    right = shift2(second_act[:, :1], 0, -1)
    ext_own = jnp.concatenate([left, second_act, right], axis=1)
    ext2 = jnp.concatenate([shift_from(ext_own, "tm", 1), ext_own], axis=0)

    decoded = conv_pallas("res", ext2, second_kernel, second_bias, entry_own)
    return jnp.transpose(decoded, (0, 2, 1, 3))


def solution(mesh):
    in_specs = (P(("tm", "tile"), None), P(), P(), P(), P(), P(), P(), P(), P())
    out_specs = P("tm", None, "tile", None)
    return jax.shard_map(body, mesh=mesh, in_specs=in_specs, out_specs=out_specs, check_vma=False)
```

```python
import functools

import jax
import jax.numpy as jnp
from jax import lax
from jax.experimental import pallas as pl
from jax.experimental.pallas import tpu as pltpu
from jax.sharding import PartitionSpec as P

LAT = 16
FR_DEV = 2
H = 96
W_DEV = 4


def shift_from(value, axis, steps):
    count = lax.axis_size(axis)
    pairs = [(i, i + steps) for i in range(max(0, -steps), min(count, count - steps))]
    return lax.ppermute(value, axis, pairs)


def _norm_silu(v, gain):
    scaled = v * lax.rsqrt(jnp.mean(v * v, axis=-1, keepdims=True) + 1e-06) * gain
    return scaled / (1.0 + jnp.exp(-scaled))


def _conv_kernel(mode, x_ref, w_ref, b_ref, e_ref, o_ref, acc_ref, cols_ref):
    d = pl.program_id(0)
    t_out, w_out, rows, co = o_ref.shape
    c = x_ref.shape[-1]
    m = t_out * w_out * rows

    @pl.when(d == 0)
    def _():
        for dt in range(3):
            for dj in range(3):
                q = dt * 3 + dj
                cols_ref[:, :, :, q * c : (q + 1) * c] = x_ref[dt : dt + t_out, dj : dj + w_out]

    lhs = cols_ref[...].reshape(m, 9 * c)
    part = jnp.dot(lhs, w_ref[:, 0].reshape(9 * c, co), preferred_element_type=jnp.float32)
    row = lax.broadcasted_iota(jnp.int32, (t_out * w_out, rows, co), 1).reshape(m, co)

    @pl.when(d == 0)
    def _():
        acc_ref[...] = jnp.where(row == 0, 0.0, pltpu.roll(part, 1, 0))

    @pl.when(d == 1)
    def _():
        acc_ref[...] += part

    @pl.when(d == 2)
    def _():
        below = jnp.where(row == rows - 1, 0.0, pltpu.roll(part, m - 1, 0))
        total = acc_ref[...] + below + b_ref[...]
        if mode == "act":
            mid = total.astype(jnp.bfloat16).astype(jnp.float32)
            res = _norm_silu(mid, e_ref[...])
        else:
            res = e_ref[...].reshape(m, co).astype(jnp.float32) + total
        o_ref[...] = res.astype(o_ref.dtype).reshape(o_ref.shape)


def conv_pallas(mode, field, kernel, bias, extra):
    tp, wp, rows, c = field.shape
    co = kernel.shape[-1]
    t_out, w_out = tp - 2, wp - 2
    out_shape = (t_out, w_out, rows, co)
    if mode == "act":
        e_spec = pl.BlockSpec((1, co), lambda d: (0, 0))
    else:
        e_spec = pl.BlockSpec(out_shape, lambda d: (0, 0, 0, 0))
    flops = 2 * t_out * w_out * rows * 27 * c * co
    return pl.pallas_call(
        functools.partial(_conv_kernel, mode),
        grid=(3,),
        in_specs=[
            pl.BlockSpec((tp, wp, rows, c), lambda d: (0, 0, 0, 0)),
            pl.BlockSpec((3, 1, 3, c, co), lambda d: (0, d, 0, 0, 0)),
            pl.BlockSpec((1, co), lambda d: (0, 0)),
            e_spec,
        ],
        out_specs=pl.BlockSpec(out_shape, lambda d: (0, 0, 0, 0)),
        out_shape=jax.ShapeDtypeStruct(out_shape, jnp.bfloat16),
        scratch_shapes=[
            pltpu.VMEM((t_out * w_out * rows, co), jnp.float32),
            pltpu.VMEM((t_out, w_out, rows, 9 * c), jnp.bfloat16),
        ],
        compiler_params=pltpu.CompilerParams(
            dimension_semantics=("arbitrary",), vmem_limit_bytes=48 * 1024 * 1024
        ),
        cost_estimate=pl.CostEstimate(
            flops=flops,
            transcendentals=0,
            bytes_accessed=field.size * 2 + kernel.size * 2 + t_out * w_out * rows * co * 4,
        ),
    )(field, kernel, bias.reshape(1, co), extra)


def _entry_kernel(lat_ref, k_ref, b_ref, g_ref, ok_ref, act_ref, own_ref, band_ref, patch_ref):
    t_ext, w_ext, rows, c = act_ref.shape
    lanes = lat_ref.shape[-1]
    lat_ch = k_ref.shape[1]
    band_ref[...] = jnp.zeros(band_ref.shape, band_ref.dtype)
    for dt in range(3):
        for di in range(3):
            p = dt * 3 + di
            for dj in range(3):
                for j in range(w_ext):
                    r0 = p * lanes + (j + dj) * lat_ch
                    band_ref[r0 : r0 + lat_ch, j * c : (j + 1) * c] = k_ref[p * 3 + dj]
            slab = lat_ref[dt : dt + t_ext, di : di + rows, :].reshape(t_ext * rows, lanes)
            patch_ref[:, p * lanes : (p + 1) * lanes] = slab.astype(patch_ref.dtype)
    for j in range(w_ext):
        e = jnp.dot(
            patch_ref[...], band_ref[:, j * c : (j + 1) * c], preferred_element_type=jnp.float32
        )
        e = (e + b_ref[...]).astype(jnp.bfloat16)
        if 1 <= j <= w_ext - 2:
            own_ref[:, j - 1] = e.reshape(t_ext, rows, c)[t_ext - FR_DEV :]
        fa = _norm_silu(e.astype(jnp.float32), g_ref[...]).reshape(t_ext, rows, c)
        for t in range(t_ext):
            act_ref[t, j] = (fa[t] * ok_ref[t * w_ext + j]).astype(act_ref.dtype)


def entry_pallas(lat, entry_kernel, entry_bias, gain_one, ok):
    t_ext, w_ext = FR_DEV + 2, W_DEV + 2
    lanes = lat.shape[-1]
    c = entry_kernel.shape[-1]
    kr = entry_kernel.reshape(27, LAT, c)
    vmem = pl.BlockSpec(memory_space=pltpu.VMEM)
    return pl.pallas_call(
        _entry_kernel,
        in_specs=[vmem, vmem, vmem, vmem, pl.BlockSpec(memory_space=pltpu.SMEM)],
        out_specs=(vmem, vmem),
        out_shape=(
            jax.ShapeDtypeStruct((t_ext, w_ext, H, c), jnp.bfloat16),
            jax.ShapeDtypeStruct((FR_DEV, W_DEV, H, c), jnp.bfloat16),
        ),
        scratch_shapes=[
            pltpu.VMEM((9 * lanes, w_ext * c), jnp.bfloat16),
            pltpu.VMEM((t_ext * H, 9 * lanes), jnp.bfloat16),
        ],
        compiler_params=pltpu.CompilerParams(vmem_limit_bytes=48 * 1024 * 1024),
        cost_estimate=pl.CostEstimate(
            flops=2 * t_ext * H * 9 * lanes * w_ext * c,
            transcendentals=t_ext * w_ext * H * c,
            bytes_accessed=lat.size * 4 + kr.size * 2 + (t_ext * w_ext + FR_DEV * W_DEV) * H * c * 2,
        ),
    )(lat, kr, entry_bias.reshape(1, c), gain_one.reshape(1, c), ok)


def shift2(value, ds, dk):
    n_tm, n_tile = lax.axis_size("tm"), lax.axis_size("tile")
    pairs = []
    for s in range(n_tm):
        for k in range(n_tile):
            if 0 <= s + ds < n_tm and 0 <= k + dk < n_tile:
                pairs.append((s * n_tile + k, (s + ds) * n_tile + k + dk))
    return lax.ppermute(value, ("tm", "tile"), pairs)


def gather_latent(latent_tokens, total_cols):
    n_tile = lax.axis_size("tile")
    rows_per = FR_DEV * H // n_tile
    strip = latent_tokens.reshape(rows_per, total_cols, LAT)
    strip = jnp.pad(strip, ((0, 0), (2, 2), (0, 0)))
    windows = jnp.stack(
        [strip[:, t * W_DEV : t * W_DEV + W_DEV + 4] for t in range(n_tile)], axis=0
    )
    section = lax.all_to_all(windows, "tile", 0, 0, tiled=True)
    section = section.reshape(FR_DEV, H, W_DEV + 4, LAT)
    back1 = shift_from(section, "tm", 1)
    back2 = shift_from(section, "tm", 2)
    return jnp.concatenate([back2, back1, section], axis=0)


def body(
    latent_tokens,
    entry_kernel,
    entry_bias,
    gain_one,
    first_kernel,
    first_bias,
    gain_two,
    second_kernel,
    second_bias,
):
    tiles = lax.axis_size("tile")
    total_cols = W_DEV * tiles
    s = lax.axis_index("tm")
    k = lax.axis_index("tile")
    c = entry_kernel.shape[-1]
    t_ext, w_ext = FR_DEV + 2, W_DEV + 2

    lat = gather_latent(latent_tokens, total_cols)
    lat = jnp.pad(lat, ((0, 0), (1, 1), (0, 0), (0, 0)))
    lat = lat.reshape(3 * FR_DEV, H + 2, (W_DEV + 4) * LAT).astype(jnp.float32)

    frame_ok = (s * FR_DEV - 2 + jnp.arange(t_ext)) >= 0
    col_id = k * W_DEV - 1 + jnp.arange(w_ext)
    col_ok = (col_id >= 0) & (col_id < total_cols)
    ok = (frame_ok[:, None] & col_ok[None, :]).astype(jnp.float32).reshape(-1)
    first_act, entry_own = entry_pallas(lat, entry_kernel, entry_bias, gain_one, ok)

    second_act = conv_pallas("act", first_act, first_kernel, first_bias, gain_two.reshape(1, c))

    last, first = second_act[:, W_DEV - 1 :], second_act[:, :1]
    own_row = [shift2(last, 0, 1), second_act, shift2(first, 0, -1)]
    prev_row = [shift2(last, 1, 1), shift2(second_act, 1, 0), shift2(first, 1, -1)]
    ext2 = jnp.concatenate(
        [jnp.concatenate(prev_row, axis=1), jnp.concatenate(own_row, axis=1)], axis=0
    )

    decoded = conv_pallas("res", ext2, second_kernel, second_bias, entry_own)
    return jnp.transpose(decoded, (0, 2, 1, 3))


def solution(mesh):
    in_specs = (P(("tm", "tile"), None), P(), P(), P(), P(), P(), P(), P(), P())
    out_specs = P("tm", None, "tile", None)
    return jax.shard_map(body, mesh=mesh, in_specs=in_specs, out_specs=out_specs, check_vma=False)
```

```python
import functools

import jax
import jax.numpy as jnp
from jax import lax
from jax.experimental import pallas as pl
from jax.experimental.pallas import tpu as pltpu
from jax.sharding import PartitionSpec as P

LAT = 16
FR_DEV = 2
H = 96
W_DEV = 4


def shift_from(value, axis, steps):
    count = lax.axis_size(axis)
    pairs = [(i, i + steps) for i in range(max(0, -steps), min(count, count - steps))]
    return lax.ppermute(value, axis, pairs)


def _norm_silu(v, gain):
    scaled = v * lax.rsqrt(jnp.mean(v * v, axis=-1, keepdims=True) + 1e-06) * gain
    return scaled / (1.0 + jnp.exp(-scaled))


def _conv_kernel(mode, x_ref, w_ref, b_ref, e_ref, o_ref, acc_ref, cols_ref):
    d = pl.program_id(0)
    t_out, w_out, rows, co = o_ref.shape
    c = x_ref.shape[-1]
    m = t_out * w_out * rows

    @pl.when(d == 0)
    def _():
        for dt in range(3):
            for dj in range(3):
                q = dt * 3 + dj
                cols_ref[:, :, :, q * c : (q + 1) * c] = x_ref[dt : dt + t_out, dj : dj + w_out]

    lhs = cols_ref[...].reshape(m, 9 * c)
    part = jnp.dot(lhs, w_ref[:, 0].reshape(9 * c, co), preferred_element_type=jnp.float32)
    row = lax.broadcasted_iota(jnp.int32, (t_out * w_out, rows, co), 1).reshape(m, co)

    @pl.when(d == 0)
    def _():
        acc_ref[...] = jnp.where(row == 0, 0.0, pltpu.roll(part, 1, 0))

    @pl.when(d == 1)
    def _():
        acc_ref[...] += part

    @pl.when(d == 2)
    def _():
        below = jnp.where(row == rows - 1, 0.0, pltpu.roll(part, m - 1, 0))
        total = acc_ref[...] + below + b_ref[...]
        if mode == "act":
            mid = total.astype(jnp.bfloat16).astype(jnp.float32)
            res = _norm_silu(mid, e_ref[...])
        else:
            res = e_ref[...].reshape(m, co).astype(jnp.float32) + total
        o_ref[...] = res.astype(o_ref.dtype).reshape(o_ref.shape)


def conv_pallas(mode, field, kernel, bias, extra):
    tp, wp, rows, c = field.shape
    co = kernel.shape[-1]
    t_out, w_out = tp - 2, wp - 2
    out_shape = (t_out, w_out, rows, co)
    if mode == "act":
        e_spec = pl.BlockSpec((1, co), lambda d: (0, 0))
    else:
        e_spec = pl.BlockSpec(out_shape, lambda d: (0, 0, 0, 0))
    flops = 2 * t_out * w_out * rows * 27 * c * co
    return pl.pallas_call(
        functools.partial(_conv_kernel, mode),
        grid=(3,),
        in_specs=[
            pl.BlockSpec((tp, wp, rows, c), lambda d: (0, 0, 0, 0)),
            pl.BlockSpec((3, 1, 3, c, co), lambda d: (0, d, 0, 0, 0)),
            pl.BlockSpec((1, co), lambda d: (0, 0)),
            e_spec,
        ],
        out_specs=pl.BlockSpec(out_shape, lambda d: (0, 0, 0, 0)),
        out_shape=jax.ShapeDtypeStruct(out_shape, jnp.bfloat16),
        scratch_shapes=[
            pltpu.VMEM((t_out * w_out * rows, co), jnp.float32),
            pltpu.VMEM((t_out, w_out, rows, 9 * c), jnp.bfloat16),
        ],
        compiler_params=pltpu.CompilerParams(
            dimension_semantics=("arbitrary",), vmem_limit_bytes=48 * 1024 * 1024
        ),
        cost_estimate=pl.CostEstimate(
            flops=flops,
            transcendentals=0,
            bytes_accessed=field.size * 2 + kernel.size * 2 + t_out * w_out * rows * co * 4,
        ),
    )(field, kernel, bias.reshape(1, co), extra)


def _entry_kernel(lat_ref, k_ref, b_ref, g_ref, ok_ref, act_ref, own_ref, band_ref, patch_ref):
    t_ext, w_ext, rows, c = act_ref.shape
    lanes = lat_ref.shape[-1]
    lat_ch = k_ref.shape[1]
    band_ref[...] = jnp.zeros(band_ref.shape, band_ref.dtype)
    for dt in range(3):
        for di in range(3):
            p = dt * 3 + di
            for dj in range(3):
                for j in range(w_ext):
                    r0 = p * lanes + (j + dj) * lat_ch
                    band_ref[r0 : r0 + lat_ch, j * c : (j + 1) * c] = k_ref[p * 3 + dj]
            slab = lat_ref[dt : dt + t_ext, di : di + rows, :].reshape(t_ext * rows, lanes)
            patch_ref[:, p * lanes : (p + 1) * lanes] = slab.astype(patch_ref.dtype)
    for j in range(w_ext):
        e = jnp.dot(
            patch_ref[...], band_ref[:, j * c : (j + 1) * c], preferred_element_type=jnp.float32
        )
        e = (e + b_ref[...]).astype(jnp.bfloat16)
        if 1 <= j <= w_ext - 2:
            own_ref[:, j - 1] = e.reshape(t_ext, rows, c)[t_ext - FR_DEV :]
        fa = _norm_silu(e.astype(jnp.float32), g_ref[...]).reshape(t_ext, rows, c)
        for t in range(t_ext):
            act_ref[t, j] = (fa[t] * ok_ref[t * w_ext + j]).astype(act_ref.dtype)


def entry_pallas(lat, entry_kernel, entry_bias, gain_one, ok):
    t_ext, w_ext = FR_DEV + 2, W_DEV + 2
    lanes = lat.shape[-1]
    c = entry_kernel.shape[-1]
    kr = entry_kernel.reshape(27, LAT, c)
    vmem = pl.BlockSpec(memory_space=pltpu.VMEM)
    return pl.pallas_call(
        _entry_kernel,
        in_specs=[vmem, vmem, vmem, vmem, pl.BlockSpec(memory_space=pltpu.SMEM)],
        out_specs=(vmem, vmem),
        out_shape=(
            jax.ShapeDtypeStruct((t_ext, w_ext, H, c), jnp.bfloat16),
            jax.ShapeDtypeStruct((FR_DEV, W_DEV, H, c), jnp.bfloat16),
        ),
        scratch_shapes=[
            pltpu.VMEM((9 * lanes, w_ext * c), jnp.bfloat16),
            pltpu.VMEM((t_ext * H, 9 * lanes), jnp.bfloat16),
        ],
        compiler_params=pltpu.CompilerParams(vmem_limit_bytes=48 * 1024 * 1024),
        cost_estimate=pl.CostEstimate(
            flops=2 * t_ext * H * 9 * lanes * w_ext * c,
            transcendentals=t_ext * w_ext * H * c,
            bytes_accessed=lat.size * 4 + kr.size * 2 + (t_ext * w_ext + FR_DEV * W_DEV) * H * c * 2,
        ),
    )(lat, kr, entry_bias.reshape(1, c), gain_one.reshape(1, c), ok)


def shift2(value, ds, dk):
    n_tm, n_tile = lax.axis_size("tm"), lax.axis_size("tile")
    pairs = []
    for s in range(n_tm):
        for k in range(n_tile):
            if 0 <= s + ds < n_tm and 0 <= k + dk < n_tile:
                pairs.append((s * n_tile + k, (s + ds) * n_tile + k + dk))
    return lax.ppermute(value, ("tm", "tile"), pairs)


def gather_latent(latent_tokens, total_cols):
    n_tm, n_tile = lax.axis_size("tm"), lax.axis_size("tile")
    s = lax.axis_index("tm")
    rows_per = FR_DEV * H // n_tile
    strip = latent_tokens.reshape(rows_per, total_cols, LAT)
    strip = jnp.pad(strip, ((0, 0), (2, 2), (0, 0)))
    windows = jnp.stack(
        [strip[:, t * W_DEV : t * W_DEV + W_DEV + 4] for t in range(n_tile)], axis=0
    )
    lag = jnp.arange(n_tm) - s
    wanted = ((lag >= 0) & (lag <= 2)).astype(windows.dtype)
    chunks = wanted[:, None, None, None, None] * windows[None]
    chunks = chunks.reshape((n_tm * n_tile,) + windows.shape[1:])
    got = lax.all_to_all(chunks, ("tm", "tile"), 0, 0, tiled=True)
    got = got.reshape((n_tm, n_tile) + windows.shape[1:])
    got = jnp.pad(got, ((2, 0), (0, 0), (0, 0), (0, 0), (0, 0)))
    got = lax.dynamic_slice_in_dim(got, s, 3, axis=0)
    return got.reshape(3 * FR_DEV, H, W_DEV + 4, LAT)


def body(
    latent_tokens,
    entry_kernel,
    entry_bias,
    gain_one,
    first_kernel,
    first_bias,
    gain_two,
    second_kernel,
    second_bias,
):
    tiles = lax.axis_size("tile")
    total_cols = W_DEV * tiles
    s = lax.axis_index("tm")
    k = lax.axis_index("tile")
    c = entry_kernel.shape[-1]
    t_ext, w_ext = FR_DEV + 2, W_DEV + 2

    lat = gather_latent(latent_tokens, total_cols)
    lat = jnp.pad(lat, ((0, 0), (1, 1), (0, 0), (0, 0)))
    lat = lat.reshape(3 * FR_DEV, H + 2, (W_DEV + 4) * LAT).astype(jnp.float32)

    frame_ok = (s * FR_DEV - 2 + jnp.arange(t_ext)) >= 0
    col_id = k * W_DEV - 1 + jnp.arange(w_ext)
    col_ok = (col_id >= 0) & (col_id < total_cols)
    ok = (frame_ok[:, None] & col_ok[None, :]).astype(jnp.float32).reshape(-1)
    first_act, entry_own = entry_pallas(lat, entry_kernel, entry_bias, gain_one, ok)

    second_act = conv_pallas("act", first_act, first_kernel, first_bias, gain_two.reshape(1, c))

    last, first = second_act[:, W_DEV - 1 :], second_act[:, :1]
    own_row = [shift2(last, 0, 1), second_act, shift2(first, 0, -1)]
    prev_row = [shift2(last, 1, 1), shift2(second_act, 1, 0), shift2(first, 1, -1)]
    ext2 = jnp.concatenate(
        [jnp.concatenate(prev_row, axis=1), jnp.concatenate(own_row, axis=1)], axis=0
    )

    decoded = conv_pallas("res", ext2, second_kernel, second_bias, entry_own)
    return jnp.transpose(decoded, (0, 2, 1, 3))


def solution(mesh):
    in_specs = (P(("tm", "tile"), None), P(), P(), P(), P(), P(), P(), P(), P())
    out_specs = P("tm", None, "tile", None)
    return jax.shard_map(body, mesh=mesh, in_specs=in_specs, out_specs=out_specs, check_vma=False)
```

```python
import functools

import jax
import jax.numpy as jnp
from jax import lax
from jax.experimental import pallas as pl
from jax.experimental.pallas import tpu as pltpu
from jax.sharding import PartitionSpec as P

LAT = 16
FR_DEV = 2
H = 96
W_DEV = 4


def shift_from(value, axis, steps):
    count = lax.axis_size(axis)
    pairs = [(i, i + steps) for i in range(max(0, -steps), min(count, count - steps))]
    return lax.ppermute(value, axis, pairs)


def _norm_silu(v, gain):
    scaled = v * lax.rsqrt(jnp.mean(v * v, axis=-1, keepdims=True) + 1e-06) * gain
    return scaled / (1.0 + jnp.exp(-scaled))


def _conv_kernel(mode, x_ref, w_ref, b_ref, e_ref, o_ref, acc_ref, cols_ref):
    d = pl.program_id(0)
    t_out, w_out, rows, co = o_ref.shape
    c = x_ref.shape[-1]
    m = t_out * w_out * rows

    @pl.when(d == 0)
    def _():
        for dt in range(3):
            for dj in range(3):
                q = dt * 3 + dj
                cols_ref[:, :, :, q * c : (q + 1) * c] = x_ref[dt : dt + t_out, dj : dj + w_out]

    lhs = cols_ref[...].reshape(m, 9 * c)
    part = jnp.dot(lhs, w_ref[:, 0].reshape(9 * c, co), preferred_element_type=jnp.float32)
    row = lax.broadcasted_iota(jnp.int32, (t_out * w_out, rows, co), 1).reshape(m, co)

    @pl.when(d == 0)
    def _():
        acc_ref[...] = jnp.where(row == 0, 0.0, pltpu.roll(part, 1, 0))

    @pl.when(d == 1)
    def _():
        acc_ref[...] += part

    @pl.when(d == 2)
    def _():
        below = jnp.where(row == rows - 1, 0.0, pltpu.roll(part, m - 1, 0))
        total = acc_ref[...] + below + b_ref[...]
        if mode == "act":
            mid = total.astype(jnp.bfloat16).astype(jnp.float32)
            res = _norm_silu(mid, e_ref[...])
        else:
            res = e_ref[...].reshape(m, co).astype(jnp.float32) + total
        o_ref[...] = res.astype(o_ref.dtype).reshape(o_ref.shape)


def conv_pallas(mode, field, kernel, bias, extra):
    tp, wp, rows, c = field.shape
    co = kernel.shape[-1]
    t_out, w_out = tp - 2, wp - 2
    out_shape = (t_out, w_out, rows, co)
    if mode == "act":
        e_spec = pl.BlockSpec((1, co), lambda d: (0, 0))
    else:
        e_spec = pl.BlockSpec(out_shape, lambda d: (0, 0, 0, 0))
    flops = 2 * t_out * w_out * rows * 27 * c * co
    return pl.pallas_call(
        functools.partial(_conv_kernel, mode),
        grid=(3,),
        in_specs=[
            pl.BlockSpec((tp, wp, rows, c), lambda d: (0, 0, 0, 0)),
            pl.BlockSpec((3, 1, 3, c, co), lambda d: (0, d, 0, 0, 0)),
            pl.BlockSpec((1, co), lambda d: (0, 0)),
            e_spec,
        ],
        out_specs=pl.BlockSpec(out_shape, lambda d: (0, 0, 0, 0)),
        out_shape=jax.ShapeDtypeStruct(out_shape, jnp.bfloat16),
        scratch_shapes=[
            pltpu.VMEM((t_out * w_out * rows, co), jnp.float32),
            pltpu.VMEM((t_out, w_out, rows, 9 * c), jnp.bfloat16),
        ],
        compiler_params=pltpu.CompilerParams(
            dimension_semantics=("arbitrary",), vmem_limit_bytes=48 * 1024 * 1024
        ),
        cost_estimate=pl.CostEstimate(
            flops=flops,
            transcendentals=0,
            bytes_accessed=field.size * 2 + kernel.size * 2 + t_out * w_out * rows * co * 4,
        ),
    )(field, kernel, bias.reshape(1, co), extra)


def _entry_kernel(lat_ref, k_ref, b_ref, g_ref, ok_ref, act_ref, own_ref, band_ref, patch_ref):
    t_ext, w_ext, rows, c = act_ref.shape
    lanes = lat_ref.shape[-1]
    lat_ch = k_ref.shape[1]
    band_ref[...] = jnp.zeros(band_ref.shape, band_ref.dtype)
    for dt in range(3):
        for di in range(3):
            p = dt * 3 + di
            for dj in range(3):
                for j in range(w_ext):
                    r0 = p * lanes + (j + dj) * lat_ch
                    band_ref[r0 : r0 + lat_ch, j * c : (j + 1) * c] = k_ref[p * 3 + dj]
            slab = lat_ref[dt : dt + t_ext, di : di + rows, :].reshape(t_ext * rows, lanes)
            patch_ref[:, p * lanes : (p + 1) * lanes] = slab.astype(patch_ref.dtype)
    for j in range(w_ext):
        e = jnp.dot(
            patch_ref[...], band_ref[:, j * c : (j + 1) * c], preferred_element_type=jnp.float32
        )
        e = (e + b_ref[...]).astype(jnp.bfloat16)
        if 1 <= j <= w_ext - 2:
            own_ref[:, j - 1] = e.reshape(t_ext, rows, c)[t_ext - FR_DEV :]
        fa = _norm_silu(e.astype(jnp.float32), g_ref[...]).reshape(t_ext, rows, c)
        for t in range(t_ext):
            act_ref[t, j] = (fa[t] * ok_ref[t * w_ext + j]).astype(act_ref.dtype)


def entry_pallas(lat, entry_kernel, entry_bias, gain_one, ok):
    t_ext, w_ext = FR_DEV + 2, W_DEV + 2
    lanes = lat.shape[-1]
    c = entry_kernel.shape[-1]
    kr = entry_kernel.reshape(27, LAT, c)
    vmem = pl.BlockSpec(memory_space=pltpu.VMEM)
    return pl.pallas_call(
        _entry_kernel,
        in_specs=[vmem, vmem, vmem, vmem, pl.BlockSpec(memory_space=pltpu.SMEM)],
        out_specs=(vmem, vmem),
        out_shape=(
            jax.ShapeDtypeStruct((t_ext, w_ext, H, c), jnp.bfloat16),
            jax.ShapeDtypeStruct((FR_DEV, W_DEV, H, c), jnp.bfloat16),
        ),
        scratch_shapes=[
            pltpu.VMEM((9 * lanes, w_ext * c), jnp.bfloat16),
            pltpu.VMEM((t_ext * H, 9 * lanes), jnp.bfloat16),
        ],
        compiler_params=pltpu.CompilerParams(vmem_limit_bytes=48 * 1024 * 1024),
        cost_estimate=pl.CostEstimate(
            flops=2 * t_ext * H * 9 * lanes * w_ext * c,
            transcendentals=t_ext * w_ext * H * c,
            bytes_accessed=lat.size * 4 + kr.size * 2 + (t_ext * w_ext + FR_DEV * W_DEV) * H * c * 2,
        ),
    )(lat, kr, entry_bias.reshape(1, c), gain_one.reshape(1, c), ok)


def shift2(value, ds, dk):
    n_tm, n_tile = lax.axis_size("tm"), lax.axis_size("tile")
    pairs = []
    for s in range(n_tm):
        for k in range(n_tile):
            if 0 <= s + ds < n_tm and 0 <= k + dk < n_tile:
                pairs.append((s * n_tile + k, (s + ds) * n_tile + k + dk))
    return lax.ppermute(value, ("tm", "tile"), pairs)


def gather_latent(latent_tokens, total_cols):
    n_tm, n_tile = lax.axis_size("tm"), lax.axis_size("tile")
    s = lax.axis_index("tm")
    rows_per = FR_DEV * H // n_tile
    span = (W_DEV + 4) * LAT
    strip = latent_tokens.reshape(rows_per, total_cols * LAT)
    strip = jnp.pad(strip, ((0, 0), (2 * LAT, 2 * LAT)))
    windows = jnp.stack(
        [strip[:, t * W_DEV * LAT : t * W_DEV * LAT + span] for t in range(n_tile)], axis=0
    )
    lag = jnp.arange(n_tm) - s
    wanted = ((lag >= 0) & (lag <= 2)).astype(windows.dtype)
    chunks = wanted[:, None, None, None] * windows[None]
    chunks = chunks.reshape((n_tm * n_tile,) + windows.shape[1:])
    got = lax.all_to_all(chunks, ("tm", "tile"), 0, 0, tiled=True)
    got = got.reshape((n_tm, n_tile) + windows.shape[1:])
    got = jnp.pad(got, ((2, 0), (0, 0), (0, 0), (0, 0)))
    got = lax.dynamic_slice_in_dim(got, s, 3, axis=0)
    return got.reshape(3 * FR_DEV, H, span)


def body(
    latent_tokens,
    entry_kernel,
    entry_bias,
    gain_one,
    first_kernel,
    first_bias,
    gain_two,
    second_kernel,
    second_bias,
):
    tiles = lax.axis_size("tile")
    total_cols = W_DEV * tiles
    s = lax.axis_index("tm")
    k = lax.axis_index("tile")
    c = entry_kernel.shape[-1]
    t_ext, w_ext = FR_DEV + 2, W_DEV + 2

    lat = gather_latent(latent_tokens, total_cols)
    lat = jnp.pad(lat, ((0, 0), (1, 1), (0, 0))).astype(jnp.float32)

    frame_ok = (s * FR_DEV - 2 + jnp.arange(t_ext)) >= 0
    col_id = k * W_DEV - 1 + jnp.arange(w_ext)
    col_ok = (col_id >= 0) & (col_id < total_cols)
    ok = (frame_ok[:, None] & col_ok[None, :]).astype(jnp.float32).reshape(-1)
    first_act, entry_own = entry_pallas(lat, entry_kernel, entry_bias, gain_one, ok)

    second_act = conv_pallas("act", first_act, first_kernel, first_bias, gain_two.reshape(1, c))

    last, first = second_act[:, W_DEV - 1 :], second_act[:, :1]
    own_row = [shift2(last, 0, 1), second_act, shift2(first, 0, -1)]
    prev_row = [shift2(last, 1, 1), shift2(second_act, 1, 0), shift2(first, 1, -1)]
    ext2 = jnp.concatenate(
        [jnp.concatenate(prev_row, axis=1), jnp.concatenate(own_row, axis=1)], axis=0
    )

    decoded = conv_pallas("res", ext2, second_kernel, second_bias, entry_own)
    return jnp.transpose(decoded, (0, 2, 1, 3))


def solution(mesh):
    in_specs = (P(("tm", "tile"), None), P(), P(), P(), P(), P(), P(), P(), P())
    out_specs = P("tm", None, "tile", None)
    return jax.shard_map(body, mesh=mesh, in_specs=in_specs, out_specs=out_specs, check_vma=False)
```

```python
import functools

import jax
import jax.numpy as jnp
from jax import lax
from jax.experimental import pallas as pl
from jax.experimental.pallas import tpu as pltpu
from jax.sharding import PartitionSpec as P

LAT = 16
FR_DEV = 2
H = 96
W_DEV = 4


def shift_from(value, axis, steps):
    count = lax.axis_size(axis)
    pairs = [(i, i + steps) for i in range(max(0, -steps), min(count, count - steps))]
    return lax.ppermute(value, axis, pairs)


def _norm_silu(v, gain):
    scaled = v * lax.rsqrt(jnp.mean(v * v, axis=-1, keepdims=True) + 1e-06) * gain
    return scaled / (1.0 + jnp.exp(-scaled))


def _conv_kernel(mode, bases, x_ref, w_ref, b_ref, e_ref, o_ref, acc_ref, cols_ref):
    d = pl.program_id(0)
    t_out, w_out, rows, co = o_ref.shape
    c = x_ref.shape[-1]
    m = t_out * w_out * rows

    @pl.when(d == 0)
    def _():
        for dt in range(3):
            for dj in range(3):
                q = dt * 3 + dj
                for j, base in enumerate(bases):
                    cols_ref[:, j, :, q * c : (q + 1) * c] = x_ref[dt : dt + t_out, base + dj]

    lhs = cols_ref[...].reshape(m, 9 * c)
    part = jnp.dot(lhs, w_ref[:, 0].reshape(9 * c, co), preferred_element_type=jnp.float32)
    row = lax.broadcasted_iota(jnp.int32, (t_out * w_out, rows, co), 1).reshape(m, co)

    @pl.when(d == 0)
    def _():
        acc_ref[...] = jnp.where(row == 0, 0.0, pltpu.roll(part, 1, 0))

    @pl.when(d == 1)
    def _():
        acc_ref[...] += part

    @pl.when(d == 2)
    def _():
        below = jnp.where(row == rows - 1, 0.0, pltpu.roll(part, m - 1, 0))
        total = acc_ref[...] + below + b_ref[...]
        if mode == "act":
            mid = total.astype(jnp.bfloat16).astype(jnp.float32)
            res = _norm_silu(mid, e_ref[...])
        else:
            res = e_ref[...].reshape(m, co).astype(jnp.float32) + total
        o_ref[...] = res.astype(o_ref.dtype).reshape(o_ref.shape)


def conv_pallas(mode, field, kernel, bias, extra, bases=None):
    tp, wp, rows, c = field.shape
    co = kernel.shape[-1]
    bases = tuple(range(wp - 2)) if bases is None else tuple(bases)
    t_out, w_out = tp - 2, len(bases)
    out_shape = (t_out, w_out, rows, co)
    if mode == "act":
        e_spec = pl.BlockSpec((1, co), lambda d: (0, 0))
    else:
        e_spec = pl.BlockSpec(out_shape, lambda d: (0, 0, 0, 0))
    flops = 2 * t_out * w_out * rows * 27 * c * co
    return pl.pallas_call(
        functools.partial(_conv_kernel, mode, bases),
        grid=(3,),
        in_specs=[
            pl.BlockSpec((tp, wp, rows, c), lambda d: (0, 0, 0, 0)),
            pl.BlockSpec((3, 1, 3, c, co), lambda d: (0, d, 0, 0, 0)),
            pl.BlockSpec((1, co), lambda d: (0, 0)),
            e_spec,
        ],
        out_specs=pl.BlockSpec(out_shape, lambda d: (0, 0, 0, 0)),
        out_shape=jax.ShapeDtypeStruct(out_shape, jnp.bfloat16),
        scratch_shapes=[
            pltpu.VMEM((t_out * w_out * rows, co), jnp.float32),
            pltpu.VMEM((t_out, w_out, rows, 9 * c), jnp.bfloat16),
        ],
        compiler_params=pltpu.CompilerParams(
            dimension_semantics=("arbitrary",), vmem_limit_bytes=48 * 1024 * 1024
        ),
        cost_estimate=pl.CostEstimate(
            flops=flops,
            transcendentals=0,
            bytes_accessed=t_out * w_out * rows * c * 6 + kernel.size * 2 + t_out * w_out * rows * co * 4,
        ),
    )(field, kernel, bias.reshape(1, co), extra)


def _entry_kernel(lat_ref, k_ref, b_ref, g_ref, ok_ref, act_ref, own_ref, band_ref, patch_ref):
    t_ext, w_ext, rows, c = act_ref.shape
    lanes = lat_ref.shape[-1]
    lat_ch = k_ref.shape[1]
    band_ref[...] = jnp.zeros(band_ref.shape, band_ref.dtype)
    for dt in range(3):
        for di in range(3):
            p = dt * 3 + di
            for dj in range(3):
                for j in range(w_ext):
                    r0 = p * lanes + (j + dj) * lat_ch
                    band_ref[r0 : r0 + lat_ch, j * c : (j + 1) * c] = k_ref[p * 3 + dj]
            slab = lat_ref[dt : dt + t_ext, di : di + rows, :].reshape(t_ext * rows, lanes)
            patch_ref[:, p * lanes : (p + 1) * lanes] = slab.astype(patch_ref.dtype)
    for j in range(w_ext):
        e = jnp.dot(
            patch_ref[...], band_ref[:, j * c : (j + 1) * c], preferred_element_type=jnp.float32
        )
        e = (e + b_ref[...]).astype(jnp.bfloat16)
        if 1 <= j <= w_ext - 2:
            own_ref[:, j - 1] = e.reshape(t_ext, rows, c)[t_ext - FR_DEV :]
        fa = _norm_silu(e.astype(jnp.float32), g_ref[...]).reshape(t_ext, rows, c)
        for t in range(t_ext):
            act_ref[t, j] = (fa[t] * ok_ref[t * w_ext + j]).astype(act_ref.dtype)


def entry_pallas(lat, entry_kernel, entry_bias, gain_one, ok):
    t_ext, w_ext = FR_DEV + 2, W_DEV + 2
    lanes = lat.shape[-1]
    c = entry_kernel.shape[-1]
    kr = entry_kernel.reshape(27, LAT, c)
    vmem = pl.BlockSpec(memory_space=pltpu.VMEM)
    return pl.pallas_call(
        _entry_kernel,
        in_specs=[vmem, vmem, vmem, vmem, pl.BlockSpec(memory_space=pltpu.SMEM)],
        out_specs=(vmem, vmem),
        out_shape=(
            jax.ShapeDtypeStruct((t_ext, w_ext, H, c), jnp.bfloat16),
            jax.ShapeDtypeStruct((FR_DEV, W_DEV, H, c), jnp.bfloat16),
        ),
        scratch_shapes=[
            pltpu.VMEM((9 * lanes, w_ext * c), jnp.bfloat16),
            pltpu.VMEM((t_ext * H, 9 * lanes), jnp.bfloat16),
        ],
        compiler_params=pltpu.CompilerParams(vmem_limit_bytes=48 * 1024 * 1024),
        cost_estimate=pl.CostEstimate(
            flops=2 * t_ext * H * 9 * lanes * w_ext * c,
            transcendentals=t_ext * w_ext * H * c,
            bytes_accessed=lat.size * 4 + kr.size * 2 + (t_ext * w_ext + FR_DEV * W_DEV) * H * c * 2,
        ),
    )(lat, kr, entry_bias.reshape(1, c), gain_one.reshape(1, c), ok)


def shift2(value, ds, dk):
    n_tm, n_tile = lax.axis_size("tm"), lax.axis_size("tile")
    pairs = []
    for s in range(n_tm):
        for k in range(n_tile):
            if 0 <= s + ds < n_tm and 0 <= k + dk < n_tile:
                pairs.append((s * n_tile + k, (s + ds) * n_tile + k + dk))
    return lax.ppermute(value, ("tm", "tile"), pairs)


def gather_latent(latent_tokens, total_cols):
    n_tm, n_tile = lax.axis_size("tm"), lax.axis_size("tile")
    s = lax.axis_index("tm")
    rows_per = FR_DEV * H // n_tile
    span = (W_DEV + 4) * LAT
    strip = latent_tokens.reshape(rows_per, total_cols * LAT)
    strip = jnp.pad(strip, ((0, 0), (2 * LAT, 2 * LAT)))
    windows = jnp.stack(
        [strip[:, t * W_DEV * LAT : t * W_DEV * LAT + span] for t in range(n_tile)], axis=0
    )
    lag = jnp.arange(n_tm) - s
    wanted = ((lag >= 0) & (lag <= 2)).astype(windows.dtype)
    chunks = wanted[:, None, None, None] * windows[None]
    chunks = chunks.reshape((n_tm * n_tile,) + windows.shape[1:])
    got = lax.all_to_all(chunks, ("tm", "tile"), 0, 0, tiled=True)
    got = got.reshape((n_tm, n_tile) + windows.shape[1:])
    got = jnp.pad(got, ((2, 0), (0, 0), (0, 0), (0, 0)))
    got = lax.dynamic_slice_in_dim(got, s, 3, axis=0)
    return got.reshape(3 * FR_DEV, H, span)


def body(
    latent_tokens,
    entry_kernel,
    entry_bias,
    gain_one,
    first_kernel,
    first_bias,
    gain_two,
    second_kernel,
    second_bias,
):
    tiles = lax.axis_size("tile")
    total_cols = W_DEV * tiles
    s = lax.axis_index("tm")
    k = lax.axis_index("tile")
    c = entry_kernel.shape[-1]
    t_ext, w_ext = FR_DEV + 2, W_DEV + 2

    lat = gather_latent(latent_tokens, total_cols)
    lat = jnp.pad(lat, ((0, 0), (1, 1), (0, 0))).astype(jnp.float32)

    frame_ok = (s * FR_DEV - 2 + jnp.arange(t_ext)) >= 0
    col_id = k * W_DEV - 1 + jnp.arange(w_ext)
    col_ok = (col_id >= 0) & (col_id < total_cols)
    ok = (frame_ok[:, None] & col_ok[None, :]).astype(jnp.float32).reshape(-1)
    first_act, entry_own = entry_pallas(lat, entry_kernel, entry_bias, gain_one, ok)

    g2 = gain_two.reshape(1, c)
    rim = conv_pallas("act", first_act, first_kernel, first_bias, g2, bases=(0, W_DEV - 1))
    first, last = rim[:, :1], rim[:, 1:]
    left, right = shift2(last, 0, 1), shift2(first, 0, -1)
    prev_left, prev_right = shift2(last, 1, 1), shift2(first, 1, -1)
    prev_rim = shift2(rim, 1, 0)
    inner = conv_pallas("act", first_act, first_kernel, first_bias, g2, bases=range(1, W_DEV - 1))
    prev_inner = shift2(inner, 1, 0)
    own_ext = jnp.concatenate([left, first, inner, last, right], axis=1)
    prev_ext = jnp.concatenate(
        [prev_left, prev_rim[:, :1], prev_inner, prev_rim[:, 1:], prev_right], axis=1
    )
    ext2 = jnp.concatenate([prev_ext, own_ext], axis=0)

    decoded = conv_pallas("res", ext2, second_kernel, second_bias, entry_own)
    return jnp.transpose(decoded, (0, 2, 1, 3))


def solution(mesh):
    in_specs = (P(("tm", "tile"), None), P(), P(), P(), P(), P(), P(), P(), P())
    out_specs = P("tm", None, "tile", None)
    return jax.shard_map(body, mesh=mesh, in_specs=in_specs, out_specs=out_specs, check_vma=False)
```

```python
import functools

import jax
import jax.numpy as jnp
from jax import lax
from jax.experimental import pallas as pl
from jax.experimental.pallas import tpu as pltpu
from jax.sharding import PartitionSpec as P

LAT = 16
FR_DEV = 2
H = 96
W_DEV = 4


def shift_from(value, axis, steps):
    count = lax.axis_size(axis)
    pairs = [(i, i + steps) for i in range(max(0, -steps), min(count, count - steps))]
    return lax.ppermute(value, axis, pairs)


def _norm_silu(v, gain):
    scaled = v * lax.rsqrt(jnp.mean(v * v, axis=-1, keepdims=True) + 1e-06) * gain
    return scaled / (1.0 + jnp.exp(-scaled))


def _conv_kernel(mode, x_ref, w_ref, b_ref, e_ref, o_ref, acc_ref, cols_ref):
    d = pl.program_id(0)
    t_out, w_out, rows, co = o_ref.shape
    c = x_ref.shape[-1]
    m = t_out * w_out * rows

    @pl.when(d == 0)
    def _():
        for dt in range(3):
            for dj in range(3):
                q = dt * 3 + dj
                cols_ref[:, :, :, q * c : (q + 1) * c] = x_ref[dt : dt + t_out, dj : dj + w_out]

    lhs = cols_ref[...].reshape(m, 9 * c)
    part = jnp.dot(lhs, w_ref[:, 0].reshape(9 * c, co), preferred_element_type=jnp.float32)
    row = lax.broadcasted_iota(jnp.int32, (t_out * w_out, rows, co), 1).reshape(m, co)

    @pl.when(d == 0)
    def _():
        acc_ref[...] = jnp.where(row == 0, 0.0, pltpu.roll(part, 1, 0))

    @pl.when(d == 1)
    def _():
        acc_ref[...] += part

    @pl.when(d == 2)
    def _():
        below = jnp.where(row == rows - 1, 0.0, pltpu.roll(part, m - 1, 0))
        total = acc_ref[...] + below + b_ref[...]
        if mode == "act":
            mid = total.astype(jnp.bfloat16).astype(jnp.float32)
            res = _norm_silu(mid, e_ref[...])
        else:
            res = e_ref[...].reshape(m, co).astype(jnp.float32) + total
        o_ref[...] = res.astype(o_ref.dtype).reshape(o_ref.shape)


def conv_pallas(mode, field, kernel, bias, extra):
    tp, wp, rows, c = field.shape
    co = kernel.shape[-1]
    t_out, w_out = tp - 2, wp - 2
    out_shape = (t_out, w_out, rows, co)
    if mode == "act":
        e_spec = pl.BlockSpec((1, co), lambda d: (0, 0))
    else:
        e_spec = pl.BlockSpec(out_shape, lambda d: (0, 0, 0, 0))
    flops = 2 * t_out * w_out * rows * 27 * c * co
    return pl.pallas_call(
        functools.partial(_conv_kernel, mode),
        grid=(3,),
        in_specs=[
            pl.BlockSpec((tp, wp, rows, c), lambda d: (0, 0, 0, 0)),
            pl.BlockSpec((3, 1, 3, c, co), lambda d: (0, d, 0, 0, 0)),
            pl.BlockSpec((1, co), lambda d: (0, 0)),
            e_spec,
        ],
        out_specs=pl.BlockSpec(out_shape, lambda d: (0, 0, 0, 0)),
        out_shape=jax.ShapeDtypeStruct(out_shape, jnp.bfloat16),
        scratch_shapes=[
            pltpu.VMEM((t_out * w_out * rows, co), jnp.float32),
            pltpu.VMEM((t_out, w_out, rows, 9 * c), jnp.bfloat16),
        ],
        compiler_params=pltpu.CompilerParams(
            dimension_semantics=("arbitrary",), vmem_limit_bytes=48 * 1024 * 1024
        ),
        cost_estimate=pl.CostEstimate(
            flops=flops,
            transcendentals=0,
            bytes_accessed=field.size * 2 + kernel.size * 2 + t_out * w_out * rows * co * 4,
        ),
    )(field, kernel, bias.reshape(1, co), extra)


def _entry_kernel(lat_ref, k_ref, b_ref, g_ref, ok_ref, act_ref, own_ref, band_ref, patch_ref):
    t_ext, w_ext, rows, c = act_ref.shape
    lanes = lat_ref.shape[-1]
    lat_ch = k_ref.shape[1]
    band_ref[...] = jnp.zeros(band_ref.shape, band_ref.dtype)
    for dt in range(3):
        for di in range(3):
            p = dt * 3 + di
            for dj in range(3):
                for j in range(w_ext):
                    r0 = p * lanes + (j + dj) * lat_ch
                    band_ref[r0 : r0 + lat_ch, j * c : (j + 1) * c] = k_ref[p * 3 + dj]
            slab = lat_ref[dt : dt + t_ext, di : di + rows, :].reshape(t_ext * rows, lanes)
            patch_ref[:, p * lanes : (p + 1) * lanes] = slab.astype(patch_ref.dtype)
    for j in range(w_ext):
        e = jnp.dot(
            patch_ref[...], band_ref[:, j * c : (j + 1) * c], preferred_element_type=jnp.float32
        )
        e = (e + b_ref[...]).astype(jnp.bfloat16)
        if 1 <= j <= w_ext - 2:
            own_ref[:, j - 1] = e.reshape(t_ext, rows, c)[t_ext - FR_DEV :]
        fa = _norm_silu(e.astype(jnp.float32), g_ref[...]).reshape(t_ext, rows, c)
        for t in range(t_ext):
            act_ref[t, j] = (fa[t] * ok_ref[t * w_ext + j]).astype(act_ref.dtype)


def entry_pallas(lat, entry_kernel, entry_bias, gain_one, ok):
    t_ext, w_ext = FR_DEV + 2, W_DEV + 2
    lanes = lat.shape[-1]
    c = entry_kernel.shape[-1]
    kr = entry_kernel.reshape(27, LAT, c)
    vmem = pl.BlockSpec(memory_space=pltpu.VMEM)
    return pl.pallas_call(
        _entry_kernel,
        in_specs=[vmem, vmem, vmem, vmem, pl.BlockSpec(memory_space=pltpu.SMEM)],
        out_specs=(vmem, vmem),
        out_shape=(
            jax.ShapeDtypeStruct((t_ext, w_ext, H, c), jnp.bfloat16),
            jax.ShapeDtypeStruct((FR_DEV, W_DEV, H, c), jnp.bfloat16),
        ),
        scratch_shapes=[
            pltpu.VMEM((9 * lanes, w_ext * c), jnp.bfloat16),
            pltpu.VMEM((t_ext * H, 9 * lanes), jnp.bfloat16),
        ],
        compiler_params=pltpu.CompilerParams(vmem_limit_bytes=48 * 1024 * 1024),
        cost_estimate=pl.CostEstimate(
            flops=2 * t_ext * H * 9 * lanes * w_ext * c,
            transcendentals=t_ext * w_ext * H * c,
            bytes_accessed=lat.size * 4 + kr.size * 2 + (t_ext * w_ext + FR_DEV * W_DEV) * H * c * 2,
        ),
    )(lat, kr, entry_bias.reshape(1, c), gain_one.reshape(1, c), ok)


def _entry_conv_kernel(
    lat_ref, ke_ref, be_ref, g1_ref, ok_ref, w_ref, b_ref, g2_ref,
    o_ref, own_ref, act_ref, band_ref, patch_ref, acc_ref, cols_ref,
):
    @pl.when(pl.program_id(0) == 0)
    def _():
        _entry_kernel(lat_ref, ke_ref, be_ref, g1_ref, ok_ref, act_ref, own_ref, band_ref, patch_ref)

    _conv_kernel("act", act_ref, w_ref, b_ref, g2_ref, o_ref, acc_ref, cols_ref)


def entry_conv_pallas(lat, entry_kernel, entry_bias, gain_one, ok, kernel, bias, gain_two):
    t_ext, w_ext = FR_DEV + 2, W_DEV + 2
    lanes = lat.shape[-1]
    c = entry_kernel.shape[-1]
    co = kernel.shape[-1]
    kr = entry_kernel.reshape(27, LAT, c)
    out_shape = (FR_DEV, W_DEV, H, co)
    m = FR_DEV * W_DEV * H
    const3 = lambda d: (0, 0, 0)
    row = pl.BlockSpec((1, c), lambda d: (0, 0))
    whole = pl.BlockSpec(out_shape, lambda d: (0, 0, 0, 0))
    flops = 2 * t_ext * H * 9 * lanes * w_ext * c + 2 * m * 27 * c * co
    return pl.pallas_call(
        _entry_conv_kernel,
        grid=(3,),
        in_specs=[
            pl.BlockSpec(lat.shape, const3),
            pl.BlockSpec(kr.shape, const3),
            row,
            row,
            pl.BlockSpec(memory_space=pltpu.SMEM),
            pl.BlockSpec((3, 1, 3, c, co), lambda d: (0, d, 0, 0, 0)),
            row,
            row,
        ],
        out_specs=(whole, whole),
        out_shape=(
            jax.ShapeDtypeStruct(out_shape, jnp.bfloat16),
            jax.ShapeDtypeStruct(out_shape, jnp.bfloat16),
        ),
        scratch_shapes=[
            pltpu.VMEM((t_ext, w_ext, H, c), jnp.bfloat16),
            pltpu.VMEM((9 * lanes, w_ext * c), jnp.bfloat16),
            pltpu.VMEM((t_ext * H, 9 * lanes), jnp.bfloat16),
            pltpu.VMEM((m, co), jnp.float32),
            pltpu.VMEM((FR_DEV, W_DEV, H, 9 * c), jnp.bfloat16),
        ],
        compiler_params=pltpu.CompilerParams(
            dimension_semantics=("arbitrary",), vmem_limit_bytes=48 * 1024 * 1024
        ),
        cost_estimate=pl.CostEstimate(
            flops=flops,
            transcendentals=t_ext * w_ext * H * c + m * co,
            bytes_accessed=lat.size * 4 + kr.size * 2 + kernel.size * 2 + 2 * m * co * 2,
        ),
    )(lat, kr, entry_bias.reshape(1, c), gain_one.reshape(1, c), ok, kernel,
      bias.reshape(1, co), gain_two.reshape(1, c))


def shift2(value, ds, dk):
    n_tm, n_tile = lax.axis_size("tm"), lax.axis_size("tile")
    pairs = []
    for s in range(n_tm):
        for k in range(n_tile):
            if 0 <= s + ds < n_tm and 0 <= k + dk < n_tile:
                pairs.append((s * n_tile + k, (s + ds) * n_tile + k + dk))
    return lax.ppermute(value, ("tm", "tile"), pairs)


def gather_latent(latent_tokens, total_cols):
    n_tm, n_tile = lax.axis_size("tm"), lax.axis_size("tile")
    s = lax.axis_index("tm")
    rows_per = FR_DEV * H // n_tile
    span = (W_DEV + 4) * LAT
    strip = latent_tokens.reshape(rows_per, total_cols * LAT)
    strip = jnp.pad(strip, ((0, 0), (2 * LAT, 2 * LAT)))
    windows = jnp.stack(
        [strip[:, t * W_DEV * LAT : t * W_DEV * LAT + span] for t in range(n_tile)], axis=0
    )
    lag = jnp.arange(n_tm) - s
    wanted = ((lag >= 0) & (lag <= 2)).astype(windows.dtype)
    chunks = wanted[:, None, None, None] * windows[None]
    chunks = chunks.reshape((n_tm * n_tile,) + windows.shape[1:])
    got = lax.all_to_all(chunks, ("tm", "tile"), 0, 0, tiled=True)
    got = got.reshape((n_tm, n_tile) + windows.shape[1:])
    got = jnp.pad(got, ((2, 0), (0, 0), (0, 0), (0, 0)))
    got = lax.dynamic_slice_in_dim(got, s, 3, axis=0)
    return got.reshape(3 * FR_DEV, H, span)


def body(
    latent_tokens,
    entry_kernel,
    entry_bias,
    gain_one,
    first_kernel,
    first_bias,
    gain_two,
    second_kernel,
    second_bias,
):
    tiles = lax.axis_size("tile")
    total_cols = W_DEV * tiles
    s = lax.axis_index("tm")
    k = lax.axis_index("tile")
    c = entry_kernel.shape[-1]
    t_ext, w_ext = FR_DEV + 2, W_DEV + 2

    lat = gather_latent(latent_tokens, total_cols)
    lat = jnp.pad(lat, ((0, 0), (1, 1), (0, 0))).astype(jnp.float32)

    frame_ok = (s * FR_DEV - 2 + jnp.arange(t_ext)) >= 0
    col_id = k * W_DEV - 1 + jnp.arange(w_ext)
    col_ok = (col_id >= 0) & (col_id < total_cols)
    ok = (frame_ok[:, None] & col_ok[None, :]).astype(jnp.float32).reshape(-1)
    second_act, entry_own = entry_conv_pallas(
        lat, entry_kernel, entry_bias, gain_one, ok, first_kernel, first_bias, gain_two
    )

    last, first = second_act[:, W_DEV - 1 :], second_act[:, :1]
    own_row = [shift2(last, 0, 1), second_act, shift2(first, 0, -1)]
    prev_row = [shift2(last, 1, 1), shift2(second_act, 1, 0), shift2(first, 1, -1)]
    ext2 = jnp.concatenate(
        [jnp.concatenate(prev_row, axis=1), jnp.concatenate(own_row, axis=1)], axis=0
    )

    decoded = conv_pallas("res", ext2, second_kernel, second_bias, entry_own)
    return jnp.transpose(decoded, (0, 2, 1, 3))


def solution(mesh):
    in_specs = (P(("tm", "tile"), None), P(), P(), P(), P(), P(), P(), P(), P())
    out_specs = P("tm", None, "tile", None)
    return jax.shard_map(body, mesh=mesh, in_specs=in_specs, out_specs=out_specs, check_vma=False)
```

```python
import functools

import jax
import jax.numpy as jnp
from jax import lax
from jax.experimental import pallas as pl
from jax.experimental.pallas import tpu as pltpu
from jax.sharding import PartitionSpec as P

LAT = 16
FR_DEV = 2
H = 96
W_DEV = 4


def shift_from(value, axis, steps):
    count = lax.axis_size(axis)
    pairs = [(i, i + steps) for i in range(max(0, -steps), min(count, count - steps))]
    return lax.ppermute(value, axis, pairs)


def _norm_silu(v, gain):
    scaled = v * lax.rsqrt(jnp.mean(v * v, axis=-1, keepdims=True) + 1e-06) * gain
    return scaled / (1.0 + jnp.exp(-scaled))


def _conv_kernel(mode, x_ref, w_ref, b_ref, e_ref, o_ref, acc_ref, cols_ref):
    d = pl.program_id(0)
    t_out, w_out, rows = cols_ref.shape[:3]
    co = o_ref.shape[-1]
    c = x_ref.shape[-1]
    m = t_out * w_out * rows

    @pl.when(d == 0)
    def _():
        for dt in range(3):
            for dj in range(3):
                q = dt * 3 + dj
                cols_ref[:, :, :, q * c : (q + 1) * c] = x_ref[dt : dt + t_out, dj : dj + w_out]

    lhs = cols_ref[...].reshape(m, 9 * c)
    part = jnp.dot(lhs, w_ref[:, 0].reshape(9 * c, co), preferred_element_type=jnp.float32)
    row = lax.broadcasted_iota(jnp.int32, (t_out * w_out, rows, co), 1).reshape(m, co)

    @pl.when(d == 0)
    def _():
        acc_ref[...] = jnp.where(row == 0, 0.0, pltpu.roll(part, 1, 0))

    @pl.when(d == 1)
    def _():
        acc_ref[...] += part

    @pl.when(d == 2)
    def _():
        below = jnp.where(row == rows - 1, 0.0, pltpu.roll(part, m - 1, 0))
        total = acc_ref[...] + below + b_ref[...]
        if mode == "act":
            mid = total.astype(jnp.bfloat16).astype(jnp.float32)
            res = _norm_silu(mid, e_ref[...])
            o_ref[...] = res.astype(o_ref.dtype).reshape(o_ref.shape)
        else:
            res = e_ref[...].reshape(m, co).astype(jnp.float32) + total
            res = res.astype(o_ref.dtype).reshape(t_out, w_out, rows, co)
            for t in range(t_out):
                for j in range(w_out):
                    o_ref[t, :, j, :] = res[t, j]


def conv_pallas(mode, field, kernel, bias, extra):
    tp, wp, rows, c = field.shape
    co = kernel.shape[-1]
    t_out, w_out = tp - 2, wp - 2
    out_shape = (t_out, w_out, rows, co)
    if mode == "act":
        e_spec = pl.BlockSpec((1, co), lambda d: (0, 0))
    else:
        e_spec = pl.BlockSpec(out_shape, lambda d: (0, 0, 0, 0))
    final_shape = (t_out, rows, w_out, co) if mode == "res" else out_shape
    flops = 2 * t_out * w_out * rows * 27 * c * co
    return pl.pallas_call(
        functools.partial(_conv_kernel, mode),
        grid=(3,),
        in_specs=[
            pl.BlockSpec((tp, wp, rows, c), lambda d: (0, 0, 0, 0)),
            pl.BlockSpec((3, 1, 3, c, co), lambda d: (0, d, 0, 0, 0)),
            pl.BlockSpec((1, co), lambda d: (0, 0)),
            e_spec,
        ],
        out_specs=pl.BlockSpec(final_shape, lambda d: (0, 0, 0, 0)),
        out_shape=jax.ShapeDtypeStruct(final_shape, jnp.bfloat16),
        scratch_shapes=[
            pltpu.VMEM((t_out * w_out * rows, co), jnp.float32),
            pltpu.VMEM((t_out, w_out, rows, 9 * c), jnp.bfloat16),
        ],
        compiler_params=pltpu.CompilerParams(
            dimension_semantics=("arbitrary",), vmem_limit_bytes=48 * 1024 * 1024
        ),
        cost_estimate=pl.CostEstimate(
            flops=flops,
            transcendentals=0,
            bytes_accessed=field.size * 2 + kernel.size * 2 + t_out * w_out * rows * co * 4,
        ),
    )(field, kernel, bias.reshape(1, co), extra)


def _entry_kernel(lat_ref, k_ref, b_ref, g_ref, ok_ref, act_ref, own_ref, band_ref, patch_ref):
    t_ext, w_ext, rows, c = act_ref.shape
    lanes = lat_ref.shape[-1]
    lat_ch = k_ref.shape[1]
    band_ref[...] = jnp.zeros(band_ref.shape, band_ref.dtype)
    for dt in range(3):
        for di in range(3):
            p = dt * 3 + di
            for dj in range(3):
                for j in range(w_ext):
                    r0 = p * lanes + (j + dj) * lat_ch
                    band_ref[r0 : r0 + lat_ch, j * c : (j + 1) * c] = k_ref[p * 3 + dj]
            slab = lat_ref[dt : dt + t_ext, di : di + rows, :].reshape(t_ext * rows, lanes)
            patch_ref[:, p * lanes : (p + 1) * lanes] = slab.astype(patch_ref.dtype)
    for j in range(w_ext):
        e = jnp.dot(
            patch_ref[...], band_ref[:, j * c : (j + 1) * c], preferred_element_type=jnp.float32
        )
        e = (e + b_ref[...]).astype(jnp.bfloat16)
        if 1 <= j <= w_ext - 2:
            own_ref[:, j - 1] = e.reshape(t_ext, rows, c)[t_ext - FR_DEV :]
        fa = _norm_silu(e.astype(jnp.float32), g_ref[...]).reshape(t_ext, rows, c)
        for t in range(t_ext):
            act_ref[t, j] = (fa[t] * ok_ref[t * w_ext + j]).astype(act_ref.dtype)


def entry_pallas(lat, entry_kernel, entry_bias, gain_one, ok):
    t_ext, w_ext = FR_DEV + 2, W_DEV + 2
    lanes = lat.shape[-1]
    c = entry_kernel.shape[-1]
    kr = entry_kernel.reshape(27, LAT, c)
    vmem = pl.BlockSpec(memory_space=pltpu.VMEM)
    return pl.pallas_call(
        _entry_kernel,
        in_specs=[vmem, vmem, vmem, vmem, pl.BlockSpec(memory_space=pltpu.SMEM)],
        out_specs=(vmem, vmem),
        out_shape=(
            jax.ShapeDtypeStruct((t_ext, w_ext, H, c), jnp.bfloat16),
            jax.ShapeDtypeStruct((FR_DEV, W_DEV, H, c), jnp.bfloat16),
        ),
        scratch_shapes=[
            pltpu.VMEM((9 * lanes, w_ext * c), jnp.bfloat16),
            pltpu.VMEM((t_ext * H, 9 * lanes), jnp.bfloat16),
        ],
        compiler_params=pltpu.CompilerParams(vmem_limit_bytes=48 * 1024 * 1024),
        cost_estimate=pl.CostEstimate(
            flops=2 * t_ext * H * 9 * lanes * w_ext * c,
            transcendentals=t_ext * w_ext * H * c,
            bytes_accessed=lat.size * 4 + kr.size * 2 + (t_ext * w_ext + FR_DEV * W_DEV) * H * c * 2,
        ),
    )(lat, kr, entry_bias.reshape(1, c), gain_one.reshape(1, c), ok)


def _entry_conv_kernel(
    lat_ref, ke_ref, be_ref, g1_ref, ok_ref, w_ref, b_ref, g2_ref,
    o_ref, own_ref, act_ref, band_ref, patch_ref, acc_ref, cols_ref,
):
    @pl.when(pl.program_id(0) == 0)
    def _():
        _entry_kernel(lat_ref, ke_ref, be_ref, g1_ref, ok_ref, act_ref, own_ref, band_ref, patch_ref)

    _conv_kernel("act", act_ref, w_ref, b_ref, g2_ref, o_ref, acc_ref, cols_ref)


def entry_conv_pallas(lat, entry_kernel, entry_bias, gain_one, ok, kernel, bias, gain_two):
    t_ext, w_ext = FR_DEV + 2, W_DEV + 2
    lanes = lat.shape[-1]
    c = entry_kernel.shape[-1]
    co = kernel.shape[-1]
    kr = entry_kernel.reshape(27, LAT, c)
    out_shape = (FR_DEV, W_DEV, H, co)
    m = FR_DEV * W_DEV * H
    const3 = lambda d: (0, 0, 0)
    row = pl.BlockSpec((1, c), lambda d: (0, 0))
    whole = pl.BlockSpec(out_shape, lambda d: (0, 0, 0, 0))
    flops = 2 * t_ext * H * 9 * lanes * w_ext * c + 2 * m * 27 * c * co
    return pl.pallas_call(
        _entry_conv_kernel,
        grid=(3,),
        in_specs=[
            pl.BlockSpec(lat.shape, const3),
            pl.BlockSpec(kr.shape, const3),
            row,
            row,
            pl.BlockSpec(memory_space=pltpu.SMEM),
            pl.BlockSpec((3, 1, 3, c, co), lambda d: (0, d, 0, 0, 0)),
            row,
            row,
        ],
        out_specs=(whole, whole),
        out_shape=(
            jax.ShapeDtypeStruct(out_shape, jnp.bfloat16),
            jax.ShapeDtypeStruct(out_shape, jnp.bfloat16),
        ),
        scratch_shapes=[
            pltpu.VMEM((t_ext, w_ext, H, c), jnp.bfloat16),
            pltpu.VMEM((9 * lanes, w_ext * c), jnp.bfloat16),
            pltpu.VMEM((t_ext * H, 9 * lanes), jnp.bfloat16),
            pltpu.VMEM((m, co), jnp.float32),
            pltpu.VMEM((FR_DEV, W_DEV, H, 9 * c), jnp.bfloat16),
        ],
        compiler_params=pltpu.CompilerParams(
            dimension_semantics=("arbitrary",), vmem_limit_bytes=48 * 1024 * 1024
        ),
        cost_estimate=pl.CostEstimate(
            flops=flops,
            transcendentals=t_ext * w_ext * H * c + m * co,
            bytes_accessed=lat.size * 4 + kr.size * 2 + kernel.size * 2 + 2 * m * co * 2,
        ),
    )(lat, kr, entry_bias.reshape(1, c), gain_one.reshape(1, c), ok, kernel,
      bias.reshape(1, co), gain_two.reshape(1, c))


def shift2(value, ds, dk):
    n_tm, n_tile = lax.axis_size("tm"), lax.axis_size("tile")
    pairs = []
    for s in range(n_tm):
        for k in range(n_tile):
            if 0 <= s + ds < n_tm and 0 <= k + dk < n_tile:
                pairs.append((s * n_tile + k, (s + ds) * n_tile + k + dk))
    return lax.ppermute(value, ("tm", "tile"), pairs)


def gather_latent(latent_tokens, total_cols):
    n_tm, n_tile = lax.axis_size("tm"), lax.axis_size("tile")
    s = lax.axis_index("tm")
    rows_per = FR_DEV * H // n_tile
    span = (W_DEV + 4) * LAT
    strip = latent_tokens.reshape(rows_per, total_cols * LAT)
    strip = jnp.pad(strip, ((0, 0), (2 * LAT, 2 * LAT)))
    windows = jnp.stack(
        [strip[:, t * W_DEV * LAT : t * W_DEV * LAT + span] for t in range(n_tile)], axis=0
    )
    lag = jnp.arange(n_tm) - s
    wanted = ((lag >= 0) & (lag <= 2)).astype(windows.dtype)
    chunks = wanted[:, None, None, None] * windows[None]
    chunks = chunks.reshape((n_tm * n_tile,) + windows.shape[1:])
    got = lax.all_to_all(chunks, ("tm", "tile"), 0, 0, tiled=True)
    got = got.reshape((n_tm, n_tile) + windows.shape[1:])
    got = jnp.pad(got, ((2, 0), (0, 0), (0, 0), (0, 0)))
    got = lax.dynamic_slice_in_dim(got, s, 3, axis=0)
    return got.reshape(3 * FR_DEV, H, span)


def body(
    latent_tokens,
    entry_kernel,
    entry_bias,
    gain_one,
    first_kernel,
    first_bias,
    gain_two,
    second_kernel,
    second_bias,
):
    tiles = lax.axis_size("tile")
    total_cols = W_DEV * tiles
    s = lax.axis_index("tm")
    k = lax.axis_index("tile")
    c = entry_kernel.shape[-1]
    t_ext, w_ext = FR_DEV + 2, W_DEV + 2

    lat = gather_latent(latent_tokens, total_cols)
    lat = jnp.pad(lat, ((0, 0), (1, 1), (0, 0))).astype(jnp.float32)

    frame_ok = (s * FR_DEV - 2 + jnp.arange(t_ext)) >= 0
    col_id = k * W_DEV - 1 + jnp.arange(w_ext)
    col_ok = (col_id >= 0) & (col_id < total_cols)
    ok = (frame_ok[:, None] & col_ok[None, :]).astype(jnp.float32).reshape(-1)
    second_act, entry_own = entry_conv_pallas(
        lat, entry_kernel, entry_bias, gain_one, ok, first_kernel, first_bias, gain_two
    )

    last, first = second_act[:, W_DEV - 1 :], second_act[:, :1]
    own_row = [shift2(last, 0, 1), second_act, shift2(first, 0, -1)]
    prev_row = [shift2(last, 1, 1), shift2(second_act, 1, 0), shift2(first, 1, -1)]
    ext2 = jnp.concatenate(
        [jnp.concatenate(prev_row, axis=1), jnp.concatenate(own_row, axis=1)], axis=0
    )

    return conv_pallas("res", ext2, second_kernel, second_bias, entry_own)


def solution(mesh):
    in_specs = (P(("tm", "tile"), None), P(), P(), P(), P(), P(), P(), P(), P())
    out_specs = P("tm", None, "tile", None)
    return jax.shard_map(body, mesh=mesh, in_specs=in_specs, out_specs=out_specs, check_vma=False)
```

```python
import functools

import jax
import jax.numpy as jnp
from jax import lax
from jax.experimental import pallas as pl
from jax.experimental.pallas import tpu as pltpu
from jax.sharding import PartitionSpec as P

LAT = 16
FR_DEV = 2
H = 96
W_DEV = 4


def shift_from(value, axis, steps):
    count = lax.axis_size(axis)
    pairs = [(i, i + steps) for i in range(max(0, -steps), min(count, count - steps))]
    return lax.ppermute(value, axis, pairs)


def _norm_silu(v, gain):
    scaled = v * lax.rsqrt(jnp.mean(v * v, axis=-1, keepdims=True) + 1e-06) * gain
    return scaled / (1.0 + jnp.exp(-scaled))


def _conv_kernel(mode, x_ref, w_ref, b_ref, e_ref, o_ref, acc_ref, cols_ref):
    d = pl.program_id(0)
    t_out, w_out, rows, co = o_ref.shape
    c = cols_ref.shape[-1] // 9
    m = t_out * w_out * rows

    if x_ref is not None:

        @pl.when(d == 0)
        def _():
            for dt in range(3):
                for dj in range(3):
                    q = dt * 3 + dj
                    cols_ref[:, :, :, q * c : (q + 1) * c] = x_ref[
                        dt : dt + t_out, dj : dj + w_out
                    ]

    lhs = cols_ref[...].reshape(m, 9 * c)
    part = jnp.dot(lhs, w_ref[:, 0].reshape(9 * c, co), preferred_element_type=jnp.float32)
    row = lax.broadcasted_iota(jnp.int32, (t_out * w_out, rows, co), 1).reshape(m, co)

    @pl.when(d == 0)
    def _():
        acc_ref[...] = jnp.where(row == 0, 0.0, pltpu.roll(part, 1, 0))

    @pl.when(d == 1)
    def _():
        acc_ref[...] += part

    @pl.when(d == 2)
    def _():
        below = jnp.where(row == rows - 1, 0.0, pltpu.roll(part, m - 1, 0))
        total = acc_ref[...] + below + b_ref[...]
        if mode == "act":
            mid = total.astype(jnp.bfloat16).astype(jnp.float32)
            res = _norm_silu(mid, e_ref[...])
        else:
            res = e_ref[...].reshape(m, co).astype(jnp.float32) + total
        o_ref[...] = res.astype(o_ref.dtype).reshape(o_ref.shape)


def conv_pallas(mode, field, kernel, bias, extra):
    tp, wp, rows, c = field.shape
    co = kernel.shape[-1]
    t_out, w_out = tp - 2, wp - 2
    out_shape = (t_out, w_out, rows, co)
    if mode == "act":
        e_spec = pl.BlockSpec((1, co), lambda d: (0, 0))
    else:
        e_spec = pl.BlockSpec(out_shape, lambda d: (0, 0, 0, 0))
    flops = 2 * t_out * w_out * rows * 27 * c * co
    return pl.pallas_call(
        functools.partial(_conv_kernel, mode),
        grid=(3,),
        in_specs=[
            pl.BlockSpec((tp, wp, rows, c), lambda d: (0, 0, 0, 0)),
            pl.BlockSpec((3, 1, 3, c, co), lambda d: (0, d, 0, 0, 0)),
            pl.BlockSpec((1, co), lambda d: (0, 0)),
            e_spec,
        ],
        out_specs=pl.BlockSpec(out_shape, lambda d: (0, 0, 0, 0)),
        out_shape=jax.ShapeDtypeStruct(out_shape, jnp.bfloat16),
        scratch_shapes=[
            pltpu.VMEM((t_out * w_out * rows, co), jnp.float32),
            pltpu.VMEM((t_out, w_out, rows, 9 * c), jnp.bfloat16),
        ],
        compiler_params=pltpu.CompilerParams(
            dimension_semantics=("arbitrary",), vmem_limit_bytes=48 * 1024 * 1024
        ),
        cost_estimate=pl.CostEstimate(
            flops=flops,
            transcendentals=0,
            bytes_accessed=field.size * 2 + kernel.size * 2 + t_out * w_out * rows * co * 4,
        ),
    )(field, kernel, bias.reshape(1, co), extra)


def _entry_kernel(lat_ref, k_ref, b_ref, g_ref, ok_ref, act_ref, own_ref, band_ref, patch_ref):
    t_ext, w_ext, rows, c = act_ref.shape
    lanes = lat_ref.shape[-1]
    lat_ch = k_ref.shape[1]
    band_ref[...] = jnp.zeros(band_ref.shape, band_ref.dtype)
    for dt in range(3):
        for di in range(3):
            p = dt * 3 + di
            for dj in range(3):
                for j in range(w_ext):
                    r0 = p * lanes + (j + dj) * lat_ch
                    band_ref[r0 : r0 + lat_ch, j * c : (j + 1) * c] = k_ref[p * 3 + dj]
            slab = lat_ref[dt : dt + t_ext, di : di + rows, :].reshape(t_ext * rows, lanes)
            patch_ref[:, p * lanes : (p + 1) * lanes] = slab.astype(patch_ref.dtype)
    for j in range(w_ext):
        e = jnp.dot(
            patch_ref[...], band_ref[:, j * c : (j + 1) * c], preferred_element_type=jnp.float32
        )
        e = (e + b_ref[...]).astype(jnp.bfloat16)
        if 1 <= j <= w_ext - 2:
            own_ref[:, j - 1] = e.reshape(t_ext, rows, c)[t_ext - FR_DEV :]
        fa = _norm_silu(e.astype(jnp.float32), g_ref[...]).reshape(t_ext, rows, c)
        for t in range(t_ext):
            act_ref[t, j] = (fa[t] * ok_ref[t * w_ext + j]).astype(act_ref.dtype)


def entry_pallas(lat, entry_kernel, entry_bias, gain_one, ok):
    t_ext, w_ext = FR_DEV + 2, W_DEV + 2
    lanes = lat.shape[-1]
    c = entry_kernel.shape[-1]
    kr = entry_kernel.reshape(27, LAT, c)
    vmem = pl.BlockSpec(memory_space=pltpu.VMEM)
    return pl.pallas_call(
        _entry_kernel,
        in_specs=[vmem, vmem, vmem, vmem, pl.BlockSpec(memory_space=pltpu.SMEM)],
        out_specs=(vmem, vmem),
        out_shape=(
            jax.ShapeDtypeStruct((t_ext, w_ext, H, c), jnp.bfloat16),
            jax.ShapeDtypeStruct((FR_DEV, W_DEV, H, c), jnp.bfloat16),
        ),
        scratch_shapes=[
            pltpu.VMEM((9 * lanes, w_ext * c), jnp.bfloat16),
            pltpu.VMEM((t_ext * H, 9 * lanes), jnp.bfloat16),
        ],
        compiler_params=pltpu.CompilerParams(vmem_limit_bytes=48 * 1024 * 1024),
        cost_estimate=pl.CostEstimate(
            flops=2 * t_ext * H * 9 * lanes * w_ext * c,
            transcendentals=t_ext * w_ext * H * c,
            bytes_accessed=lat.size * 4 + kr.size * 2 + (t_ext * w_ext + FR_DEV * W_DEV) * H * c * 2,
        ),
    )(lat, kr, entry_bias.reshape(1, c), gain_one.reshape(1, c), ok)


def _entry_conv_kernel(
    lat_ref, ke_ref, be_ref, g1_ref, ok_ref, w_ref, b_ref, g2_ref,
    o_ref, own_ref, act_ref, band_ref, patch_ref, acc_ref, cols_ref,
):
    @pl.when(pl.program_id(0) == 0)
    def _():
        _entry_kernel(lat_ref, ke_ref, be_ref, g1_ref, ok_ref, act_ref, own_ref, band_ref, patch_ref)

    _conv_kernel("act", act_ref, w_ref, b_ref, g2_ref, o_ref, acc_ref, cols_ref)


def entry_conv_pallas(lat, entry_kernel, entry_bias, gain_one, ok, kernel, bias, gain_two):
    t_ext, w_ext = FR_DEV + 2, W_DEV + 2
    lanes = lat.shape[-1]
    c = entry_kernel.shape[-1]
    co = kernel.shape[-1]
    kr = entry_kernel.reshape(27, LAT, c)
    out_shape = (FR_DEV, W_DEV, H, co)
    m = FR_DEV * W_DEV * H
    const3 = lambda d: (0, 0, 0)
    row = pl.BlockSpec((1, c), lambda d: (0, 0))
    whole = pl.BlockSpec(out_shape, lambda d: (0, 0, 0, 0))
    flops = 2 * t_ext * H * 9 * lanes * w_ext * c + 2 * m * 27 * c * co
    return pl.pallas_call(
        _entry_conv_kernel,
        grid=(3,),
        in_specs=[
            pl.BlockSpec(lat.shape, const3),
            pl.BlockSpec(kr.shape, const3),
            row,
            row,
            pl.BlockSpec(memory_space=pltpu.SMEM),
            pl.BlockSpec((3, 1, 3, c, co), lambda d: (0, d, 0, 0, 0)),
            row,
            row,
        ],
        out_specs=(whole, whole),
        out_shape=(
            jax.ShapeDtypeStruct(out_shape, jnp.bfloat16),
            jax.ShapeDtypeStruct(out_shape, jnp.bfloat16),
        ),
        scratch_shapes=[
            pltpu.VMEM((t_ext, w_ext, H, c), jnp.bfloat16),
            pltpu.VMEM((9 * lanes, w_ext * c), jnp.bfloat16),
            pltpu.VMEM((t_ext * H, 9 * lanes), jnp.bfloat16),
            pltpu.VMEM((m, co), jnp.float32),
            pltpu.VMEM((FR_DEV, W_DEV, H, 9 * c), jnp.bfloat16),
        ],
        compiler_params=pltpu.CompilerParams(
            dimension_semantics=("arbitrary",), vmem_limit_bytes=48 * 1024 * 1024
        ),
        cost_estimate=pl.CostEstimate(
            flops=flops,
            transcendentals=t_ext * w_ext * H * c + m * co,
            bytes_accessed=lat.size * 4 + kr.size * 2 + kernel.size * 2 + 2 * m * co * 2,
        ),
    )(lat, kr, entry_bias.reshape(1, c), gain_one.reshape(1, c), ok, kernel,
      bias.reshape(1, co), gain_two.reshape(1, c))


def _res_kernel(
    prev_ref, pl_ref, pr_ref, own_ref, l_ref, r_ref, w_ref, b_ref, e_ref, o_ref, acc_ref, cols_ref
):
    t_out, w_out, rows = cols_ref.shape[:3]
    c = own_ref.shape[-1]

    @pl.when(pl.program_id(0) == 0)
    def _():
        frames = [(prev_ref, pl_ref, pr_ref, f) for f in range(t_out)]
        frames += [(own_ref, l_ref, r_ref, f) for f in range(t_out)]
        for dt in range(3):
            for dj in range(3):
                q = dt * 3 + dj
                for t in range(t_out):
                    mid, lft, rgt, f = frames[t + dt]
                    for j in range(w_out):
                        e = j + dj
                        if e == 0:
                            src = lft[f, 0]
                        elif e == w_out + 1:
                            src = rgt[f, 0]
                        else:
                            src = mid[f, e - 1]
                        cols_ref[t, j, :, q * c : (q + 1) * c] = src

    _conv_kernel("res", None, w_ref, b_ref, e_ref, o_ref, acc_ref, cols_ref)


def res_pallas(prev, prev_left, prev_right, own, left, right, kernel, bias, entry_own):
    t_out, w_out, rows, c = own.shape
    co = kernel.shape[-1]
    out_shape = (t_out, w_out, rows, co)
    whole = pl.BlockSpec(out_shape, lambda d: (0, 0, 0, 0))
    rim = pl.BlockSpec((t_out, 1, rows, c), lambda d: (0, 0, 0, 0))
    m = t_out * w_out * rows
    return pl.pallas_call(
        _res_kernel,
        grid=(3,),
        in_specs=[
            whole, rim, rim, whole, rim, rim,
            pl.BlockSpec((3, 1, 3, c, co), lambda d: (0, d, 0, 0, 0)),
            pl.BlockSpec((1, co), lambda d: (0, 0)),
            whole,
        ],
        out_specs=whole,
        out_shape=jax.ShapeDtypeStruct(out_shape, jnp.bfloat16),
        scratch_shapes=[
            pltpu.VMEM((m, co), jnp.float32),
            pltpu.VMEM((t_out, w_out, rows, 9 * c), jnp.bfloat16),
        ],
        compiler_params=pltpu.CompilerParams(
            dimension_semantics=("arbitrary",), vmem_limit_bytes=48 * 1024 * 1024
        ),
        cost_estimate=pl.CostEstimate(
            flops=2 * m * 27 * c * co,
            transcendentals=0,
            bytes_accessed=3 * m * c * 2 + kernel.size * 2 + m * co * 4,
        ),
    )(prev, prev_left, prev_right, own, left, right, kernel, bias.reshape(1, co), entry_own)


def shift2(value, ds, dk):
    n_tm, n_tile = lax.axis_size("tm"), lax.axis_size("tile")
    pairs = []
    for s in range(n_tm):
        for k in range(n_tile):
            if 0 <= s + ds < n_tm and 0 <= k + dk < n_tile:
                pairs.append((s * n_tile + k, (s + ds) * n_tile + k + dk))
    return lax.ppermute(value, ("tm", "tile"), pairs)


def gather_latent(latent_tokens, total_cols):
    n_tm, n_tile = lax.axis_size("tm"), lax.axis_size("tile")
    s = lax.axis_index("tm")
    rows_per = FR_DEV * H // n_tile
    span = (W_DEV + 4) * LAT
    strip = latent_tokens.reshape(rows_per, total_cols * LAT)
    strip = jnp.pad(strip, ((0, 0), (2 * LAT, 2 * LAT)))
    windows = jnp.stack(
        [strip[:, t * W_DEV * LAT : t * W_DEV * LAT + span] for t in range(n_tile)], axis=0
    )
    lag = jnp.arange(n_tm) - s
    wanted = ((lag >= 0) & (lag <= 2)).astype(windows.dtype)
    chunks = wanted[:, None, None, None] * windows[None]
    chunks = chunks.reshape((n_tm * n_tile,) + windows.shape[1:])
    got = lax.all_to_all(chunks, ("tm", "tile"), 0, 0, tiled=True)
    got = got.reshape((n_tm, n_tile) + windows.shape[1:])
    got = jnp.pad(got, ((2, 0), (0, 0), (0, 0), (0, 0)))
    got = lax.dynamic_slice_in_dim(got, s, 3, axis=0)
    return got.reshape(3 * FR_DEV, H, span)


def body(
    latent_tokens,
    entry_kernel,
    entry_bias,
    gain_one,
    first_kernel,
    first_bias,
    gain_two,
    second_kernel,
    second_bias,
):
    tiles = lax.axis_size("tile")
    total_cols = W_DEV * tiles
    s = lax.axis_index("tm")
    k = lax.axis_index("tile")
    c = entry_kernel.shape[-1]
    t_ext, w_ext = FR_DEV + 2, W_DEV + 2

    lat = gather_latent(latent_tokens, total_cols)
    lat = jnp.pad(lat, ((0, 0), (1, 1), (0, 0))).astype(jnp.float32)

    frame_ok = (s * FR_DEV - 2 + jnp.arange(t_ext)) >= 0
    col_id = k * W_DEV - 1 + jnp.arange(w_ext)
    col_ok = (col_id >= 0) & (col_id < total_cols)
    ok = (frame_ok[:, None] & col_ok[None, :]).astype(jnp.float32).reshape(-1)
    second_act, entry_own = entry_conv_pallas(
        lat, entry_kernel, entry_bias, gain_one, ok, first_kernel, first_bias, gain_two
    )

    last, first = second_act[:, W_DEV - 1 :], second_act[:, :1]
    decoded = res_pallas(
        shift2(second_act, 1, 0), shift2(last, 1, 1), shift2(first, 1, -1),
        second_act, shift2(last, 0, 1), shift2(first, 0, -1),
        second_kernel, second_bias, entry_own,
    )
    return jnp.transpose(decoded, (0, 2, 1, 3))


def solution(mesh):
    in_specs = (P(("tm", "tile"), None), P(), P(), P(), P(), P(), P(), P(), P())
    out_specs = P("tm", None, "tile", None)
    return jax.shard_map(body, mesh=mesh, in_specs=in_specs, out_specs=out_specs, check_vma=False)
```

```python
import functools

import jax
import jax.numpy as jnp
from jax import lax
from jax.experimental import pallas as pl
from jax.experimental.pallas import tpu as pltpu
from jax.sharding import PartitionSpec as P

LAT = 16
FR_DEV = 2
H = 96
W_DEV = 4


def shift_from(value, axis, steps):
    count = lax.axis_size(axis)
    pairs = [(i, i + steps) for i in range(max(0, -steps), min(count, count - steps))]
    return lax.ppermute(value, axis, pairs)


def _norm_silu(v, gain):
    scaled = v * lax.rsqrt(jnp.mean(v * v, axis=-1, keepdims=True) + 1e-06) * gain
    return scaled / (1.0 + jnp.exp(-scaled))


def _conv_kernel(mode, x_ref, w_ref, b_ref, e_ref, o_ref, acc_ref, cols_ref):
    d = pl.program_id(0)
    t_out, w_out, rows, co = o_ref.shape
    c = x_ref.shape[-1]
    m = t_out * w_out * rows

    @pl.when(d == 0)
    def _():
        for dt in range(3):
            for dj in range(3):
                q = dt * 3 + dj
                cols_ref[:, :, :, q * c : (q + 1) * c] = x_ref[dt : dt + t_out, dj : dj + w_out]

    lhs = cols_ref[...].reshape(m, 9 * c)
    part = jnp.dot(lhs, w_ref[:, 0].reshape(9 * c, co), preferred_element_type=jnp.float32)
    row = lax.broadcasted_iota(jnp.int32, (t_out * w_out, rows, co), 1).reshape(m, co)

    @pl.when(d == 0)
    def _():
        acc_ref[...] = jnp.where(row == 0, 0.0, pltpu.roll(part, 1, 0))

    @pl.when(d == 1)
    def _():
        acc_ref[...] += part

    @pl.when(d == 2)
    def _():
        below = jnp.where(row == rows - 1, 0.0, pltpu.roll(part, m - 1, 0))
        total = acc_ref[...] + below + b_ref[...]
        if mode == "act":
            mid = total.astype(jnp.bfloat16).astype(jnp.float32)
            res = _norm_silu(mid, e_ref[...])
        else:
            res = e_ref[...].reshape(m, co).astype(jnp.float32) + total
        o_ref[...] = res.astype(o_ref.dtype).reshape(o_ref.shape)


def conv_pallas(mode, field, kernel, bias, extra):
    tp, wp, rows, c = field.shape
    co = kernel.shape[-1]
    t_out, w_out = tp - 2, wp - 2
    out_shape = (t_out, w_out, rows, co)
    if mode == "act":
        e_spec = pl.BlockSpec((1, co), lambda d: (0, 0))
    else:
        e_spec = pl.BlockSpec(out_shape, lambda d: (0, 0, 0, 0))
    flops = 2 * t_out * w_out * rows * 27 * c * co
    return pl.pallas_call(
        functools.partial(_conv_kernel, mode),
        grid=(3,),
        in_specs=[
            pl.BlockSpec((tp, wp, rows, c), lambda d: (0, 0, 0, 0)),
            pl.BlockSpec((3, 1, 3, c, co), lambda d: (0, d, 0, 0, 0)),
            pl.BlockSpec((1, co), lambda d: (0, 0)),
            e_spec,
        ],
        out_specs=pl.BlockSpec(out_shape, lambda d: (0, 0, 0, 0)),
        out_shape=jax.ShapeDtypeStruct(out_shape, jnp.bfloat16),
        scratch_shapes=[
            pltpu.VMEM((t_out * w_out * rows, co), jnp.float32),
            pltpu.VMEM((t_out, w_out, rows, 9 * c), jnp.bfloat16),
        ],
        compiler_params=pltpu.CompilerParams(
            dimension_semantics=("arbitrary",), vmem_limit_bytes=48 * 1024 * 1024
        ),
        cost_estimate=pl.CostEstimate(
            flops=flops,
            transcendentals=0,
            bytes_accessed=field.size * 2 + kernel.size * 2 + t_out * w_out * rows * co * 4,
        ),
    )(field, kernel, bias.reshape(1, co), extra)


def _entry_kernel(lat_ref, k_ref, b_ref, g_ref, ok_ref, act_ref, own_ref, band_ref, patch_ref):
    t_ext, w_ext, rows, c = act_ref.shape
    lanes = lat_ref.shape[-1]
    lat_ch = k_ref.shape[1]
    band_ref[...] = jnp.zeros(band_ref.shape, band_ref.dtype)
    for dt in range(3):
        for di in range(3):
            p = dt * 3 + di
            for dj in range(3):
                for j in range(w_ext):
                    r0 = p * lanes + (j + dj) * lat_ch
                    band_ref[r0 : r0 + lat_ch, j * c : (j + 1) * c] = k_ref[p * 3 + dj]
            slab = lat_ref[dt : dt + t_ext, di : di + rows, :].reshape(t_ext * rows, lanes)
            patch_ref[:, p * lanes : (p + 1) * lanes] = slab.astype(patch_ref.dtype)
    for j in range(w_ext):
        e = jnp.dot(
            patch_ref[...], band_ref[:, j * c : (j + 1) * c], preferred_element_type=jnp.float32
        )
        e = (e + b_ref[...]).astype(jnp.bfloat16)
        if 1 <= j <= w_ext - 2:
            own_ref[:, j - 1] = e.reshape(t_ext, rows, c)[t_ext - FR_DEV :]
        fa = _norm_silu(e.astype(jnp.float32), g_ref[...]).reshape(t_ext, rows, c)
        for t in range(t_ext):
            act_ref[t, j] = (fa[t] * ok_ref[t * w_ext + j]).astype(act_ref.dtype)


def entry_pallas(lat, entry_kernel, entry_bias, gain_one, ok):
    t_ext, w_ext = FR_DEV + 2, W_DEV + 2
    lanes = lat.shape[-1]
    c = entry_kernel.shape[-1]
    kr = entry_kernel.reshape(27, LAT, c)
    vmem = pl.BlockSpec(memory_space=pltpu.VMEM)
    return pl.pallas_call(
        _entry_kernel,
        in_specs=[vmem, vmem, vmem, vmem, pl.BlockSpec(memory_space=pltpu.SMEM)],
        out_specs=(vmem, vmem),
        out_shape=(
            jax.ShapeDtypeStruct((t_ext, w_ext, H, c), jnp.bfloat16),
            jax.ShapeDtypeStruct((FR_DEV, W_DEV, H, c), jnp.bfloat16),
        ),
        scratch_shapes=[
            pltpu.VMEM((9 * lanes, w_ext * c), jnp.bfloat16),
            pltpu.VMEM((t_ext * H, 9 * lanes), jnp.bfloat16),
        ],
        compiler_params=pltpu.CompilerParams(vmem_limit_bytes=48 * 1024 * 1024),
        cost_estimate=pl.CostEstimate(
            flops=2 * t_ext * H * 9 * lanes * w_ext * c,
            transcendentals=t_ext * w_ext * H * c,
            bytes_accessed=lat.size * 4 + kr.size * 2 + (t_ext * w_ext + FR_DEV * W_DEV) * H * c * 2,
        ),
    )(lat, kr, entry_bias.reshape(1, c), gain_one.reshape(1, c), ok)


def _entry_conv_kernel(
    lat_ref, ke_ref, be_ref, g1_ref, ok_ref, w_ref, b_ref, g2_ref,
    o_ref, own_ref, act_ref, band_ref, patch_ref, acc_ref, cols_ref,
):
    @pl.when(pl.program_id(0) == 0)
    def _():
        _entry_kernel(lat_ref, ke_ref, be_ref, g1_ref, ok_ref, act_ref, own_ref, band_ref, patch_ref)

    _conv_kernel("act", act_ref, w_ref, b_ref, g2_ref, o_ref, acc_ref, cols_ref)


def entry_conv_pallas(lat, entry_kernel, entry_bias, gain_one, ok, kernel, bias, gain_two):
    t_ext, w_ext = FR_DEV + 2, W_DEV + 2
    lanes = lat.shape[-1]
    c = entry_kernel.shape[-1]
    co = kernel.shape[-1]
    kr = entry_kernel.reshape(27, LAT, c)
    out_shape = (FR_DEV, W_DEV, H, co)
    m = FR_DEV * W_DEV * H
    const3 = lambda d: (0, 0, 0)
    row = pl.BlockSpec((1, c), lambda d: (0, 0))
    whole = pl.BlockSpec(out_shape, lambda d: (0, 0, 0, 0))
    flops = 2 * t_ext * H * 9 * lanes * w_ext * c + 2 * m * 27 * c * co
    return pl.pallas_call(
        _entry_conv_kernel,
        grid=(3,),
        in_specs=[
            pl.BlockSpec(lat.shape, const3),
            pl.BlockSpec(kr.shape, const3),
            row,
            row,
            pl.BlockSpec(memory_space=pltpu.SMEM),
            pl.BlockSpec((3, 1, 3, c, co), lambda d: (0, d, 0, 0, 0)),
            row,
            row,
        ],
        out_specs=(whole, whole),
        out_shape=(
            jax.ShapeDtypeStruct(out_shape, jnp.bfloat16),
            jax.ShapeDtypeStruct(out_shape, jnp.bfloat16),
        ),
        scratch_shapes=[
            pltpu.VMEM((t_ext, w_ext, H, c), jnp.bfloat16),
            pltpu.VMEM((9 * lanes, w_ext * c), jnp.bfloat16),
            pltpu.VMEM((t_ext * H, 9 * lanes), jnp.bfloat16),
            pltpu.VMEM((m, co), jnp.float32),
            pltpu.VMEM((FR_DEV, W_DEV, H, 9 * c), jnp.bfloat16),
        ],
        compiler_params=pltpu.CompilerParams(
            dimension_semantics=("arbitrary",), vmem_limit_bytes=48 * 1024 * 1024
        ),
        cost_estimate=pl.CostEstimate(
            flops=flops,
            transcendentals=t_ext * w_ext * H * c + m * co,
            bytes_accessed=lat.size * 4 + kr.size * 2 + kernel.size * 2 + 2 * m * co * 2,
        ),
    )(lat, kr, entry_bias.reshape(1, c), gain_one.reshape(1, c), ok, kernel,
      bias.reshape(1, co), gain_two.reshape(1, c))


def shift2(value, ds, dk):
    n_tm, n_tile = lax.axis_size("tm"), lax.axis_size("tile")
    pairs = []
    for s in range(n_tm):
        for k in range(n_tile):
            if 0 <= s + ds < n_tm and 0 <= k + dk < n_tile:
                pairs.append((s * n_tile + k, (s + ds) * n_tile + k + dk))
    return lax.ppermute(value, ("tm", "tile"), pairs)


def gather_latent(latent_tokens, total_cols):
    n_tm, n_tile = lax.axis_size("tm"), lax.axis_size("tile")
    s = lax.axis_index("tm")
    rows_per = FR_DEV * H // n_tile
    span = (W_DEV + 4) * LAT
    strip = latent_tokens.reshape(rows_per, total_cols * LAT)
    strip = jnp.pad(strip, ((0, 0), (2 * LAT, 2 * LAT)))
    windows = jnp.stack(
        [strip[:, t * W_DEV * LAT : t * W_DEV * LAT + span] for t in range(n_tile)], axis=0
    )
    lag = jnp.arange(n_tm) - s
    wanted = ((lag >= 0) & (lag <= 2)).astype(windows.dtype)
    chunks = windows[:, None] * wanted[None, :, None, None]
    chunks = chunks.reshape((n_tile * n_tm,) + windows.shape[1:])
    got = lax.all_to_all(chunks, ("tile", "tm"), 0, 0, tiled=True)
    got = got.reshape((n_tile, n_tm) + windows.shape[1:]).transpose(1, 0, 2, 3)
    got = jnp.pad(got, ((2, 0), (0, 0), (0, 0), (0, 0)))
    got = lax.dynamic_slice_in_dim(got, s, 3, axis=0)
    return got.reshape(3 * FR_DEV, H, span)


def body(
    latent_tokens,
    entry_kernel,
    entry_bias,
    gain_one,
    first_kernel,
    first_bias,
    gain_two,
    second_kernel,
    second_bias,
):
    tiles = lax.axis_size("tile")
    total_cols = W_DEV * tiles
    s = lax.axis_index("tm")
    k = lax.axis_index("tile")
    c = entry_kernel.shape[-1]
    t_ext, w_ext = FR_DEV + 2, W_DEV + 2

    lat = gather_latent(latent_tokens, total_cols)
    lat = jnp.pad(lat, ((0, 0), (1, 1), (0, 0))).astype(jnp.float32)

    frame_ok = (s * FR_DEV - 2 + jnp.arange(t_ext)) >= 0
    col_id = k * W_DEV - 1 + jnp.arange(w_ext)
    col_ok = (col_id >= 0) & (col_id < total_cols)
    ok = (frame_ok[:, None] & col_ok[None, :]).astype(jnp.float32).reshape(-1)
    second_act, entry_own = entry_conv_pallas(
        lat, entry_kernel, entry_bias, gain_one, ok, first_kernel, first_bias, gain_two
    )

    last, first = second_act[:, W_DEV - 1 :], second_act[:, :1]
    own_row = [shift2(last, 0, 1), second_act, shift2(first, 0, -1)]
    prev_row = [shift2(last, 1, 1), shift2(second_act, 1, 0), shift2(first, 1, -1)]
    ext2 = jnp.concatenate(
        [jnp.concatenate(prev_row, axis=1), jnp.concatenate(own_row, axis=1)], axis=0
    )

    decoded = conv_pallas("res", ext2, second_kernel, second_bias, entry_own)
    return jnp.transpose(decoded, (0, 2, 1, 3))


def solution(mesh):
    in_specs = (P(("tm", "tile"), None), P(), P(), P(), P(), P(), P(), P(), P())
    out_specs = P("tm", None, "tile", None)
    return jax.shard_map(body, mesh=mesh, in_specs=in_specs, out_specs=out_specs, check_vma=False)
```

```python
import functools

import jax
import jax.numpy as jnp
from jax import lax
from jax.experimental import pallas as pl
from jax.experimental.pallas import tpu as pltpu
from jax.sharding import PartitionSpec as P

LAT = 16
FR_DEV = 2
H = 96
W_DEV = 4


def shift_from(value, axis, steps):
    count = lax.axis_size(axis)
    pairs = [(i, i + steps) for i in range(max(0, -steps), min(count, count - steps))]
    return lax.ppermute(value, axis, pairs)


def _norm_silu(v, gain):
    scaled = v * lax.rsqrt(jnp.mean(v * v, axis=-1, keepdims=True) + 1e-06) * gain
    return scaled / (1.0 + jnp.exp(-scaled))


def _conv_kernel(mode, x_ref, w_ref, b_ref, e_ref, o_ref, acc_ref, cols_ref):
    d = pl.program_id(0)
    t_out, w_out, rows, co = o_ref.shape
    c = x_ref.shape[-1]
    m = t_out * w_out * rows

    @pl.when(d == 0)
    def _():
        for dt in range(3):
            for dj in range(3):
                q = dt * 3 + dj
                cols_ref[:, :, :, q * c : (q + 1) * c] = x_ref[dt : dt + t_out, dj : dj + w_out]

    lhs = cols_ref[...].reshape(m, 9 * c)
    part = jnp.dot(lhs, w_ref[:, 0].reshape(9 * c, co), preferred_element_type=jnp.float32)
    row = lax.broadcasted_iota(jnp.int32, (t_out * w_out, rows, co), 1).reshape(m, co)

    @pl.when(d == 0)
    def _():
        acc_ref[...] = jnp.where(row == 0, 0.0, pltpu.roll(part, 1, 0))

    @pl.when(d == 1)
    def _():
        acc_ref[...] += part

    @pl.when(d == 2)
    def _():
        below = jnp.where(row == rows - 1, 0.0, pltpu.roll(part, m - 1, 0))
        total = acc_ref[...] + below + b_ref[...]
        if mode == "act":
            mid = total.astype(jnp.bfloat16).astype(jnp.float32)
            res = _norm_silu(mid, e_ref[...])
        else:
            res = e_ref[...].reshape(m, co).astype(jnp.float32) + total
        o_ref[...] = res.astype(o_ref.dtype).reshape(o_ref.shape)


def conv_pallas(mode, field, kernel, bias, extra):
    tp, wp, rows, c = field.shape
    co = kernel.shape[-1]
    t_out, w_out = tp - 2, wp - 2
    out_shape = (t_out, w_out, rows, co)
    if mode == "act":
        e_spec = pl.BlockSpec((1, co), lambda d: (0, 0))
    else:
        e_spec = pl.BlockSpec(out_shape, lambda d: (0, 0, 0, 0))
    flops = 2 * t_out * w_out * rows * 27 * c * co
    return pl.pallas_call(
        functools.partial(_conv_kernel, mode),
        grid=(3,),
        in_specs=[
            pl.BlockSpec((tp, wp, rows, c), lambda d: (0, 0, 0, 0)),
            pl.BlockSpec((3, 1, 3, c, co), lambda d: (0, d, 0, 0, 0)),
            pl.BlockSpec((1, co), lambda d: (0, 0)),
            e_spec,
        ],
        out_specs=pl.BlockSpec(out_shape, lambda d: (0, 0, 0, 0)),
        out_shape=jax.ShapeDtypeStruct(out_shape, jnp.bfloat16),
        scratch_shapes=[
            pltpu.VMEM((t_out * w_out * rows, co), jnp.float32),
            pltpu.VMEM((t_out, w_out, rows, 9 * c), jnp.bfloat16),
        ],
        compiler_params=pltpu.CompilerParams(
            dimension_semantics=("arbitrary",), vmem_limit_bytes=48 * 1024 * 1024
        ),
        cost_estimate=pl.CostEstimate(
            flops=flops,
            transcendentals=0,
            bytes_accessed=field.size * 2 + kernel.size * 2 + t_out * w_out * rows * co * 4,
        ),
    )(field, kernel, bias.reshape(1, co), extra)


def _entry_kernel(lat_ref, k_ref, b_ref, g_ref, ok_ref, act_ref, own_ref, band_ref, patch_ref):
    t_ext, w_ext, rows, c = act_ref.shape
    lanes = lat_ref.shape[-1]
    lat_ch = k_ref.shape[1]
    band_ref[...] = jnp.zeros(band_ref.shape, band_ref.dtype)
    for dt in range(3):
        for di in range(3):
            p = dt * 3 + di
            for dj in range(3):
                for j in range(w_ext):
                    r0 = p * lanes + (j + dj) * lat_ch
                    band_ref[r0 : r0 + lat_ch, j * c : (j + 1) * c] = k_ref[p * 3 + dj]
            slab = lat_ref[dt : dt + t_ext, di : di + rows, :].reshape(t_ext * rows, lanes)
            patch_ref[:, p * lanes : (p + 1) * lanes] = slab.astype(patch_ref.dtype)
    for j in range(w_ext):
        e = jnp.dot(
            patch_ref[...], band_ref[:, j * c : (j + 1) * c], preferred_element_type=jnp.float32
        )
        e = (e + b_ref[...]).astype(jnp.bfloat16)
        if 1 <= j <= w_ext - 2:
            own_ref[:, j - 1] = e.reshape(t_ext, rows, c)[t_ext - FR_DEV :]
        fa = _norm_silu(e.astype(jnp.float32), g_ref[...]).reshape(t_ext, rows, c)
        for t in range(t_ext):
            act_ref[t, j] = (fa[t] * ok_ref[t * w_ext + j]).astype(act_ref.dtype)


def entry_pallas(lat, entry_kernel, entry_bias, gain_one, ok):
    t_ext, w_ext = FR_DEV + 2, W_DEV + 2
    lanes = lat.shape[-1]
    c = entry_kernel.shape[-1]
    kr = entry_kernel.reshape(27, LAT, c)
    vmem = pl.BlockSpec(memory_space=pltpu.VMEM)
    return pl.pallas_call(
        _entry_kernel,
        in_specs=[vmem, vmem, vmem, vmem, pl.BlockSpec(memory_space=pltpu.SMEM)],
        out_specs=(vmem, vmem),
        out_shape=(
            jax.ShapeDtypeStruct((t_ext, w_ext, H, c), jnp.bfloat16),
            jax.ShapeDtypeStruct((FR_DEV, W_DEV, H, c), jnp.bfloat16),
        ),
        scratch_shapes=[
            pltpu.VMEM((9 * lanes, w_ext * c), jnp.bfloat16),
            pltpu.VMEM((t_ext * H, 9 * lanes), jnp.bfloat16),
        ],
        compiler_params=pltpu.CompilerParams(vmem_limit_bytes=48 * 1024 * 1024),
        cost_estimate=pl.CostEstimate(
            flops=2 * t_ext * H * 9 * lanes * w_ext * c,
            transcendentals=t_ext * w_ext * H * c,
            bytes_accessed=lat.size * 4 + kr.size * 2 + (t_ext * w_ext + FR_DEV * W_DEV) * H * c * 2,
        ),
    )(lat, kr, entry_bias.reshape(1, c), gain_one.reshape(1, c), ok)


def _entry_conv_kernel(
    lat_ref, ke_ref, be_ref, g1_ref, ok_ref, w_ref, b_ref, g2_ref,
    o_ref, own_ref, act_ref, band_ref, patch_ref, acc_ref, cols_ref,
):
    @pl.when(pl.program_id(0) == 0)
    def _():
        _entry_kernel(lat_ref, ke_ref, be_ref, g1_ref, ok_ref, act_ref, own_ref, band_ref, patch_ref)

    _conv_kernel("act", act_ref, w_ref, b_ref, g2_ref, o_ref, acc_ref, cols_ref)


def entry_conv_pallas(lat, entry_kernel, entry_bias, gain_one, ok, kernel, bias, gain_two):
    t_ext, w_ext = FR_DEV + 2, W_DEV + 2
    lanes = lat.shape[-1]
    c = entry_kernel.shape[-1]
    co = kernel.shape[-1]
    kr = entry_kernel.reshape(27, LAT, c)
    out_shape = (FR_DEV, W_DEV, H, co)
    m = FR_DEV * W_DEV * H
    const3 = lambda d: (0, 0, 0)
    row = pl.BlockSpec((1, c), lambda d: (0, 0))
    whole = pl.BlockSpec(out_shape, lambda d: (0, 0, 0, 0))
    flops = 2 * t_ext * H * 9 * lanes * w_ext * c + 2 * m * 27 * c * co
    return pl.pallas_call(
        _entry_conv_kernel,
        grid=(3,),
        in_specs=[
            pl.BlockSpec(lat.shape, const3),
            pl.BlockSpec(kr.shape, const3),
            row,
            row,
            pl.BlockSpec(memory_space=pltpu.SMEM),
            pl.BlockSpec((3, 1, 3, c, co), lambda d: (0, d, 0, 0, 0)),
            row,
            row,
        ],
        out_specs=(whole, whole),
        out_shape=(
            jax.ShapeDtypeStruct(out_shape, jnp.bfloat16),
            jax.ShapeDtypeStruct(out_shape, jnp.bfloat16),
        ),
        scratch_shapes=[
            pltpu.VMEM((t_ext, w_ext, H, c), jnp.bfloat16),
            pltpu.VMEM((9 * lanes, w_ext * c), jnp.bfloat16),
            pltpu.VMEM((t_ext * H, 9 * lanes), jnp.bfloat16),
            pltpu.VMEM((m, co), jnp.float32),
            pltpu.VMEM((FR_DEV, W_DEV, H, 9 * c), jnp.bfloat16),
        ],
        compiler_params=pltpu.CompilerParams(
            dimension_semantics=("arbitrary",), vmem_limit_bytes=48 * 1024 * 1024
        ),
        cost_estimate=pl.CostEstimate(
            flops=flops,
            transcendentals=t_ext * w_ext * H * c + m * co,
            bytes_accessed=lat.size * 4 + kr.size * 2 + kernel.size * 2 + 2 * m * co * 2,
        ),
    )(lat, kr, entry_bias.reshape(1, c), gain_one.reshape(1, c), ok, kernel,
      bias.reshape(1, co), gain_two.reshape(1, c))


def shift2(value, ds, dk):
    n_tm, n_tile = lax.axis_size("tm"), lax.axis_size("tile")
    pairs = []
    for s in range(n_tm):
        for k in range(n_tile):
            if 0 <= s + ds < n_tm and 0 <= k + dk < n_tile:
                pairs.append((s * n_tile + k, (s + ds) * n_tile + k + dk))
    return lax.ppermute(value, ("tm", "tile"), pairs)


def gather_latent(latent_tokens, total_cols):
    n_tm, n_tile = lax.axis_size("tm"), lax.axis_size("tile")
    s = lax.axis_index("tm")
    rows_per = FR_DEV * H // n_tile
    span = (W_DEV + 4) * LAT
    strip = latent_tokens.reshape(rows_per, total_cols * LAT)
    strip = jnp.pad(strip, ((0, 0), (2 * LAT, 2 * LAT)))
    windows = jnp.stack(
        [strip[:, t * W_DEV * LAT : t * W_DEV * LAT + span] for t in range(n_tile)], axis=0
    )
    chunks = jnp.broadcast_to(windows[:, None], (n_tile, n_tm) + windows.shape[1:])
    chunks = chunks.reshape((n_tile * n_tm,) + windows.shape[1:])
    got = lax.all_to_all(chunks, ("tile", "tm"), 0, 0, tiled=True)
    got = got.reshape((n_tile, n_tm) + windows.shape[1:]).transpose(1, 0, 2, 3)
    got = jnp.pad(got, ((2, 0), (0, 0), (0, 0), (0, 0)))
    got = lax.dynamic_slice_in_dim(got, s, 3, axis=0)
    return got.reshape(3 * FR_DEV, H, span)


def body(
    latent_tokens,
    entry_kernel,
    entry_bias,
    gain_one,
    first_kernel,
    first_bias,
    gain_two,
    second_kernel,
    second_bias,
):
    tiles = lax.axis_size("tile")
    total_cols = W_DEV * tiles
    s = lax.axis_index("tm")
    k = lax.axis_index("tile")
    c = entry_kernel.shape[-1]
    t_ext, w_ext = FR_DEV + 2, W_DEV + 2

    lat = gather_latent(latent_tokens, total_cols)
    lat = jnp.pad(lat, ((0, 0), (1, 1), (0, 0))).astype(jnp.float32)

    frame_ok = (s * FR_DEV - 2 + jnp.arange(t_ext)) >= 0
    col_id = k * W_DEV - 1 + jnp.arange(w_ext)
    col_ok = (col_id >= 0) & (col_id < total_cols)
    ok = (frame_ok[:, None] & col_ok[None, :]).astype(jnp.float32).reshape(-1)
    second_act, entry_own = entry_conv_pallas(
        lat, entry_kernel, entry_bias, gain_one, ok, first_kernel, first_bias, gain_two
    )

    last, first = second_act[:, W_DEV - 1 :], second_act[:, :1]
    own_row = [shift2(last, 0, 1), second_act, shift2(first, 0, -1)]
    prev_row = [shift2(last, 1, 1), shift2(second_act, 1, 0), shift2(first, 1, -1)]
    ext2 = jnp.concatenate(
        [jnp.concatenate(prev_row, axis=1), jnp.concatenate(own_row, axis=1)], axis=0
    )

    decoded = conv_pallas("res", ext2, second_kernel, second_bias, entry_own)
    return jnp.transpose(decoded, (0, 2, 1, 3))


def solution(mesh):
    in_specs = (P(("tm", "tile"), None), P(), P(), P(), P(), P(), P(), P(), P())
    out_specs = P("tm", None, "tile", None)
    return jax.shard_map(body, mesh=mesh, in_specs=in_specs, out_specs=out_specs, check_vma=False)
```

```python
import functools

import jax
import jax.numpy as jnp
from jax import lax
from jax.experimental import pallas as pl
from jax.experimental.pallas import tpu as pltpu
from jax.sharding import PartitionSpec as P

LAT = 16
FR_DEV = 2
H = 96
W_DEV = 4


def shift_from(value, axis, steps):
    count = lax.axis_size(axis)
    pairs = [(i, i + steps) for i in range(max(0, -steps), min(count, count - steps))]
    return lax.ppermute(value, axis, pairs)


def _norm_silu(v, gain):
    scaled = v * lax.rsqrt(jnp.mean(v * v, axis=-1, keepdims=True) + 1e-06) * gain
    return scaled / (1.0 + jnp.exp(-scaled))


def _conv_body(mode, x_ref, w_hbm, b_ref, e_ref, o_ref, acc_ref, cols_ref, wbuf, sems, before=None):
    t_out, w_out, rows, co = o_ref.shape
    c = x_ref.shape[-1]
    m = t_out * w_out * rows
    copies = [pltpu.make_async_copy(w_hbm.at[:, di], wbuf.at[di], sems.at[di]) for di in range(3)]
    for cp in copies:
        cp.start()
    if before is not None:
        before()
    for dt in range(3):
        for dj in range(3):
            q = dt * 3 + dj
            cols_ref[:, :, :, q * c : (q + 1) * c] = x_ref[dt : dt + t_out, dj : dj + w_out]
    row = lax.broadcasted_iota(jnp.int32, (t_out * w_out, rows, co), 1).reshape(m, co)
    for di in range(3):
        copies[di].wait()
        lhs = cols_ref[...].reshape(m, 9 * c)
        part = jnp.dot(lhs, wbuf[di].reshape(9 * c, co), preferred_element_type=jnp.float32)
        if di == 0:
            acc_ref[...] = jnp.where(row == 0, 0.0, pltpu.roll(part, 1, 0))
        elif di == 1:
            acc_ref[...] += part
        else:
            below = jnp.where(row == rows - 1, 0.0, pltpu.roll(part, m - 1, 0))
            total = acc_ref[...] + below + b_ref[...]
            if mode == "act":
                mid = total.astype(jnp.bfloat16).astype(jnp.float32)
                res = _norm_silu(mid, e_ref[...])
            else:
                res = e_ref[...].reshape(m, co).astype(jnp.float32) + total
            o_ref[...] = res.astype(o_ref.dtype).reshape(o_ref.shape)


def conv_pallas(mode, field, kernel, bias, extra):
    tp, wp, rows, c = field.shape
    co = kernel.shape[-1]
    t_out, w_out = tp - 2, wp - 2
    out_shape = (t_out, w_out, rows, co)
    vmem = pl.BlockSpec(memory_space=pltpu.VMEM)
    flops = 2 * t_out * w_out * rows * 27 * c * co
    return pl.pallas_call(
        functools.partial(_conv_body, mode),
        in_specs=[vmem, pl.BlockSpec(memory_space=pl.ANY), vmem, vmem],
        out_specs=vmem,
        out_shape=jax.ShapeDtypeStruct(out_shape, jnp.bfloat16),
        scratch_shapes=[
            pltpu.VMEM((t_out * w_out * rows, co), jnp.float32),
            pltpu.VMEM((t_out, w_out, rows, 9 * c), jnp.bfloat16),
            pltpu.VMEM(kernel.shape, kernel.dtype),
            pltpu.SemaphoreType.DMA((3,)),
        ],
        compiler_params=pltpu.CompilerParams(vmem_limit_bytes=48 * 1024 * 1024),
        cost_estimate=pl.CostEstimate(
            flops=flops,
            transcendentals=0,
            bytes_accessed=field.size * 2 + kernel.size * 2 + t_out * w_out * rows * co * 4,
        ),
    )(field, kernel, bias.reshape(1, co), extra)


def _entry_kernel(lat_ref, k_ref, b_ref, g_ref, ok_ref, act_ref, own_ref, band_ref, patch_ref):
    t_ext, w_ext, rows, c = act_ref.shape
    lanes = lat_ref.shape[-1]
    lat_ch = k_ref.shape[1]
    band_ref[...] = jnp.zeros(band_ref.shape, band_ref.dtype)
    for dt in range(3):
        for di in range(3):
            p = dt * 3 + di
            for dj in range(3):
                for j in range(w_ext):
                    r0 = p * lanes + (j + dj) * lat_ch
                    band_ref[r0 : r0 + lat_ch, j * c : (j + 1) * c] = k_ref[p * 3 + dj]
            slab = lat_ref[dt : dt + t_ext, di : di + rows, :].reshape(t_ext * rows, lanes)
            patch_ref[:, p * lanes : (p + 1) * lanes] = slab.astype(patch_ref.dtype)
    for j in range(w_ext):
        e = jnp.dot(
            patch_ref[...], band_ref[:, j * c : (j + 1) * c], preferred_element_type=jnp.float32
        )
        e = (e + b_ref[...]).astype(jnp.bfloat16)
        if 1 <= j <= w_ext - 2:
            own_ref[:, j - 1] = e.reshape(t_ext, rows, c)[t_ext - FR_DEV :]
        fa = _norm_silu(e.astype(jnp.float32), g_ref[...]).reshape(t_ext, rows, c)
        for t in range(t_ext):
            act_ref[t, j] = (fa[t] * ok_ref[t * w_ext + j]).astype(act_ref.dtype)


def entry_pallas(lat, entry_kernel, entry_bias, gain_one, ok):
    t_ext, w_ext = FR_DEV + 2, W_DEV + 2
    lanes = lat.shape[-1]
    c = entry_kernel.shape[-1]
    kr = entry_kernel.reshape(27, LAT, c)
    vmem = pl.BlockSpec(memory_space=pltpu.VMEM)
    return pl.pallas_call(
        _entry_kernel,
        in_specs=[vmem, vmem, vmem, vmem, pl.BlockSpec(memory_space=pltpu.SMEM)],
        out_specs=(vmem, vmem),
        out_shape=(
            jax.ShapeDtypeStruct((t_ext, w_ext, H, c), jnp.bfloat16),
            jax.ShapeDtypeStruct((FR_DEV, W_DEV, H, c), jnp.bfloat16),
        ),
        scratch_shapes=[
            pltpu.VMEM((9 * lanes, w_ext * c), jnp.bfloat16),
            pltpu.VMEM((t_ext * H, 9 * lanes), jnp.bfloat16),
        ],
        compiler_params=pltpu.CompilerParams(vmem_limit_bytes=48 * 1024 * 1024),
        cost_estimate=pl.CostEstimate(
            flops=2 * t_ext * H * 9 * lanes * w_ext * c,
            transcendentals=t_ext * w_ext * H * c,
            bytes_accessed=lat.size * 4 + kr.size * 2 + (t_ext * w_ext + FR_DEV * W_DEV) * H * c * 2,
        ),
    )(lat, kr, entry_bias.reshape(1, c), gain_one.reshape(1, c), ok)


def _entry_conv_kernel(
    lat_ref, ke_ref, be_ref, g1_ref, ok_ref, w_hbm, b_ref, g2_ref,
    o_ref, own_ref, act_ref, band_ref, patch_ref, acc_ref, cols_ref, wbuf, sems,
):
    def entry():
        _entry_kernel(lat_ref, ke_ref, be_ref, g1_ref, ok_ref, act_ref, own_ref, band_ref, patch_ref)

    _conv_body("act", act_ref, w_hbm, b_ref, g2_ref, o_ref, acc_ref, cols_ref, wbuf, sems, entry)


def entry_conv_pallas(lat, entry_kernel, entry_bias, gain_one, ok, kernel, bias, gain_two):
    t_ext, w_ext = FR_DEV + 2, W_DEV + 2
    lanes = lat.shape[-1]
    c = entry_kernel.shape[-1]
    co = kernel.shape[-1]
    kr = entry_kernel.reshape(27, LAT, c)
    out_shape = (FR_DEV, W_DEV, H, co)
    m = FR_DEV * W_DEV * H
    vmem = pl.BlockSpec(memory_space=pltpu.VMEM)
    flops = 2 * t_ext * H * 9 * lanes * w_ext * c + 2 * m * 27 * c * co
    return pl.pallas_call(
        _entry_conv_kernel,
        in_specs=[
            vmem, vmem, vmem, vmem, pl.BlockSpec(memory_space=pltpu.SMEM),
            pl.BlockSpec(memory_space=pl.ANY), vmem, vmem,
        ],
        out_specs=(vmem, vmem),
        out_shape=(
            jax.ShapeDtypeStruct(out_shape, jnp.bfloat16),
            jax.ShapeDtypeStruct(out_shape, jnp.bfloat16),
        ),
        scratch_shapes=[
            pltpu.VMEM((t_ext, w_ext, H, c), jnp.bfloat16),
            pltpu.VMEM((9 * lanes, w_ext * c), jnp.bfloat16),
            pltpu.VMEM((t_ext * H, 9 * lanes), jnp.bfloat16),
            pltpu.VMEM((m, co), jnp.float32),
            pltpu.VMEM((FR_DEV, W_DEV, H, 9 * c), jnp.bfloat16),
            pltpu.VMEM(kernel.shape, kernel.dtype),
            pltpu.SemaphoreType.DMA((3,)),
        ],
        compiler_params=pltpu.CompilerParams(vmem_limit_bytes=48 * 1024 * 1024),
        cost_estimate=pl.CostEstimate(
            flops=flops,
            transcendentals=t_ext * w_ext * H * c + m * co,
            bytes_accessed=lat.size * 4 + kr.size * 2 + kernel.size * 2 + 2 * m * co * 2,
        ),
    )(lat, kr, entry_bias.reshape(1, c), gain_one.reshape(1, c), ok, kernel,
      bias.reshape(1, co), gain_two.reshape(1, c))


def shift2(value, ds, dk):
    n_tm, n_tile = lax.axis_size("tm"), lax.axis_size("tile")
    pairs = []
    for s in range(n_tm):
        for k in range(n_tile):
            if 0 <= s + ds < n_tm and 0 <= k + dk < n_tile:
                pairs.append((s * n_tile + k, (s + ds) * n_tile + k + dk))
    return lax.ppermute(value, ("tm", "tile"), pairs)


def gather_latent(latent_tokens, total_cols):
    n_tm, n_tile = lax.axis_size("tm"), lax.axis_size("tile")
    s = lax.axis_index("tm")
    rows_per = FR_DEV * H // n_tile
    span = (W_DEV + 4) * LAT
    strip = latent_tokens.reshape(rows_per, total_cols * LAT)
    strip = jnp.pad(strip, ((0, 0), (2 * LAT, 2 * LAT)))
    windows = jnp.stack(
        [strip[:, t * W_DEV * LAT : t * W_DEV * LAT + span] for t in range(n_tile)], axis=0
    )
    chunks = jnp.broadcast_to(windows[:, None], (n_tile, n_tm) + windows.shape[1:])
    chunks = chunks.reshape((n_tile * n_tm,) + windows.shape[1:])
    got = lax.all_to_all(chunks, ("tile", "tm"), 0, 0, tiled=True)
    got = got.reshape((n_tile, n_tm) + windows.shape[1:]).transpose(1, 0, 2, 3)
    got = jnp.pad(got, ((2, 0), (0, 0), (0, 0), (0, 0)))
    got = lax.dynamic_slice_in_dim(got, s, 3, axis=0)
    return got.reshape(3 * FR_DEV, H, span)


def body(
    latent_tokens,
    entry_kernel,
    entry_bias,
    gain_one,
    first_kernel,
    first_bias,
    gain_two,
    second_kernel,
    second_bias,
):
    tiles = lax.axis_size("tile")
    total_cols = W_DEV * tiles
    s = lax.axis_index("tm")
    k = lax.axis_index("tile")
    c = entry_kernel.shape[-1]
    t_ext, w_ext = FR_DEV + 2, W_DEV + 2

    lat = gather_latent(latent_tokens, total_cols)
    lat = jnp.pad(lat, ((0, 0), (1, 1), (0, 0))).astype(jnp.float32)

    frame_ok = (s * FR_DEV - 2 + jnp.arange(t_ext)) >= 0
    col_id = k * W_DEV - 1 + jnp.arange(w_ext)
    col_ok = (col_id >= 0) & (col_id < total_cols)
    ok = (frame_ok[:, None] & col_ok[None, :]).astype(jnp.float32).reshape(-1)
    second_act, entry_own = entry_conv_pallas(
        lat, entry_kernel, entry_bias, gain_one, ok, first_kernel, first_bias, gain_two
    )

    last, first = second_act[:, W_DEV - 1 :], second_act[:, :1]
    own_row = [shift2(last, 0, 1), second_act, shift2(first, 0, -1)]
    prev_row = [shift2(last, 1, 1), shift2(second_act, 1, 0), shift2(first, 1, -1)]
    ext2 = jnp.concatenate(
        [jnp.concatenate(prev_row, axis=1), jnp.concatenate(own_row, axis=1)], axis=0
    )

    decoded = conv_pallas("res", ext2, second_kernel, second_bias, entry_own)
    return jnp.transpose(decoded, (0, 2, 1, 3))


def solution(mesh):
    in_specs = (P(("tm", "tile"), None), P(), P(), P(), P(), P(), P(), P(), P())
    out_specs = P("tm", None, "tile", None)
    return jax.shard_map(body, mesh=mesh, in_specs=in_specs, out_specs=out_specs, check_vma=False)
```

```python
import functools

import jax
import jax.numpy as jnp
from jax import lax
from jax.experimental import pallas as pl
from jax.experimental.pallas import tpu as pltpu
from jax.sharding import PartitionSpec as P

LAT = 16
FR_DEV = 2
H = 96
W_DEV = 4


def shift_from(value, axis, steps):
    count = lax.axis_size(axis)
    pairs = [(i, i + steps) for i in range(max(0, -steps), min(count, count - steps))]
    return lax.ppermute(value, axis, pairs)


def _norm_silu(v, gain):
    scaled = v * lax.rsqrt(jnp.mean(v * v, axis=-1, keepdims=True) + 1e-06) * gain
    return scaled / (1.0 + jnp.exp(-scaled))


def _conv_body(mode, x_ref, w_hbm, b_ref, e_ref, o_ref, acc_ref, cols_ref, wbuf, sems, before=None):
    t_out, w_out, rows, co = o_ref.shape
    c = x_ref.shape[-1]
    m = t_out * w_out * rows
    copies = [pltpu.make_async_copy(w_hbm.at[:, di], wbuf.at[di], sems.at[di]) for di in range(3)]
    for cp in copies:
        cp.start()
    if mode == "res":
        e_hbm, e_ref = e_ref
        e_copy = pltpu.make_async_copy(e_hbm, e_ref, sems.at[3])
        e_copy.start()
    if before is not None:
        before()
    for dt in range(3):
        for dj in range(3):
            q = dt * 3 + dj
            cols_ref[:, :, :, q * c : (q + 1) * c] = x_ref[dt : dt + t_out, dj : dj + w_out]
    row = lax.broadcasted_iota(jnp.int32, (t_out * w_out, rows, co), 1).reshape(m, co)
    for di in range(3):
        copies[di].wait()
        lhs = cols_ref[...].reshape(m, 9 * c)
        part = jnp.dot(lhs, wbuf[di].reshape(9 * c, co), preferred_element_type=jnp.float32)
        if di == 0:
            acc_ref[...] = jnp.where(row == 0, 0.0, pltpu.roll(part, 1, 0))
        elif di == 1:
            acc_ref[...] += part
        else:
            below = jnp.where(row == rows - 1, 0.0, pltpu.roll(part, m - 1, 0))
            total = acc_ref[...] + below + b_ref[...]
            if mode == "act":
                mid = total.astype(jnp.bfloat16).astype(jnp.float32)
                res = _norm_silu(mid, e_ref[...])
            else:
                e_copy.wait()
                res = e_ref[...].reshape(m, co).astype(jnp.float32) + total
            o_ref[...] = res.astype(o_ref.dtype).reshape(o_ref.shape)


def conv_pallas(mode, field, kernel, bias, extra):
    tp, wp, rows, c = field.shape
    co = kernel.shape[-1]
    t_out, w_out = tp - 2, wp - 2
    out_shape = (t_out, w_out, rows, co)
    vmem = pl.BlockSpec(memory_space=pltpu.VMEM)
    flops = 2 * t_out * w_out * rows * 27 * c * co
    anyspace = pl.BlockSpec(memory_space=pl.ANY)

    def run(x_ref, w_hbm, b_ref, e_hbm, o_ref, acc_ref, cols_ref, wbuf, sems, e_ref):
        _conv_body("res", x_ref, w_hbm, b_ref, (e_hbm, e_ref), o_ref, acc_ref, cols_ref, wbuf, sems)

    assert mode == "res"
    return pl.pallas_call(
        run,
        in_specs=[vmem, anyspace, vmem, anyspace],
        out_specs=vmem,
        out_shape=jax.ShapeDtypeStruct(out_shape, jnp.bfloat16),
        scratch_shapes=[
            pltpu.VMEM((t_out * w_out * rows, co), jnp.float32),
            pltpu.VMEM((t_out, w_out, rows, 9 * c), jnp.bfloat16),
            pltpu.VMEM(kernel.shape, kernel.dtype),
            pltpu.SemaphoreType.DMA((4,)),
            pltpu.VMEM(out_shape, extra.dtype),
        ],
        compiler_params=pltpu.CompilerParams(vmem_limit_bytes=48 * 1024 * 1024),
        cost_estimate=pl.CostEstimate(
            flops=flops,
            transcendentals=0,
            bytes_accessed=field.size * 2 + kernel.size * 2 + t_out * w_out * rows * co * 4,
        ),
    )(field, kernel, bias.reshape(1, co), extra)


def _entry_kernel(lat_ref, k_ref, b_ref, g_ref, ok_ref, act_ref, own_ref, band_ref, patch_ref):
    t_ext, w_ext, rows, c = act_ref.shape
    lanes = lat_ref.shape[-1]
    lat_ch = k_ref.shape[1]
    zero = jnp.zeros((lat_ch, c), band_ref.dtype)
    for dt in range(3):
        for di in range(3):
            p = dt * 3 + di
            for j in range(w_ext):
                for jj in range(lanes // lat_ch):
                    r0 = p * lanes + jj * lat_ch
                    dj = jj - j
                    blk = k_ref[p * 3 + dj] if 0 <= dj <= 2 else zero
                    band_ref[r0 : r0 + lat_ch, j * c : (j + 1) * c] = blk
            slab = lat_ref[dt : dt + t_ext, di : di + rows, :].reshape(t_ext * rows, lanes)
            patch_ref[:, p * lanes : (p + 1) * lanes] = slab.astype(patch_ref.dtype)
    for j in range(w_ext):
        e = jnp.dot(
            patch_ref[...], band_ref[:, j * c : (j + 1) * c], preferred_element_type=jnp.float32
        )
        e = (e + b_ref[...]).astype(jnp.bfloat16)
        if 1 <= j <= w_ext - 2:
            own_ref[:, j - 1] = e.reshape(t_ext, rows, c)[t_ext - FR_DEV :]
        fa = _norm_silu(e.astype(jnp.float32), g_ref[...]).reshape(t_ext, rows, c)
        for t in range(t_ext):
            act_ref[t, j] = (fa[t] * ok_ref[t * w_ext + j]).astype(act_ref.dtype)


def entry_pallas(lat, entry_kernel, entry_bias, gain_one, ok):
    t_ext, w_ext = FR_DEV + 2, W_DEV + 2
    lanes = lat.shape[-1]
    c = entry_kernel.shape[-1]
    kr = entry_kernel.reshape(27, LAT, c)
    vmem = pl.BlockSpec(memory_space=pltpu.VMEM)
    return pl.pallas_call(
        _entry_kernel,
        in_specs=[vmem, vmem, vmem, vmem, pl.BlockSpec(memory_space=pltpu.SMEM)],
        out_specs=(vmem, vmem),
        out_shape=(
            jax.ShapeDtypeStruct((t_ext, w_ext, H, c), jnp.bfloat16),
            jax.ShapeDtypeStruct((FR_DEV, W_DEV, H, c), jnp.bfloat16),
        ),
        scratch_shapes=[
            pltpu.VMEM((9 * lanes, w_ext * c), jnp.bfloat16),
            pltpu.VMEM((t_ext * H, 9 * lanes), jnp.bfloat16),
        ],
        compiler_params=pltpu.CompilerParams(vmem_limit_bytes=48 * 1024 * 1024),
        cost_estimate=pl.CostEstimate(
            flops=2 * t_ext * H * 9 * lanes * w_ext * c,
            transcendentals=t_ext * w_ext * H * c,
            bytes_accessed=lat.size * 4 + kr.size * 2 + (t_ext * w_ext + FR_DEV * W_DEV) * H * c * 2,
        ),
    )(lat, kr, entry_bias.reshape(1, c), gain_one.reshape(1, c), ok)


def _entry_conv_kernel(
    lat_ref, ke_ref, be_ref, g1_ref, ok_ref, w_hbm, b_ref, g2_ref,
    o_ref, own_ref, act_ref, band_ref, patch_ref, acc_ref, cols_ref, wbuf, sems,
):
    def entry():
        _entry_kernel(lat_ref, ke_ref, be_ref, g1_ref, ok_ref, act_ref, own_ref, band_ref, patch_ref)

    _conv_body("act", act_ref, w_hbm, b_ref, g2_ref, o_ref, acc_ref, cols_ref, wbuf, sems, entry)


def entry_conv_pallas(lat, entry_kernel, entry_bias, gain_one, ok, kernel, bias, gain_two):
    t_ext, w_ext = FR_DEV + 2, W_DEV + 2
    lanes = lat.shape[-1]
    c = entry_kernel.shape[-1]
    co = kernel.shape[-1]
    kr = entry_kernel.reshape(27, LAT, c)
    out_shape = (FR_DEV, W_DEV, H, co)
    m = FR_DEV * W_DEV * H
    vmem = pl.BlockSpec(memory_space=pltpu.VMEM)
    flops = 2 * t_ext * H * 9 * lanes * w_ext * c + 2 * m * 27 * c * co
    return pl.pallas_call(
        _entry_conv_kernel,
        in_specs=[
            vmem, vmem, vmem, vmem, pl.BlockSpec(memory_space=pltpu.SMEM),
            pl.BlockSpec(memory_space=pl.ANY), vmem, vmem,
        ],
        out_specs=(vmem, vmem),
        out_shape=(
            jax.ShapeDtypeStruct(out_shape, jnp.bfloat16),
            jax.ShapeDtypeStruct(out_shape, jnp.bfloat16),
        ),
        scratch_shapes=[
            pltpu.VMEM((t_ext, w_ext, H, c), jnp.bfloat16),
            pltpu.VMEM((9 * lanes, w_ext * c), jnp.bfloat16),
            pltpu.VMEM((t_ext * H, 9 * lanes), jnp.bfloat16),
            pltpu.VMEM((m, co), jnp.float32),
            pltpu.VMEM((FR_DEV, W_DEV, H, 9 * c), jnp.bfloat16),
            pltpu.VMEM(kernel.shape, kernel.dtype),
            pltpu.SemaphoreType.DMA((4,)),
        ],
        compiler_params=pltpu.CompilerParams(vmem_limit_bytes=48 * 1024 * 1024),
        cost_estimate=pl.CostEstimate(
            flops=flops,
            transcendentals=t_ext * w_ext * H * c + m * co,
            bytes_accessed=lat.size * 4 + kr.size * 2 + kernel.size * 2 + 2 * m * co * 2,
        ),
    )(lat, kr, entry_bias.reshape(1, c), gain_one.reshape(1, c), ok, kernel,
      bias.reshape(1, co), gain_two.reshape(1, c))


def shift2(value, ds, dk):
    n_tm, n_tile = lax.axis_size("tm"), lax.axis_size("tile")
    pairs = []
    for s in range(n_tm):
        for k in range(n_tile):
            if 0 <= s + ds < n_tm and 0 <= k + dk < n_tile:
                pairs.append((s * n_tile + k, (s + ds) * n_tile + k + dk))
    return lax.ppermute(value, ("tm", "tile"), pairs)


def gather_latent(latent_tokens, total_cols):
    n_tm, n_tile = lax.axis_size("tm"), lax.axis_size("tile")
    s = lax.axis_index("tm")
    rows_per = FR_DEV * H // n_tile
    span = (W_DEV + 4) * LAT
    strip = latent_tokens.reshape(rows_per, total_cols * LAT)
    strip = jnp.pad(strip, ((0, 0), (2 * LAT, 2 * LAT)))
    windows = jnp.stack(
        [strip[:, t * W_DEV * LAT : t * W_DEV * LAT + span] for t in range(n_tile)], axis=0
    )
    chunks = jnp.broadcast_to(windows[:, None], (n_tile, n_tm) + windows.shape[1:])
    chunks = chunks.reshape((n_tile * n_tm,) + windows.shape[1:])
    got = lax.all_to_all(chunks, ("tile", "tm"), 0, 0, tiled=True)
    got = got.reshape((n_tile, n_tm) + windows.shape[1:]).transpose(1, 0, 2, 3)
    got = jnp.pad(got, ((2, 0), (0, 0), (0, 0), (0, 0)))
    got = lax.dynamic_slice_in_dim(got, s, 3, axis=0)
    return got.reshape(3 * FR_DEV, H, span)


def body(
    latent_tokens,
    entry_kernel,
    entry_bias,
    gain_one,
    first_kernel,
    first_bias,
    gain_two,
    second_kernel,
    second_bias,
):
    tiles = lax.axis_size("tile")
    total_cols = W_DEV * tiles
    s = lax.axis_index("tm")
    k = lax.axis_index("tile")
    c = entry_kernel.shape[-1]
    t_ext, w_ext = FR_DEV + 2, W_DEV + 2

    lat = gather_latent(latent_tokens, total_cols)
    lat = jnp.pad(lat, ((0, 0), (1, 1), (0, 0))).astype(jnp.float32)

    frame_ok = (s * FR_DEV - 2 + jnp.arange(t_ext)) >= 0
    col_id = k * W_DEV - 1 + jnp.arange(w_ext)
    col_ok = (col_id >= 0) & (col_id < total_cols)
    ok = (frame_ok[:, None] & col_ok[None, :]).astype(jnp.float32).reshape(-1)
    second_act, entry_own = entry_conv_pallas(
        lat, entry_kernel, entry_bias, gain_one, ok, first_kernel, first_bias, gain_two
    )

    last, first = second_act[:, W_DEV - 1 :], second_act[:, :1]
    own_row = [shift2(last, 0, 1), second_act, shift2(first, 0, -1)]
    prev_row = [shift2(last, 1, 1), shift2(second_act, 1, 0), shift2(first, 1, -1)]
    ext2 = jnp.concatenate(
        [jnp.concatenate(prev_row, axis=1), jnp.concatenate(own_row, axis=1)], axis=0
    )

    decoded = conv_pallas("res", ext2, second_kernel, second_bias, entry_own)
    return jnp.transpose(decoded, (0, 2, 1, 3))


def solution(mesh):
    in_specs = (P(("tm", "tile"), None), P(), P(), P(), P(), P(), P(), P(), P())
    out_specs = P("tm", None, "tile", None)
    return jax.shard_map(body, mesh=mesh, in_specs=in_specs, out_specs=out_specs, check_vma=False)
```

```python
import functools

import jax
import jax.numpy as jnp
from jax import lax
from jax.experimental import pallas as pl
from jax.experimental.pallas import tpu as pltpu
from jax.sharding import PartitionSpec as P

LAT = 16
FR_DEV = 2
H = 96
W_DEV = 4


def shift_from(value, axis, steps):
    count = lax.axis_size(axis)
    pairs = [(i, i + steps) for i in range(max(0, -steps), min(count, count - steps))]
    return lax.ppermute(value, axis, pairs)


def _norm_silu(v, gain):
    scaled = v * lax.rsqrt(jnp.mean(v * v, axis=-1, keepdims=True) + 1e-06) * gain
    return scaled / (1.0 + jnp.exp(-scaled))


def _conv_body(mode, x_ref, w_hbm, b_ref, e_ref, o_ref, acc_ref, cols_ref, wbuf, sems, before=None):
    t_out, w_out, rows, co = o_ref.shape
    c = x_ref.shape[-1]
    m = t_out * w_out * rows
    copies = [pltpu.make_async_copy(w_hbm.at[:, di], wbuf.at[di], sems.at[di]) for di in range(3)]
    for cp in copies:
        cp.start()
    if mode == "res":
        e_hbm, e_ref = e_ref
        e_copy = pltpu.make_async_copy(e_hbm, e_ref, sems.at[3])
        e_copy.start()
    if before is not None:
        before()
    for dt in range(3):
        for dj in range(3):
            q = dt * 3 + dj
            cols_ref[:, :, :, q * c : (q + 1) * c] = x_ref[dt : dt + t_out, dj : dj + w_out]
    row = lax.broadcasted_iota(jnp.int32, (t_out * w_out, rows, co), 1).reshape(m, co)
    for di in range(3):
        copies[di].wait()
        lhs = cols_ref[...].reshape(m, 9 * c)
        part = jnp.dot(lhs, wbuf[di].reshape(9 * c, co), preferred_element_type=jnp.float32)
        if di == 0:
            acc_ref[...] = jnp.where(row == 0, 0.0, pltpu.roll(part, 1, 0))
        elif di == 1:
            acc_ref[...] += part
        else:
            below = jnp.where(row == rows - 1, 0.0, pltpu.roll(part, m - 1, 0))
            total = acc_ref[...] + below + b_ref[...]
            if mode == "act":
                mid = total.astype(jnp.bfloat16).astype(jnp.float32)
                res = _norm_silu(mid, e_ref[...])
            else:
                e_copy.wait()
                res = e_ref[...].reshape(m, co).astype(jnp.float32) + total
            o_ref[...] = res.astype(o_ref.dtype).reshape(o_ref.shape)


def conv_pallas(mode, field, kernel, bias, extra):
    tp, wp, rows, c = field.shape
    co = kernel.shape[-1]
    t_out, w_out = tp - 2, wp - 2
    out_shape = (t_out, w_out, rows, co)
    vmem = pl.BlockSpec(memory_space=pltpu.VMEM)
    flops = 2 * t_out * w_out * rows * 27 * c * co
    anyspace = pl.BlockSpec(memory_space=pl.ANY)

    def run(x_ref, w_hbm, b_ref, e_hbm, o_ref, acc_ref, cols_ref, wbuf, sems, e_ref):
        _conv_body("res", x_ref, w_hbm, b_ref, (e_hbm, e_ref), o_ref, acc_ref, cols_ref, wbuf, sems)

    assert mode == "res"
    return pl.pallas_call(
        run,
        in_specs=[vmem, anyspace, vmem, anyspace],
        out_specs=vmem,
        out_shape=jax.ShapeDtypeStruct(out_shape, jnp.bfloat16),
        scratch_shapes=[
            pltpu.VMEM((t_out * w_out * rows, co), jnp.float32),
            pltpu.VMEM((t_out, w_out, rows, 9 * c), jnp.bfloat16),
            pltpu.VMEM(kernel.shape, kernel.dtype),
            pltpu.SemaphoreType.DMA((4,)),
            pltpu.VMEM(out_shape, extra.dtype),
        ],
        compiler_params=pltpu.CompilerParams(vmem_limit_bytes=48 * 1024 * 1024),
        cost_estimate=pl.CostEstimate(
            flops=flops,
            transcendentals=0,
            bytes_accessed=field.size * 2 + kernel.size * 2 + t_out * w_out * rows * co * 4,
        ),
    )(field, kernel, bias.reshape(1, co), extra)


def _entry_kernel(lat_ref, k_ref, b_ref, g_ref, ok_ref, act_ref, own_ref, band_ref, patch_ref):
    t_ext, w_ext, rows, c = act_ref.shape
    lanes = lat_ref.shape[-1]
    lat_ch = k_ref.shape[1]
    zero = jnp.zeros((lat_ch, c), band_ref.dtype)
    for dt in range(3):
        for di in range(3):
            p = dt * 3 + di
            for j in range(w_ext):
                for jj in range(lanes // lat_ch):
                    r0 = p * lanes + jj * lat_ch
                    dj = jj - j
                    blk = k_ref[p * 3 + dj] if 0 <= dj <= 2 else zero
                    band_ref[r0 : r0 + lat_ch, j * c : (j + 1) * c] = blk
            slab = lat_ref[dt : dt + t_ext, di : di + rows, :].reshape(t_ext * rows, lanes)
            patch_ref[:, p * lanes : (p + 1) * lanes] = slab.astype(patch_ref.dtype)
    entry = jnp.dot(patch_ref[...], band_ref[...], preferred_element_type=jnp.float32)
    for j in range(w_ext):
        e = (entry[:, j * c : (j + 1) * c] + b_ref[...]).astype(jnp.bfloat16)
        if 1 <= j <= w_ext - 2:
            own_ref[:, j - 1] = e.reshape(t_ext, rows, c)[t_ext - FR_DEV :]
        fa = _norm_silu(e.astype(jnp.float32), g_ref[...]).reshape(t_ext, rows, c)
        for t in range(t_ext):
            act_ref[t, j] = (fa[t] * ok_ref[t * w_ext + j]).astype(act_ref.dtype)


def entry_pallas(lat, entry_kernel, entry_bias, gain_one, ok):
    t_ext, w_ext = FR_DEV + 2, W_DEV + 2
    lanes = lat.shape[-1]
    c = entry_kernel.shape[-1]
    kr = entry_kernel.reshape(27, LAT, c)
    vmem = pl.BlockSpec(memory_space=pltpu.VMEM)
    return pl.pallas_call(
        _entry_kernel,
        in_specs=[vmem, vmem, vmem, vmem, pl.BlockSpec(memory_space=pltpu.SMEM)],
        out_specs=(vmem, vmem),
        out_shape=(
            jax.ShapeDtypeStruct((t_ext, w_ext, H, c), jnp.bfloat16),
            jax.ShapeDtypeStruct((FR_DEV, W_DEV, H, c), jnp.bfloat16),
        ),
        scratch_shapes=[
            pltpu.VMEM((9 * lanes, w_ext * c), jnp.bfloat16),
            pltpu.VMEM((t_ext * H, 9 * lanes), jnp.bfloat16),
        ],
        compiler_params=pltpu.CompilerParams(vmem_limit_bytes=48 * 1024 * 1024),
        cost_estimate=pl.CostEstimate(
            flops=2 * t_ext * H * 9 * lanes * w_ext * c,
            transcendentals=t_ext * w_ext * H * c,
            bytes_accessed=lat.size * 4 + kr.size * 2 + (t_ext * w_ext + FR_DEV * W_DEV) * H * c * 2,
        ),
    )(lat, kr, entry_bias.reshape(1, c), gain_one.reshape(1, c), ok)


def _entry_conv_kernel(
    lat_ref, ke_ref, be_ref, g1_ref, ok_ref, w_hbm, b_ref, g2_ref,
    o_ref, own_ref, act_ref, band_ref, patch_ref, acc_ref, cols_ref, wbuf, sems,
):
    def entry():
        _entry_kernel(lat_ref, ke_ref, be_ref, g1_ref, ok_ref, act_ref, own_ref, band_ref, patch_ref)

    _conv_body("act", act_ref, w_hbm, b_ref, g2_ref, o_ref, acc_ref, cols_ref, wbuf, sems, entry)


def entry_conv_pallas(lat, entry_kernel, entry_bias, gain_one, ok, kernel, bias, gain_two):
    t_ext, w_ext = FR_DEV + 2, W_DEV + 2
    lanes = lat.shape[-1]
    c = entry_kernel.shape[-1]
    co = kernel.shape[-1]
    kr = entry_kernel.reshape(27, LAT, c)
    out_shape = (FR_DEV, W_DEV, H, co)
    m = FR_DEV * W_DEV * H
    vmem = pl.BlockSpec(memory_space=pltpu.VMEM)
    flops = 2 * t_ext * H * 9 * lanes * w_ext * c + 2 * m * 27 * c * co
    return pl.pallas_call(
        _entry_conv_kernel,
        in_specs=[
            vmem, vmem, vmem, vmem, pl.BlockSpec(memory_space=pltpu.SMEM),
            pl.BlockSpec(memory_space=pl.ANY), vmem, vmem,
        ],
        out_specs=(vmem, vmem),
        out_shape=(
            jax.ShapeDtypeStruct(out_shape, jnp.bfloat16),
            jax.ShapeDtypeStruct(out_shape, jnp.bfloat16),
        ),
        scratch_shapes=[
            pltpu.VMEM((t_ext, w_ext, H, c), jnp.bfloat16),
            pltpu.VMEM((9 * lanes, w_ext * c), jnp.bfloat16),
            pltpu.VMEM((t_ext * H, 9 * lanes), jnp.bfloat16),
            pltpu.VMEM((m, co), jnp.float32),
            pltpu.VMEM((FR_DEV, W_DEV, H, 9 * c), jnp.bfloat16),
            pltpu.VMEM(kernel.shape, kernel.dtype),
            pltpu.SemaphoreType.DMA((4,)),
        ],
        compiler_params=pltpu.CompilerParams(vmem_limit_bytes=48 * 1024 * 1024),
        cost_estimate=pl.CostEstimate(
            flops=flops,
            transcendentals=t_ext * w_ext * H * c + m * co,
            bytes_accessed=lat.size * 4 + kr.size * 2 + kernel.size * 2 + 2 * m * co * 2,
        ),
    )(lat, kr, entry_bias.reshape(1, c), gain_one.reshape(1, c), ok, kernel,
      bias.reshape(1, co), gain_two.reshape(1, c))


def shift2(value, ds, dk):
    n_tm, n_tile = lax.axis_size("tm"), lax.axis_size("tile")
    pairs = []
    for s in range(n_tm):
        for k in range(n_tile):
            if 0 <= s + ds < n_tm and 0 <= k + dk < n_tile:
                pairs.append((s * n_tile + k, (s + ds) * n_tile + k + dk))
    return lax.ppermute(value, ("tm", "tile"), pairs)


def gather_latent(latent_tokens, total_cols):
    n_tm, n_tile = lax.axis_size("tm"), lax.axis_size("tile")
    s = lax.axis_index("tm")
    rows_per = FR_DEV * H // n_tile
    span = (W_DEV + 4) * LAT
    strip = latent_tokens.reshape(rows_per, total_cols * LAT)
    strip = jnp.pad(strip, ((0, 0), (2 * LAT, 2 * LAT)))
    windows = jnp.stack(
        [strip[:, t * W_DEV * LAT : t * W_DEV * LAT + span] for t in range(n_tile)], axis=0
    )
    chunks = jnp.broadcast_to(windows[:, None], (n_tile, n_tm) + windows.shape[1:])
    chunks = chunks.reshape((n_tile * n_tm,) + windows.shape[1:])
    got = lax.all_to_all(chunks, ("tile", "tm"), 0, 0, tiled=True)
    got = got.reshape((n_tile, n_tm) + windows.shape[1:]).transpose(1, 0, 2, 3)
    got = jnp.pad(got, ((2, 0), (0, 0), (0, 0), (0, 0)))
    got = lax.dynamic_slice_in_dim(got, s, 3, axis=0)
    return got.reshape(3 * FR_DEV, H, span)


def body(
    latent_tokens,
    entry_kernel,
    entry_bias,
    gain_one,
    first_kernel,
    first_bias,
    gain_two,
    second_kernel,
    second_bias,
):
    tiles = lax.axis_size("tile")
    total_cols = W_DEV * tiles
    s = lax.axis_index("tm")
    k = lax.axis_index("tile")
    c = entry_kernel.shape[-1]
    t_ext, w_ext = FR_DEV + 2, W_DEV + 2

    lat = gather_latent(latent_tokens, total_cols)
    lat = jnp.pad(lat, ((0, 0), (1, 1), (0, 0))).astype(jnp.float32)

    frame_ok = (s * FR_DEV - 2 + jnp.arange(t_ext)) >= 0
    col_id = k * W_DEV - 1 + jnp.arange(w_ext)
    col_ok = (col_id >= 0) & (col_id < total_cols)
    ok = (frame_ok[:, None] & col_ok[None, :]).astype(jnp.float32).reshape(-1)
    second_act, entry_own = entry_conv_pallas(
        lat, entry_kernel, entry_bias, gain_one, ok, first_kernel, first_bias, gain_two
    )

    last, first = second_act[:, W_DEV - 1 :], second_act[:, :1]
    own_row = [shift2(last, 0, 1), second_act, shift2(first, 0, -1)]
    prev_row = [shift2(last, 1, 1), shift2(second_act, 1, 0), shift2(first, 1, -1)]
    ext2 = jnp.concatenate(
        [jnp.concatenate(prev_row, axis=1), jnp.concatenate(own_row, axis=1)], axis=0
    )

    decoded = conv_pallas("res", ext2, second_kernel, second_bias, entry_own)
    return jnp.transpose(decoded, (0, 2, 1, 3))


def solution(mesh):
    in_specs = (P(("tm", "tile"), None), P(), P(), P(), P(), P(), P(), P(), P())
    out_specs = P("tm", None, "tile", None)
    return jax.shard_map(body, mesh=mesh, in_specs=in_specs, out_specs=out_specs, check_vma=False)
```
